128 devices in a mesh: gy: 8 (over x, core), gx: 16 (over z, y).
Axes of the slice: x: 4, y: 4, z: 4, core: 2. Of those that a mesh axis runs over, the one named last changes fastest.
Arguments:
- water_depth: float32 [4096, 8192], P('gy', 'gx'), may hold values from 1 to 3
- flux_east: float32 [4096, 8192], P('gy', 'gx'), may hold values from -1.5 to 1.5
- flux_south: float32 [4096, 8192], P('gy', 'gx'), may hold values from -1.5 to 1.5
- bed_level: float32 [4096, 8192], P('gy', 'gx'), may hold values from -3 to 3
- roughness: float32 [4096, 8192], P('gy', 'gx'), may hold values from 0.5 to 5
- land_mask: int32 [4096, 8192], P('gy', 'gx'), may hold values 0 or 1
- tile_block: int32 [32768], P(('gy', 'gx')), may hold values from 0 to 2047, as said below
- storage: float32 [2048, 128], P(('gy', 'gx')), may hold values from 0.5 to 2
- reach_rate: float32 [2048, 128], P(('gy', 'gx')), may hold values from 0.1 to 0.5
- downstream: int32 [2048], P(('gy', 'gx')), may hold values from 1 to 2048, as said below
Outputs:
- new_depth: float32 [4096, 8192], P('gy', 'gx')
- new_flux_east: float32 [4096, 8192], P('gy', 'gx')
- new_flux_south: float32 [4096, 8192], P('gy', 'gx')
- new_storage: float32 [2048, 128], P(('gy', 'gx'))
The draws below stay inside these ranges and needn't reach their ends.
Inputs may be any that keep to these rules, and one draw needn't show every extreme that they name: downstream[r] = min(r + k, 2048) with 1 <= k <= 8; in every device's 16 blocks the first has k = 8. `tile_block`: among the 256 tiles of one device, at most 4 drain into blocks held by one device (16 consecutive blocks from a multiple of 16); on every device some such owner receives exactly 4.
All inputs are finite; a program needn't handle non-finite values. No bound on the sum of `land_mask` on one device may be relied on, other than what follows from the above.
Results may differ from the reference program's by a relative error of at most 0.0001.
Values sent between devices are 32-bit elements; how exact they have to be, the bound alone decides.
No kernel may reach another device: no remote copies, remote signals or barrier semaphores. Data moves between devices by JAX's collectives and lax.ppermute only.
A program may use at most 64 MiB of HBM per device.

```python
import math
import jax
import jax.numpy as jnp

CY = 512
CX = 512
ROWS_DEV = 16
STRIP = 8
REACH_ROW = 128
STEPS = 2
SPAN = 8
NY = 4096
NX = 8192
TILES_DEV = 256
NTILES = 32768
NBLK = 2048
CAP = 4
N_GY = 8
N_GX = 16


def draw_downstream(key, part):
    offsets = jax.random.randint(key, (NBLK,), 1, SPAN + 1)
    blocks = jnp.arange(NBLK, dtype=jnp.int32)
    offsets = jnp.where(blocks % ROWS_DEV == 0, SPAN, offsets)
    return jnp.minimum(blocks + offsets, NBLK).astype(jnp.int32)


def draw_tile_block(key, part):
    owners = NTILES // TILES_DEV
    slot_count = owners * CAP

    def one_device(device):
        inner_key = jax.random.fold_in(jax.random.fold_in(key, 7001), device)
        key_fav, key_order, key_shuffle, key_inner = jax.random.split(inner_key, 4)
        favored = jax.random.randint(key_fav, (), 0, owners)
        slots = jnp.arange(slot_count, dtype=jnp.int32)
        order = jax.random.permutation(key_order, slot_count).astype(jnp.int32)
        score = order + jnp.where(slots // CAP == favored, 0, slot_count).astype(jnp.int32)
        chosen = jnp.argsort(score, stable=True)[:TILES_DEV].astype(jnp.int32)
        chosen = jax.random.permutation(key_shuffle, chosen)
        owner = chosen // CAP
        inner = jax.random.randint(key_inner, (TILES_DEV,), 0, ROWS_DEV)
        return (owner * ROWS_DEV + inner).astype(jnp.int32)
    return jax.vmap(one_device)(jnp.arange(owners, dtype=jnp.int32)).reshape(-1).astype(jnp.int32)


def plant(array, key, least, high):
    shape = array.shape
    place = [jax.random.randint(jax.random.fold_in(key, axis), (), 0, shape[axis]) for axis in range(len(shape))]
    array = array.at[tuple(place)].set(least)
    longest = shape.index(max(shape))
    place[longest] = (place[longest] + 1) % shape[longest]
    return array.at[tuple(place)].set(high)


def level_of(own_key, dims, cuts, smallest, high):
    loudness, own = 1.0, jax.random.fold_in(own_key, 6)
    for position, shards_of in cuts:
        heights = jnp.exp(jax.random.uniform(jax.random.fold_in(own, position), (shards_of,), jnp.float32, smallest / len(cuts), high / len(cuts)))
        loudness = loudness * jnp.repeat(heights, dims[position] // shards_of).reshape([-1 if axis == position else 1 for axis in range(len(dims))])
    return loudness


def scatter_about(rng, dims, scale, reach, pieces=(), kind=jnp.bfloat16):
    factor_of = level_of(rng, dims, pieces, -0.22, 0.18) if pieces else 1.0
    drawn = jax.random.normal(rng, dims, jnp.float32) * scale * factor_of
    return jnp.minimum(jnp.maximum(drawn, -reach), reach).astype(kind)


def setup_inputs(seed: int = 0) -> dict:
    arg_keys = jax.random.split(jax.random.key(seed), 11)
    return {
        "water_depth": jnp.clip(1.0 + 2.0 * jax.random.uniform(arg_keys[0], (NY, NX), jnp.float32) ** level_of(arg_keys[0], (NY, NX), ((0, 8), (1, 16)), -0.2, 0.2), 1.0, 3.0),
        "flux_east": scatter_about(arg_keys[1], (NY, NX), 0.3, 1.5, ((0, 8), (1, 16)), jnp.float32),
        "flux_south": scatter_about(arg_keys[2], (NY, NX), 0.3, 1.5, ((0, 8), (1, 16)), jnp.float32),
        "bed_level": scatter_about(arg_keys[3], (NY, NX), 0.3, 3.0, ((0, 8), (1, 16)), jnp.float32),
        "roughness": jnp.clip(jnp.exp(math.log(5.0) - 2.3025851 * jax.random.uniform(arg_keys[4], (NY, NX), jnp.float32) ** level_of(arg_keys[4], (NY, NX), ((0, 8), (1, 16)), -0.2, 0.2)), 0.5, 5.0),
        "land_mask": plant((jax.random.randint(arg_keys[5], (NY, NX), 0, 16) < 15).astype(jnp.int32), jax.random.fold_in(arg_keys[5], 1), 0, 1),
        "tile_block": draw_tile_block(jax.random.fold_in(arg_keys[10], 71), 0),
        "storage": jnp.clip(jnp.exp(math.log(2.0) - 1.3862944 * jax.random.uniform(arg_keys[7], (NBLK, REACH_ROW), jnp.float32) ** level_of(arg_keys[7], (NBLK, REACH_ROW), ((0, 128),), -0.2, 0.2)), 0.5, 2.0),
        "reach_rate": jnp.clip(jnp.exp(math.log(0.5) - 1.609438 * jax.random.uniform(arg_keys[8], (NBLK, REACH_ROW), jnp.float32) ** level_of(arg_keys[8], (NBLK, REACH_ROW), ((0, 128),), -0.2, 0.2)), 0.1, 0.5),
        "downstream": draw_downstream(jax.random.fold_in(arg_keys[10], 71), 0),
    }


rim_depth = 0.1
slope_gain = 0.1
friction_gain = 1.0
mass_gain = 0.05
drain_rate = 0.05
lateral_gain = 0.125


def face_update(flux, level, level_next, depth, depth_next, roughness, active):
    face_depth = rim_depth + 0.5 * (jnp.abs(depth) + jnp.abs(depth_next))
    drive = flux - slope_gain * face_depth * (level_next - level)
    damping = 1.0 + friction_gain * roughness * jnp.abs(flux) / jnp.power(face_depth, 7.0 / 3.0)
    return active * drive / damping


def reference(water_depth, flux_east, flux_south, bed_level, roughness, land_mask, tile_block, storage, reach_rate, downstream):
    land_float = land_mask.astype(jnp.float32)
    columns = jnp.arange(NX)
    grid_rows = jnp.arange(NY)
    east_open = land_float * (columns < NX - 1).astype(jnp.float32)[None, :]
    south_open = land_float * (grid_rows < NY - 1).astype(jnp.float32)[:, None]
    zero_col = jnp.zeros((NY, 1), jnp.float32)
    zero_row = jnp.zeros((1, NX), jnp.float32)
    depth = water_depth
    for _ in range(STEPS):
        level = bed_level + depth
        level_east = jnp.concatenate([level[:, 1:], zero_col], axis=1)
        depth_east = jnp.concatenate([depth[:, 1:], zero_col], axis=1)
        level_south = jnp.concatenate([level[1:], zero_row], axis=0)
        depth_south = jnp.concatenate([depth[1:], zero_row], axis=0)
        flux_east = face_update(flux_east, level, level_east, depth, depth_east, roughness, east_open)
        flux_south = face_update(flux_south, level, level_south, depth, depth_south, roughness, south_open)
        west_flux = jnp.concatenate([zero_col, flux_east[:, :-1]], axis=1)
        north_flux = jnp.concatenate([zero_row, flux_south[:-1]], axis=0)
        drained = drain_rate * land_float * jnp.abs(depth)
        depth = depth - mass_gain * ((flux_east - west_flux) + (flux_south - north_flux)) - drained
        tile_sums = drained.reshape(N_GY, CY // STRIP, STRIP, N_GX, CX // REACH_ROW, REACH_ROW).sum(axis=2)
        tile_sums = tile_sums.transpose(0, 2, 1, 3, 4).reshape(NTILES, REACH_ROW)
        lateral = jax.ops.segment_sum(tile_sums, tile_block, num_segments=NBLK)
        ratio = reach_rate * jnp.power(storage, 2.0 / 3.0)
        outflow = storage * ratio / (1.0 + ratio)
        upstream = jax.ops.segment_sum(outflow, downstream, num_segments=NBLK + 1)[:NBLK]
        storage = storage - outflow + upstream + lateral_gain * lateral
    return depth, flux_east, flux_south, storage
```

```python
import jax
import jax.numpy as jnp
from jax import lax
from jax.sharding import PartitionSpec as P

STRIP = 8
STEPS = 2


rim_depth = 0.1
slope_gain = 0.1
friction_gain = 1.0
mass_gain = 0.05
drain_rate = 0.05
lateral_gain = 0.125


def shifted(value, axis, steps):
    count = lax.axis_size(axis)
    first, last = (max(0, -steps), min(count, count - steps))
    return lax.ppermute(value, axis, [(source, source + steps) for source in range(first, last)])


def face_update(flux, level, level_next, depth, depth_next, roughness, active):
    face_depth = rim_depth + 0.5 * (jnp.abs(depth) + jnp.abs(depth_next))
    drive = flux - slope_gain * face_depth * (level_next - level)
    damping = 1.0 + friction_gain * roughness * jnp.abs(flux) / jnp.power(face_depth, 7.0 / 3.0)
    return active * drive / damping


def onehot_sum(ids, values, count):
    targets = lax.iota(jnp.float32, count)
    onehot = (targets[:, None] == ids[None, :]).astype(jnp.float32)
    return jnp.dot(onehot, values, precision=lax.Precision.HIGHEST)


def block_term(target_ids, values, start, count):
    targets = start + lax.iota(jnp.int32, count)
    onehot = (target_ids[:, None] == targets[None, :]).astype(jnp.float32)
    return jnp.einsum("tb,tc->bc", onehot, values, precision=lax.Precision.HIGHEST)


def body(
    water_depth,
    flux_east,
    flux_south,
    bed_level,
    roughness,
    land_mask,
    tile_block,
    storage,
    reach_rate,
    downstream,
):
    cell_rows, cell_cols = water_depth.shape
    block_rows, reach_width = storage.shape
    row_count = lax.axis_size("gy")
    col_count = lax.axis_size("gx")
    row_index = lax.axis_index("gy")
    col_index = lax.axis_index("gx")
    device_count = row_count * col_count
    tile_count = tile_block.shape[0]
    slot_cap = max(2, 2 * tile_count // device_count)
    land_float = land_mask.astype(jnp.float32)
    global_cols = col_index * cell_cols + lax.iota(jnp.int32, cell_cols)
    global_rows = row_index * cell_rows + lax.iota(jnp.int32, cell_rows)
    east_open = land_float * (global_cols < cell_cols * col_count - 1).astype(jnp.float32)[None, :]
    south_open = land_float * (global_rows < cell_rows * row_count - 1).astype(jnp.float32)[:, None]
    device_index = row_index * col_count + col_index
    first_block = device_index * block_rows

    column_slots = row_count * slot_cap
    tile_owner = tile_block // block_rows
    owner_row = tile_owner // col_count
    owner_col = tile_owner % col_count
    owner_hits = (tile_owner[:, None] == lax.iota(jnp.int32, device_count)[None, :]).astype(
        jnp.int32
    )
    earlier = jnp.sum((jnp.cumsum(owner_hits, axis=0) - owner_hits) * owner_hits, axis=1)
    send_pos = owner_col * column_slots + owner_row * slot_cap + earlier
    column_ids = (owner_row * block_rows + tile_block % block_rows).astype(jnp.float32)
    send_ids = jnp.full((col_count * column_slots,), -1.0, jnp.float32).at[send_pos].set(column_ids)
    id_rows = -(-column_slots // reach_width)
    send_ids = jnp.pad(
        send_ids.reshape(col_count, column_slots),
        ((0, 0), (0, id_rows * reach_width - column_slots)),
        constant_values=-1.0,
    ).reshape(col_count, id_rows, reach_width)
    gather_onehot = (
        lax.iota(jnp.int32, col_count * column_slots)[:, None] == send_pos[None, :]
    ).astype(jnp.float32)

    def lateral_of(drained, first):
        tile_sums = drained.reshape(
            cell_rows // STRIP, STRIP, cell_cols // reach_width, reach_width
        ).sum(axis=1)
        tile_sums = tile_sums.reshape(-1, reach_width)
        packed = jnp.dot(gather_onehot, tile_sums, precision=lax.Precision.HIGHEST)
        packed = packed.reshape(col_count, column_slots, reach_width)
        if first:
            packed = jnp.concatenate([packed, send_ids], axis=1)
        got = lax.all_to_all(packed, "gx", 0, 0, tiled=True)
        got_vals = got[:, :column_slots].reshape(-1, reach_width)
        got_ids = got[:, column_slots:].reshape(col_count, -1)[:, :column_slots].reshape(-1)
        return got_vals, got_ids

    def finish_lateral(got_vals, got_ids):
        by_column = onehot_sum(got_ids, got_vals, row_count * block_rows)
        by_column = by_column.reshape(row_count, block_rows, reach_width)
        parts = lax.all_to_all(by_column, "gy", 0, 0, tiled=True)
        return jnp.sum(parts, axis=0)

    recv_ids = None
    depth = water_depth
    for step in range(STEPS):
        level = bed_level + depth
        east_msg = shifted(jnp.stack([level[:, 0], depth[:, 0]]), "gx", -1)
        south_msg = shifted(jnp.stack([level[0, :], depth[0, :]]), "gy", -1)
        west_msg = shifted(
            jnp.stack(
                [flux_east[:, -1], level[:, -1], depth[:, -1], roughness[:, -1], east_open[:, -1]]
            ),
            "gx",
            1,
        )
        north_msg = shifted(
            jnp.stack(
                [flux_south[-1, :], level[-1, :], depth[-1, :], roughness[-1, :], south_open[-1, :]]
            ),
            "gy",
            1,
        )
        drained = drain_rate * land_float * jnp.abs(depth)
        got_vals, got_ids = lateral_of(drained, step == 0)
        if step == 0:
            recv_ids = got_ids
        level_east = jnp.concatenate([level[:, 1:], east_msg[0][:, None]], axis=1)
        depth_east = jnp.concatenate([depth[:, 1:], east_msg[1][:, None]], axis=1)
        level_south = jnp.concatenate([level[1:], south_msg[0][None, :]], axis=0)
        depth_south = jnp.concatenate([depth[1:], south_msg[1][None, :]], axis=0)
        west_edge = face_update(
            west_msg[0], west_msg[1], level[:, 0], west_msg[2], depth[:, 0], west_msg[3], west_msg[4]
        )
        north_edge = face_update(
            north_msg[0], north_msg[1], level[0, :], north_msg[2], depth[0, :], north_msg[3],
            north_msg[4],
        )
        flux_east = face_update(
            flux_east, level, level_east, depth, depth_east, roughness, east_open
        )
        flux_south = face_update(
            flux_south, level, level_south, depth, depth_south, roughness, south_open
        )
        west_flux = jnp.concatenate([west_edge[:, None], flux_east[:, :-1]], axis=1)
        north_flux = jnp.concatenate([north_edge[None, :], flux_south[:-1]], axis=0)
        depth = depth - mass_gain * (flux_east - west_flux + (flux_south - north_flux)) - drained
        lateral = finish_lateral(got_vals, recv_ids)
        ratio = reach_rate * jnp.power(storage, 2.0 / 3.0)
        outflow = storage * ratio / (1.0 + ratio)
        own_part = block_term(downstream, outflow, first_block, block_rows)
        ahead_part = block_term(downstream, outflow, first_block + block_rows, block_rows)
        upstream = own_part + shifted(ahead_part, ("gy", "gx"), 1)
        storage = storage - outflow + upstream + lateral_gain * lateral
    return (depth, flux_east, flux_south, storage)


def solution(mesh):
    placed = (
        P("gy", "gx"),
        P("gy", "gx"),
        P("gy", "gx"),
        P("gy", "gx"),
        P("gy", "gx"),
        P("gy", "gx"),
        P(("gy", "gx")),
        P(("gy", "gx"), None),
        P(("gy", "gx"), None),
        P(("gy", "gx")),
    )
    return jax.shard_map(
        body,
        mesh=mesh,
        in_specs=placed,
        out_specs=(P("gy", "gx"), P("gy", "gx"), P("gy", "gx"), P(("gy", "gx"), None)),
        check_vma=False,
    )
```

```python
import jax
import jax.numpy as jnp
from jax import lax
from jax.sharding import PartitionSpec as P

STRIP = 8
STEPS = 2


rim_depth = 0.1
slope_gain = 0.1
friction_gain = 1.0
mass_gain = 0.05
drain_rate = 0.05
lateral_gain = 0.125


def shifted(value, axis, steps):
    count = lax.axis_size(axis)
    first, last = (max(0, -steps), min(count, count - steps))
    return lax.ppermute(value, axis, [(source, source + steps) for source in range(first, last)])


def face_update(flux, level, level_next, depth, depth_next, roughness, active):
    face_depth = rim_depth + 0.5 * (jnp.abs(depth) + jnp.abs(depth_next))
    drive = flux - slope_gain * face_depth * (level_next - level)
    damping = 1.0 + friction_gain * roughness * jnp.abs(flux) / jnp.power(face_depth, 7.0 / 3.0)
    return active * drive / damping


def block_term(target_ids, values, start, count):
    targets = start + lax.iota(jnp.int32, count)
    onehot = (target_ids[:, None] == targets[None, :]).astype(jnp.float32)
    return jnp.einsum("tb,tc->bc", onehot, values, precision=lax.Precision.HIGHEST)


def body(
    water_depth,
    flux_east,
    flux_south,
    bed_level,
    roughness,
    land_mask,
    tile_block,
    storage,
    reach_rate,
    downstream,
):
    cell_rows, cell_cols = water_depth.shape
    block_rows, reach_width = storage.shape
    row_count = lax.axis_size("gy")
    col_count = lax.axis_size("gx")
    row_index = lax.axis_index("gy")
    col_index = lax.axis_index("gx")
    device_count = row_count * col_count
    tile_count = tile_block.shape[0]
    slot_cap = max(2, 2 * tile_count // device_count)
    land_float = land_mask.astype(jnp.float32)
    global_cols = col_index * cell_cols + lax.iota(jnp.int32, cell_cols)
    global_rows = row_index * cell_rows + lax.iota(jnp.int32, cell_rows)
    east_open = land_float * (global_cols < cell_cols * col_count - 1).astype(jnp.float32)[None, :]
    south_open = land_float * (global_rows < cell_rows * row_count - 1).astype(jnp.float32)[:, None]
    device_index = row_index * col_count + col_index
    first_block = device_index * block_rows

    total_blocks = block_rows * device_count

    def lateral_of(drained):
        tile_sums = drained.reshape(
            cell_rows // STRIP, STRIP, cell_cols // reach_width, reach_width
        ).sum(axis=1)
        tile_sums = tile_sums.reshape(-1, reach_width)
        every_block = block_term(tile_block, tile_sums, 0, total_blocks)
        return lax.psum_scatter(every_block, ("gy", "gx"), scatter_dimension=0, tiled=True)

    depth = water_depth
    for step in range(STEPS):
        level = bed_level + depth
        east_msg = shifted(jnp.stack([level[:, 0], depth[:, 0]]), "gx", -1)
        south_msg = shifted(jnp.stack([level[0, :], depth[0, :]]), "gy", -1)
        west_msg = shifted(
            jnp.stack(
                [flux_east[:, -1], level[:, -1], depth[:, -1], roughness[:, -1], east_open[:, -1]]
            ),
            "gx",
            1,
        )
        north_msg = shifted(
            jnp.stack(
                [flux_south[-1, :], level[-1, :], depth[-1, :], roughness[-1, :], south_open[-1, :]]
            ),
            "gy",
            1,
        )
        drained = drain_rate * land_float * jnp.abs(depth)
        lateral = lateral_of(drained)
        level_east = jnp.concatenate([level[:, 1:], east_msg[0][:, None]], axis=1)
        depth_east = jnp.concatenate([depth[:, 1:], east_msg[1][:, None]], axis=1)
        level_south = jnp.concatenate([level[1:], south_msg[0][None, :]], axis=0)
        depth_south = jnp.concatenate([depth[1:], south_msg[1][None, :]], axis=0)
        west_edge = face_update(
            west_msg[0], west_msg[1], level[:, 0], west_msg[2], depth[:, 0], west_msg[3], west_msg[4]
        )
        north_edge = face_update(
            north_msg[0], north_msg[1], level[0, :], north_msg[2], depth[0, :], north_msg[3],
            north_msg[4],
        )
        flux_east = face_update(
            flux_east, level, level_east, depth, depth_east, roughness, east_open
        )
        flux_south = face_update(
            flux_south, level, level_south, depth, depth_south, roughness, south_open
        )
        west_flux = jnp.concatenate([west_edge[:, None], flux_east[:, :-1]], axis=1)
        north_flux = jnp.concatenate([north_edge[None, :], flux_south[:-1]], axis=0)
        depth = depth - mass_gain * (flux_east - west_flux + (flux_south - north_flux)) - drained
        ratio = reach_rate * jnp.power(storage, 2.0 / 3.0)
        outflow = storage * ratio / (1.0 + ratio)
        own_part = block_term(downstream, outflow, first_block, block_rows)
        ahead_part = block_term(downstream, outflow, first_block + block_rows, block_rows)
        upstream = own_part + shifted(ahead_part, ("gy", "gx"), 1)
        storage = storage - outflow + upstream + lateral_gain * lateral
    return (depth, flux_east, flux_south, storage)


def solution(mesh):
    placed = (
        P("gy", "gx"),
        P("gy", "gx"),
        P("gy", "gx"),
        P("gy", "gx"),
        P("gy", "gx"),
        P("gy", "gx"),
        P(("gy", "gx")),
        P(("gy", "gx"), None),
        P(("gy", "gx"), None),
        P(("gy", "gx")),
    )
    return jax.shard_map(
        body,
        mesh=mesh,
        in_specs=placed,
        out_specs=(P("gy", "gx"), P("gy", "gx"), P("gy", "gx"), P(("gy", "gx"), None)),
        check_vma=False,
    )
```

```python
import functools

import jax
import jax.numpy as jnp
from jax import lax
from jax.experimental import pallas as pl
from jax.experimental.pallas import tpu as pltpu
from jax.sharding import PartitionSpec as P

STRIP = 8
STEPS = 2


rim_depth = 0.1
slope_gain = 0.1
friction_gain = 1.0
mass_gain = 0.05
drain_rate = 0.05
lateral_gain = 0.125


def shifted(value, axis, steps):
    count = lax.axis_size(axis)
    first, last = (max(0, -steps), min(count, count - steps))
    return lax.ppermute(value, axis, [(source, source + steps) for source in range(first, last)])


def face_update(flux, level, level_next, depth, depth_next, roughness, active):
    face_depth = rim_depth + 0.5 * (jnp.abs(depth) + jnp.abs(depth_next))
    drive = flux - slope_gain * face_depth * (level_next - level)
    damping = 1.0 + friction_gain * roughness * jnp.abs(flux) / jnp.power(face_depth, 7.0 / 3.0)
    return active * drive / damping


def block_term(target_ids, values, start, count):
    targets = start + lax.iota(jnp.int32, count)
    onehot = (target_ids[:, None] == targets[None, :]).astype(jnp.float32)
    return jnp.einsum("tb,tc->bc", onehot, values, precision=lax.Precision.HIGHEST)


def write_edges(level, depth, flux_e, flux_s, rough, eopen, sopen, to_west, to_north, to_east,
                to_south):
    to_west[:, 0:1] = level[:, 0:1]
    to_west[:, 1:2] = depth[:, 0:1]
    to_north[0:1, :] = level[0:1, :]
    to_north[1:2, :] = depth[0:1, :]
    to_east[:, 0:1] = flux_e[:, -1:]
    to_east[:, 1:2] = level[:, -1:]
    to_east[:, 2:3] = depth[:, -1:]
    to_east[:, 3:4] = rough[:, -1:]
    to_east[:, 4:5] = eopen[:, -1:]
    to_south[0:1, :] = flux_s[-1:, :]
    to_south[1:2, :] = level[-1:, :]
    to_south[2:3, :] = depth[-1:, :]
    to_south[3:4, :] = rough[-1:, :]
    to_south[4:5, :] = sopen[-1:, :]


def open_masks(flags_ref, land):
    ny, nx = land.shape
    col = lax.broadcasted_iota(jnp.int32, (ny, nx), 1)
    row = lax.broadcasted_iota(jnp.int32, (ny, nx), 0)
    eopen = jnp.where((col == nx - 1) & (flags_ref[0] == 1), 0.0, land)
    sopen = jnp.where((row == ny - 1) & (flags_ref[1] == 1), 0.0, land)
    return col, row, eopen, sopen


def edge_kernel(flags_ref, d_ref, e_ref, s_ref, bed_ref, r_ref, land_ref,
                to_west, to_north, to_east, to_south):
    depth = d_ref[...]
    level = bed_ref[...] + depth
    _, _, eopen, sopen = open_masks(flags_ref, land_ref[...])
    write_edges(level, depth, e_ref[...], s_ref[...], r_ref[...], eopen, sopen,
                to_west, to_north, to_east, to_south)


def step_kernel(flags_ref, d_ref, e_ref, s_ref, bed_ref, r_ref, land_ref,
                east_ref, south_ref, west_ref, north_ref,
                d_out, e_out, s_out, tile_out, to_west, to_north, to_east, to_south):
    ny, nx = d_ref.shape
    depth = d_ref[...]
    bed = bed_ref[...]
    land = land_ref[...]
    rough = r_ref[...]
    level = bed + depth
    col, row, eopen, sopen = open_masks(flags_ref, land)
    level_e = jnp.where(col == nx - 1, east_ref[:, 0:1], pltpu.roll(level, nx - 1, 1))
    depth_e = jnp.where(col == nx - 1, east_ref[:, 1:2], pltpu.roll(depth, nx - 1, 1))
    level_s = jnp.where(row == ny - 1, south_ref[0:1, :], pltpu.roll(level, ny - 1, 0))
    depth_s = jnp.where(row == ny - 1, south_ref[1:2, :], pltpu.roll(depth, ny - 1, 0))
    flux_e = face_update(e_ref[...], level, level_e, depth, depth_e, rough, eopen)
    flux_s = face_update(s_ref[...], level, level_s, depth, depth_s, rough, sopen)
    west_edge = face_update(
        west_ref[:, 0:1], west_ref[:, 1:2], level[:, 0:1], west_ref[:, 2:3], depth[:, 0:1],
        west_ref[:, 3:4], west_ref[:, 4:5],
    )
    north_edge = face_update(
        north_ref[0:1, :], north_ref[1:2, :], level[0:1, :], north_ref[2:3, :], depth[0:1, :],
        north_ref[3:4, :], north_ref[4:5, :],
    )
    west_flux = jnp.where(col == 0, west_edge, pltpu.roll(flux_e, 1, 1))
    north_flux = jnp.where(row == 0, north_edge, pltpu.roll(flux_s, 1, 0))
    drained = drain_rate * land * jnp.abs(depth)
    new_depth = depth - mass_gain * (flux_e - west_flux + (flux_s - north_flux)) - drained
    d_out[...] = new_depth
    e_out[...] = flux_e
    s_out[...] = flux_s
    tile_out[...] = drained.reshape(ny // STRIP, STRIP, nx).sum(axis=1)
    write_edges(bed + new_depth, new_depth, flux_e, flux_s, rough, eopen, sopen,
                to_west, to_north, to_east, to_south)


def edge_shapes(ny, nx):
    f32 = jnp.float32
    return (
        jax.ShapeDtypeStruct((ny, 2), f32),
        jax.ShapeDtypeStruct((2, nx), f32),
        jax.ShapeDtypeStruct((ny, 5), f32),
        jax.ShapeDtypeStruct((5, nx), f32),
    )


def vmem_specs(count):
    return [pl.BlockSpec(memory_space=pltpu.VMEM) for _ in range(count)]


def body(
    water_depth,
    flux_east,
    flux_south,
    bed_level,
    roughness,
    land_mask,
    tile_block,
    storage,
    reach_rate,
    downstream,
):
    cell_rows, cell_cols = water_depth.shape
    block_rows, reach_width = storage.shape
    row_count = lax.axis_size("gy")
    col_count = lax.axis_size("gx")
    row_index = lax.axis_index("gy")
    col_index = lax.axis_index("gx")
    device_count = row_count * col_count
    tile_count = tile_block.shape[0]
    slot_cap = max(2, 2 * tile_count // device_count)
    land_float = land_mask.astype(jnp.float32)
    flags = jnp.stack(
        [(col_index == col_count - 1).astype(jnp.int32), (row_index == row_count - 1).astype(jnp.int32)]
    )
    device_index = row_index * col_count + col_index
    first_block = device_index * block_rows
    f32 = jnp.float32
    grid_shape = jax.ShapeDtypeStruct((cell_rows, cell_cols), f32)
    smem_spec = pl.BlockSpec(memory_space=pltpu.SMEM)

    edges = pl.pallas_call(
        edge_kernel,
        out_shape=edge_shapes(cell_rows, cell_cols),
        in_specs=[smem_spec] + vmem_specs(6),
        out_specs=vmem_specs(4),
    )(flags, water_depth, flux_east, flux_south, bed_level, roughness, land_float)

    step_call = pl.pallas_call(
        step_kernel,
        out_shape=(grid_shape, grid_shape, grid_shape,
                   jax.ShapeDtypeStruct((cell_rows // STRIP, cell_cols), f32))
        + edge_shapes(cell_rows, cell_cols),
        in_specs=[smem_spec] + vmem_specs(10),
        out_specs=vmem_specs(8),
    )

    depth = water_depth
    tile_parts = []
    for step in range(STEPS):
        to_west, to_north, to_east, to_south = edges
        east_in = shifted(to_west, "gx", -1)
        south_in = shifted(to_north, "gy", -1)
        west_in = shifted(to_east, "gx", 1)
        north_in = shifted(to_south, "gy", 1)
        depth, flux_east, flux_south, tiles, *edges = step_call(
            flags, depth, flux_east, flux_south, bed_level, roughness, land_float,
            east_in, south_in, west_in, north_in,
        )
        tile_parts.append(tiles.reshape(cell_rows // STRIP, cell_cols // reach_width, reach_width)
                          .reshape(-1, reach_width))

    column_slots = row_count * slot_cap
    tile_owner = tile_block // block_rows
    owner_row = tile_owner // col_count
    owner_col = tile_owner % col_count
    owner_hits = (tile_owner[:, None] == lax.iota(jnp.int32, device_count)[None, :]).astype(
        jnp.int32
    )
    earlier = jnp.sum((jnp.cumsum(owner_hits, axis=0) - owner_hits) * owner_hits, axis=1)
    send_pos = owner_col * column_slots + owner_row * slot_cap + earlier
    column_ids = (owner_row * block_rows + tile_block % block_rows).astype(f32)
    send_ids = jnp.full((col_count * column_slots,), -1.0, f32).at[send_pos].set(column_ids)
    id_rows = -(-column_slots // reach_width)
    send_ids = jnp.pad(
        send_ids.reshape(col_count, column_slots),
        ((0, 0), (0, id_rows * reach_width - column_slots)),
        constant_values=-1.0,
    ).reshape(col_count, id_rows, reach_width)
    gather_onehot = (
        lax.iota(jnp.int32, col_count * column_slots)[:, None] == send_pos[None, :]
    ).astype(f32)
    packed = [
        jnp.dot(gather_onehot, part, precision=lax.Precision.HIGHEST).reshape(
            col_count, column_slots, reach_width
        )
        for part in tile_parts
    ]
    got = lax.all_to_all(jnp.concatenate(packed + [send_ids], axis=1), "gx", 0, 0, tiled=True)
    got_ids = got[:, STEPS * column_slots:].reshape(col_count, -1)[:, :column_slots].reshape(-1)
    targets = lax.iota(f32, row_count * block_rows)
    scatter_onehot = (targets[:, None] == got_ids[None, :]).astype(f32)
    by_column = jnp.stack(
        [
            jnp.dot(
                scatter_onehot,
                got[:, step * column_slots:(step + 1) * column_slots].reshape(-1, reach_width),
                precision=lax.Precision.HIGHEST,
            ).reshape(row_count, block_rows, reach_width)
            for step in range(STEPS)
        ],
        axis=1,
    )
    laterals = jnp.sum(lax.all_to_all(by_column, "gy", 0, 0, tiled=True), axis=0)

    for step in range(STEPS):
        ratio = reach_rate * jnp.power(storage, 2.0 / 3.0)
        outflow = storage * ratio / (1.0 + ratio)
        own_part = block_term(downstream, outflow, first_block, block_rows)
        ahead_part = block_term(downstream, outflow, first_block + block_rows, block_rows)
        upstream = own_part + shifted(ahead_part, ("gy", "gx"), 1)
        storage = storage - outflow + upstream + lateral_gain * laterals[step]
    return (depth, flux_east, flux_south, storage)


def solution(mesh):
    placed = (
        P("gy", "gx"),
        P("gy", "gx"),
        P("gy", "gx"),
        P("gy", "gx"),
        P("gy", "gx"),
        P("gy", "gx"),
        P(("gy", "gx")),
        P(("gy", "gx"), None),
        P(("gy", "gx"), None),
        P(("gy", "gx")),
    )
    return jax.shard_map(
        body,
        mesh=mesh,
        in_specs=placed,
        out_specs=(P("gy", "gx"), P("gy", "gx"), P("gy", "gx"), P(("gy", "gx"), None)),
        check_vma=False,
    )
```

```python
import functools

import jax
import jax.numpy as jnp
from jax import lax
from jax.experimental import pallas as pl
from jax.experimental.pallas import tpu as pltpu
from jax.sharding import PartitionSpec as P

STRIP = 8
STEPS = 2


rim_depth = 0.1
slope_gain = 0.1
friction_gain = 1.0
mass_gain = 0.05
drain_rate = 0.05
lateral_gain = 0.125


def shifted(value, axis, steps):
    count = lax.axis_size(axis)
    first, last = (max(0, -steps), min(count, count - steps))
    return lax.ppermute(value, axis, [(source, source + steps) for source in range(first, last)])


def face_update(flux, level, level_next, depth, depth_next, roughness, active):
    face_depth = rim_depth + 0.5 * (jnp.abs(depth) + jnp.abs(depth_next))
    drive = flux - slope_gain * face_depth * (level_next - level)
    damping = 1.0 + friction_gain * roughness * jnp.abs(flux) / jnp.power(face_depth, 7.0 / 3.0)
    return active * drive / damping


def block_term(target_ids, values, start, count):
    targets = start + lax.iota(jnp.int32, count)
    onehot = (target_ids[:, None] == targets[None, :]).astype(jnp.float32)
    return jnp.einsum("tb,tc->bc", onehot, values, precision=lax.Precision.HIGHEST)


def write_edges(level, depth, flux_e, flux_s, rough, eopen, sopen, to_west, to_north, to_east,
                to_south):
    to_west[:, 0:1] = level[:, 0:1]
    to_west[:, 1:2] = depth[:, 0:1]
    to_north[0:1, :] = level[0:1, :]
    to_north[1:2, :] = depth[0:1, :]
    to_east[:, 0:1] = flux_e[:, -1:]
    to_east[:, 1:2] = level[:, -1:]
    to_east[:, 2:3] = depth[:, -1:]
    to_east[:, 3:4] = rough[:, -1:]
    to_east[:, 4:5] = eopen[:, -1:]
    to_south[0:1, :] = flux_s[-1:, :]
    to_south[1:2, :] = level[-1:, :]
    to_south[2:3, :] = depth[-1:, :]
    to_south[3:4, :] = rough[-1:, :]
    to_south[4:5, :] = sopen[-1:, :]


def open_masks(flags_ref, land):
    ny, nx = land.shape
    col = lax.broadcasted_iota(jnp.int32, (ny, nx), 1)
    row = lax.broadcasted_iota(jnp.int32, (ny, nx), 0)
    eopen = jnp.where((col == nx - 1) & (flags_ref[0] == 1), 0.0, land)
    sopen = jnp.where((row == ny - 1) & (flags_ref[1] == 1), 0.0, land)
    return col, row, eopen, sopen


def edge_kernel(flags_ref, d_ref, land_ref, bed_first_col, bed_last_col, bed_first_row,
                bed_last_row, e_ref, s_ref, r_col, r_row,
                tile_out, to_west, to_north, to_east, to_south):
    ny, nx = d_ref.shape
    depth = d_ref[...]
    land = land_ref[...].astype(jnp.float32)
    drained = drain_rate * land * jnp.abs(depth)
    tile_out[...] = drained.reshape(ny // STRIP, STRIP, nx).sum(axis=1)
    _, _, eopen, sopen = open_masks(flags_ref, land)
    to_west[:, 0:1] = bed_first_col[:, 0:1] + depth[:, 0:1]
    to_west[:, 1:2] = depth[:, 0:1]
    to_north[0:1, :] = bed_first_row[0:1, :] + depth[0:1, :]
    to_north[1:2, :] = depth[0:1, :]
    to_east[:, 0:1] = e_ref[:, -1:]
    to_east[:, 1:2] = bed_last_col[:, -1:] + depth[:, -1:]
    to_east[:, 2:3] = depth[:, -1:]
    to_east[:, 3:4] = r_col[:, -1:]
    to_east[:, 4:5] = eopen[:, -1:]
    to_south[0:1, :] = s_ref[-1:, :]
    to_south[1:2, :] = bed_last_row[-1:, :] + depth[-1:, :]
    to_south[2:3, :] = depth[-1:, :]
    to_south[3:4, :] = r_row[-1:, :]
    to_south[4:5, :] = sopen[-1:, :]


def step_kernel(with_edges, flags_ref, d_ref, e_ref, s_ref, bed_ref, r_ref, land_ref,
                east_ref, south_ref, west_ref, north_ref,
                d_out, e_out, s_out, *more):
    ny, nx = d_ref.shape
    depth = d_ref[...]
    bed = bed_ref[...]
    land = land_ref[...].astype(jnp.float32)
    rough = r_ref[...]
    level = bed + depth
    col, row, eopen, sopen = open_masks(flags_ref, land)
    level_e = jnp.where(col == nx - 1, east_ref[:, 0:1], pltpu.roll(level, nx - 1, 1))
    depth_e = jnp.where(col == nx - 1, east_ref[:, 1:2], pltpu.roll(depth, nx - 1, 1))
    level_s = jnp.where(row == ny - 1, south_ref[0:1, :], pltpu.roll(level, ny - 1, 0))
    depth_s = jnp.where(row == ny - 1, south_ref[1:2, :], pltpu.roll(depth, ny - 1, 0))
    flux_e = face_update(e_ref[...], level, level_e, depth, depth_e, rough, eopen)
    flux_s = face_update(s_ref[...], level, level_s, depth, depth_s, rough, sopen)
    west_edge = face_update(
        west_ref[:, 0:1], west_ref[:, 1:2], level[:, 0:1], west_ref[:, 2:3], depth[:, 0:1],
        west_ref[:, 3:4], west_ref[:, 4:5],
    )
    north_edge = face_update(
        north_ref[0:1, :], north_ref[1:2, :], level[0:1, :], north_ref[2:3, :], depth[0:1, :],
        north_ref[3:4, :], north_ref[4:5, :],
    )
    west_flux = jnp.where(col == 0, west_edge, pltpu.roll(flux_e, 1, 1))
    north_flux = jnp.where(row == 0, north_edge, pltpu.roll(flux_s, 1, 0))
    drained = drain_rate * land * jnp.abs(depth)
    new_depth = depth - mass_gain * (flux_e - west_flux + (flux_s - north_flux)) - drained
    d_out[...] = new_depth
    e_out[...] = flux_e
    s_out[...] = flux_s
    if with_edges:
        tile_out, to_west, to_north, to_east, to_south = more
        next_drained = drain_rate * land * jnp.abs(new_depth)
        tile_out[...] = next_drained.reshape(ny // STRIP, STRIP, nx).sum(axis=1)
        write_edges(bed + new_depth, new_depth, flux_e, flux_s, rough, eopen, sopen,
                    to_west, to_north, to_east, to_south)


def edge_shapes(ny, nx):
    f32 = jnp.float32
    return (
        jax.ShapeDtypeStruct((ny, 2), f32),
        jax.ShapeDtypeStruct((2, nx), f32),
        jax.ShapeDtypeStruct((ny, 5), f32),
        jax.ShapeDtypeStruct((5, nx), f32),
    )


def vmem_specs(count):
    return [pl.BlockSpec(memory_space=pltpu.VMEM) for _ in range(count)]


def body(
    water_depth,
    flux_east,
    flux_south,
    bed_level,
    roughness,
    land_mask,
    tile_block,
    storage,
    reach_rate,
    downstream,
):
    cell_rows, cell_cols = water_depth.shape
    block_rows, reach_width = storage.shape
    row_count = lax.axis_size("gy")
    col_count = lax.axis_size("gx")
    row_index = lax.axis_index("gy")
    col_index = lax.axis_index("gx")
    device_count = row_count * col_count
    tile_count = tile_block.shape[0]
    slot_cap = max(2, 2 * tile_count // device_count)
    flags = jnp.stack(
        [(col_index == col_count - 1).astype(jnp.int32), (row_index == row_count - 1).astype(jnp.int32)]
    )
    device_index = row_index * col_count + col_index
    first_block = device_index * block_rows
    f32 = jnp.float32
    grid_shape = jax.ShapeDtypeStruct((cell_rows, cell_cols), f32)
    smem_spec = pl.BlockSpec(memory_space=pltpu.SMEM)

    col_blocks = cell_cols // 128
    row_blocks = cell_rows // 8
    col_spec = lambda k: pl.BlockSpec((cell_rows, 128), lambda i: (0, k))
    row_spec = lambda k: pl.BlockSpec((8, cell_cols), lambda i: (k, 0))
    tile_shape = jax.ShapeDtypeStruct((cell_rows // STRIP, cell_cols), f32)
    tiles, *edges = pl.pallas_call(
        edge_kernel,
        grid=(1,),
        out_shape=(tile_shape,) + edge_shapes(cell_rows, cell_cols),
        in_specs=[smem_spec] + vmem_specs(2)
        + [col_spec(0), col_spec(col_blocks - 1), row_spec(0), row_spec(row_blocks - 1),
           col_spec(col_blocks - 1), row_spec(row_blocks - 1),
           col_spec(col_blocks - 1), row_spec(row_blocks - 1)],
        out_specs=vmem_specs(5),
    )(flags, water_depth, land_mask, bed_level, bed_level, bed_level, bed_level,
      flux_east, flux_south, roughness, roughness)
    tile_parts = [tiles]

    def step_call(with_edges):
        outs = (grid_shape, grid_shape, grid_shape)
        if with_edges:
            outs = outs + (tile_shape,) + edge_shapes(cell_rows, cell_cols)
        return pl.pallas_call(
            functools.partial(step_kernel, with_edges),
            out_shape=outs,
            in_specs=[smem_spec] + vmem_specs(10),
            out_specs=vmem_specs(len(outs)),
        )

    column_slots = row_count * slot_cap
    tile_owner = tile_block // block_rows
    owner_row = tile_owner // col_count
    owner_col = tile_owner % col_count
    owner_hits = (tile_owner[:, None] == lax.iota(jnp.int32, device_count)[None, :]).astype(
        jnp.int32
    )
    earlier = jnp.sum((jnp.cumsum(owner_hits, axis=0) - owner_hits) * owner_hits, axis=1)
    send_pos = owner_col * column_slots + owner_row * slot_cap + earlier
    column_ids = (owner_row * block_rows + tile_block % block_rows).astype(f32)
    send_ids = jnp.full((col_count * column_slots,), -1.0, f32).at[send_pos].set(column_ids)
    id_rows = -(-column_slots // reach_width)
    send_ids = jnp.pad(
        send_ids.reshape(col_count, column_slots),
        ((0, 0), (0, id_rows * reach_width - column_slots)),
        constant_values=-1.0,
    ).reshape(col_count, id_rows, reach_width)
    gather_onehot = (
        lax.iota(jnp.int32, col_count * column_slots)[:, None] == send_pos[None, :]
    ).astype(f32)
    def start_lateral(parts):
        parts = [
            part.reshape(cell_rows // STRIP, cell_cols // reach_width, reach_width).reshape(
                -1, reach_width
            )
            for part in parts
        ]
        packed = [
            jnp.dot(gather_onehot, part, precision=lax.Precision.HIGHEST).reshape(
                col_count, column_slots, reach_width
            )
            for part in parts
        ]
        return jnp.concatenate(packed + [send_ids], axis=1)

    depth = water_depth
    for step in range(STEPS):
        to_west, to_north, to_east, to_south = edges
        east_in = shifted(to_west, "gx", -1)
        south_in = shifted(to_north, "gy", -1)
        west_in = shifted(to_east, "gx", 1)
        north_in = shifted(to_south, "gy", 1)
        last = step == STEPS - 1
        if last:
            lateral_started = start_lateral(tile_parts)
            east_in, south_in, west_in, north_in, lateral_started = lax.optimization_barrier(
                (east_in, south_in, west_in, north_in, lateral_started)
            )
        outs = step_call(not last)(
            flags, depth, flux_east, flux_south, bed_level, roughness, land_mask,
            east_in, south_in, west_in, north_in,
        )
        depth, flux_east, flux_south = outs[:3]
        if not last:
            tile_parts.append(outs[3])
            edges = outs[4:]

    got = lax.all_to_all(lateral_started, "gx", 0, 0, tiled=True)
    got_ids = got[:, STEPS * column_slots:].reshape(col_count, -1)[:, :column_slots].reshape(-1)
    targets = lax.iota(f32, row_count * block_rows)
    scatter_onehot = (targets[:, None] == got_ids[None, :]).astype(f32)
    by_column = jnp.stack(
        [
            jnp.dot(
                scatter_onehot,
                got[:, step * column_slots:(step + 1) * column_slots].reshape(-1, reach_width),
                precision=lax.Precision.HIGHEST,
            ).reshape(row_count, block_rows, reach_width)
            for step in range(STEPS)
        ],
        axis=1,
    )
    laterals = jnp.sum(lax.all_to_all(by_column, "gy", 0, 0, tiled=True), axis=0)

    for step in range(STEPS):
        ratio = reach_rate * jnp.power(storage, 2.0 / 3.0)
        outflow = storage * ratio / (1.0 + ratio)
        own_part = block_term(downstream, outflow, first_block, block_rows)
        ahead_part = block_term(downstream, outflow, first_block + block_rows, block_rows)
        upstream = own_part + shifted(ahead_part, ("gy", "gx"), 1)
        storage = storage - outflow + upstream + lateral_gain * laterals[step]
    return (depth, flux_east, flux_south, storage)


def solution(mesh):
    placed = (
        P("gy", "gx"),
        P("gy", "gx"),
        P("gy", "gx"),
        P("gy", "gx"),
        P("gy", "gx"),
        P("gy", "gx"),
        P(("gy", "gx")),
        P(("gy", "gx"), None),
        P(("gy", "gx"), None),
        P(("gy", "gx")),
    )
    return jax.shard_map(
        body,
        mesh=mesh,
        in_specs=placed,
        out_specs=(P("gy", "gx"), P("gy", "gx"), P("gy", "gx"), P(("gy", "gx"), None)),
        check_vma=False,
    )
```

```python
import functools

import jax
import jax.numpy as jnp
from jax import lax
from jax.experimental import pallas as pl
from jax.experimental.pallas import tpu as pltpu
from jax.sharding import PartitionSpec as P

STRIP = 8
STEPS = 2


rim_depth = 0.1
slope_gain = 0.1
friction_gain = 1.0
mass_gain = 0.05
drain_rate = 0.05
lateral_gain = 0.125


def shifted(value, axis, steps):
    count = lax.axis_size(axis)
    first, last = (max(0, -steps), min(count, count - steps))
    return lax.ppermute(value, axis, [(source, source + steps) for source in range(first, last)])


def face_update(flux, level, level_next, depth, depth_next, roughness, active):
    face_depth = rim_depth + 0.5 * (jnp.abs(depth) + jnp.abs(depth_next))
    drive = flux - slope_gain * face_depth * (level_next - level)
    damping = 1.0 + friction_gain * roughness * jnp.abs(flux) / jnp.power(face_depth, 7.0 / 3.0)
    return active * drive / damping


def block_term(target_ids, values, start, count):
    targets = start + lax.iota(jnp.int32, count)
    onehot = (target_ids[:, None] == targets[None, :]).astype(jnp.float32)
    return jnp.einsum("tb,tc->bc", onehot, values, precision=lax.Precision.HIGHEST)


def write_edges(level, depth, flux_e, flux_s, rough, eopen, sopen, to_west, to_north, to_east,
                to_south):
    to_west[:, 0:1] = level[:, 0:1]
    to_west[:, 1:2] = depth[:, 0:1]
    to_north[0:1, :] = level[0:1, :]
    to_north[1:2, :] = depth[0:1, :]
    to_east[:, 0:1] = flux_e[:, -1:]
    to_east[:, 1:2] = level[:, -1:]
    to_east[:, 2:3] = depth[:, -1:]
    to_east[:, 3:4] = rough[:, -1:]
    to_east[:, 4:5] = eopen[:, -1:]
    to_south[0:1, :] = flux_s[-1:, :]
    to_south[1:2, :] = level[-1:, :]
    to_south[2:3, :] = depth[-1:, :]
    to_south[3:4, :] = rough[-1:, :]
    to_south[4:5, :] = sopen[-1:, :]


def open_masks(flags_ref, land):
    ny, nx = land.shape
    col = lax.broadcasted_iota(jnp.int32, (ny, nx), 1)
    row = lax.broadcasted_iota(jnp.int32, (ny, nx), 0)
    eopen = jnp.where((col == nx - 1) & (flags_ref[0] == 1), 0.0, land)
    sopen = jnp.where((row == ny - 1) & (flags_ref[1] == 1), 0.0, land)
    return col, row, eopen, sopen


def edge_kernel(flags_ref, d_ref, land_ref, bed_first_col, bed_last_col, bed_first_row,
                bed_last_row, e_ref, s_ref, r_col, r_row,
                tile_out, to_west, to_north, to_east, to_south):
    ny, nx = d_ref.shape
    depth = d_ref[...]
    land = land_ref[...].astype(jnp.float32)
    drained = drain_rate * land * jnp.abs(depth)
    tile_out[...] = drained.reshape(ny // STRIP, STRIP, nx).sum(axis=1)
    _, _, eopen, sopen = open_masks(flags_ref, land)
    to_west[:, 0:1] = bed_first_col[:, 0:1] + depth[:, 0:1]
    to_west[:, 1:2] = depth[:, 0:1]
    to_north[0:1, :] = bed_first_row[0:1, :] + depth[0:1, :]
    to_north[1:2, :] = depth[0:1, :]
    to_east[:, 0:1] = e_ref[:, -1:]
    to_east[:, 1:2] = bed_last_col[:, -1:] + depth[:, -1:]
    to_east[:, 2:3] = depth[:, -1:]
    to_east[:, 3:4] = r_col[:, -1:]
    to_east[:, 4:5] = eopen[:, -1:]
    to_south[0:1, :] = s_ref[-1:, :]
    to_south[1:2, :] = bed_last_row[-1:, :] + depth[-1:, :]
    to_south[2:3, :] = depth[-1:, :]
    to_south[3:4, :] = r_row[-1:, :]
    to_south[4:5, :] = sopen[-1:, :]


def step_kernel(with_edges, flags_ref, d_ref, e_ref, s_ref, bed_ref, r_ref, land_ref,
                east_ref, south_ref, west_ref, north_ref,
                d_out, e_out, s_out, *more):
    ny, nx = d_ref.shape
    depth = d_ref[...]
    bed = bed_ref[...]
    land = land_ref[...].astype(jnp.float32)
    rough = r_ref[...]
    level = bed + depth
    col, row, eopen, sopen = open_masks(flags_ref, land)
    level_e = jnp.where(col == nx - 1, east_ref[:, 0:1], pltpu.roll(level, nx - 1, 1))
    depth_e = jnp.where(col == nx - 1, east_ref[:, 1:2], pltpu.roll(depth, nx - 1, 1))
    level_s = jnp.where(row == ny - 1, south_ref[0:1, :], pltpu.roll(level, ny - 1, 0))
    depth_s = jnp.where(row == ny - 1, south_ref[1:2, :], pltpu.roll(depth, ny - 1, 0))
    flux_e = face_update(e_ref[...], level, level_e, depth, depth_e, rough, eopen)
    flux_s = face_update(s_ref[...], level, level_s, depth, depth_s, rough, sopen)
    west_edge = face_update(
        west_ref[:, 0:1], west_ref[:, 1:2], level[:, 0:1], west_ref[:, 2:3], depth[:, 0:1],
        west_ref[:, 3:4], west_ref[:, 4:5],
    )
    north_edge = face_update(
        north_ref[0:1, :], north_ref[1:2, :], level[0:1, :], north_ref[2:3, :], depth[0:1, :],
        north_ref[3:4, :], north_ref[4:5, :],
    )
    west_flux = jnp.where(col == 0, west_edge, pltpu.roll(flux_e, 1, 1))
    north_flux = jnp.where(row == 0, north_edge, pltpu.roll(flux_s, 1, 0))
    drained = drain_rate * land * jnp.abs(depth)
    new_depth = depth - mass_gain * (flux_e - west_flux + (flux_s - north_flux)) - drained
    d_out[...] = new_depth
    e_out[...] = flux_e
    s_out[...] = flux_s
    if with_edges:
        tile_out, to_west, to_north, to_east, to_south = more
        next_drained = drain_rate * land * jnp.abs(new_depth)
        tile_out[...] = next_drained.reshape(ny // STRIP, STRIP, nx).sum(axis=1)
        write_edges(bed + new_depth, new_depth, flux_e, flux_s, rough, eopen, sopen,
                    to_west, to_north, to_east, to_south)


def edge_shapes(ny, nx):
    f32 = jnp.float32
    return (
        jax.ShapeDtypeStruct((ny, 2), f32),
        jax.ShapeDtypeStruct((2, nx), f32),
        jax.ShapeDtypeStruct((ny, 5), f32),
        jax.ShapeDtypeStruct((5, nx), f32),
    )


def vmem_specs(count):
    return [pl.BlockSpec(memory_space=pltpu.VMEM) for _ in range(count)]


def body(
    water_depth,
    flux_east,
    flux_south,
    bed_level,
    roughness,
    land_mask,
    tile_block,
    storage,
    reach_rate,
    downstream,
):
    cell_rows, cell_cols = water_depth.shape
    block_rows, reach_width = storage.shape
    row_count = lax.axis_size("gy")
    col_count = lax.axis_size("gx")
    row_index = lax.axis_index("gy")
    col_index = lax.axis_index("gx")
    device_count = row_count * col_count
    tile_count = tile_block.shape[0]
    slot_cap = max(2, 2 * tile_count // device_count)
    flags = jnp.stack(
        [(col_index == col_count - 1).astype(jnp.int32), (row_index == row_count - 1).astype(jnp.int32)]
    )
    device_index = row_index * col_count + col_index
    first_block = device_index * block_rows
    f32 = jnp.float32
    grid_shape = jax.ShapeDtypeStruct((cell_rows, cell_cols), f32)
    smem_spec = pl.BlockSpec(memory_space=pltpu.SMEM)

    col_blocks = cell_cols // 128
    row_blocks = cell_rows // 8
    col_spec = lambda k: pl.BlockSpec((cell_rows, 128), lambda i: (0, k))
    row_spec = lambda k: pl.BlockSpec((8, cell_cols), lambda i: (k, 0))
    tile_shape = jax.ShapeDtypeStruct((cell_rows // STRIP, cell_cols), f32)
    tiles, *edges = pl.pallas_call(
        edge_kernel,
        grid=(1,),
        out_shape=(tile_shape,) + edge_shapes(cell_rows, cell_cols),
        in_specs=[smem_spec] + vmem_specs(2)
        + [col_spec(0), col_spec(col_blocks - 1), row_spec(0), row_spec(row_blocks - 1),
           col_spec(col_blocks - 1), row_spec(row_blocks - 1),
           col_spec(col_blocks - 1), row_spec(row_blocks - 1)],
        out_specs=vmem_specs(5),
    )(flags, water_depth, land_mask, bed_level, bed_level, bed_level, bed_level,
      flux_east, flux_south, roughness, roughness)
    tile_parts = [tiles]

    def step_call(with_edges):
        outs = (grid_shape, grid_shape, grid_shape)
        if with_edges:
            outs = outs + (tile_shape,) + edge_shapes(cell_rows, cell_cols)
        return pl.pallas_call(
            functools.partial(step_kernel, with_edges),
            out_shape=outs,
            in_specs=[smem_spec] + vmem_specs(10),
            out_specs=vmem_specs(len(outs)),
        )

    tile_owner = tile_block // block_rows
    owner_hits = (tile_owner[:, None] == lax.iota(jnp.int32, device_count)[None, :]).astype(
        jnp.int32
    )
    earlier = jnp.sum((jnp.cumsum(owner_hits, axis=0) - owner_hits) * owner_hits, axis=1)
    send_pos = tile_owner * slot_cap + earlier
    local_ids = (tile_block % block_rows).astype(f32)
    send_ids = jnp.full((device_count * slot_cap,), -1.0, f32).at[send_pos].set(local_ids)
    id_rows = -(-slot_cap // reach_width)
    send_ids = jnp.pad(
        send_ids.reshape(device_count, slot_cap),
        ((0, 0), (0, id_rows * reach_width - slot_cap)),
        constant_values=-1.0,
    ).reshape(device_count, id_rows, reach_width)
    gather_onehot = (
        lax.iota(jnp.int32, device_count * slot_cap)[:, None] == send_pos[None, :]
    ).astype(f32)
    def start_lateral(parts):
        parts = [
            part.reshape(cell_rows // STRIP, cell_cols // reach_width, reach_width).reshape(
                -1, reach_width
            )
            for part in parts
        ]
        packed = [
            jnp.dot(gather_onehot, part, precision=lax.Precision.HIGHEST).reshape(
                device_count, slot_cap, reach_width
            )
            for part in parts
        ]
        return jnp.concatenate(packed + [send_ids], axis=1)

    depth = water_depth
    for step in range(STEPS):
        to_west, to_north, to_east, to_south = edges
        east_in = shifted(to_west, "gx", -1)
        south_in = shifted(to_north, "gy", -1)
        west_in = shifted(to_east, "gx", 1)
        north_in = shifted(to_south, "gy", 1)
        last = step == STEPS - 1
        if last:
            lateral_started = start_lateral(tile_parts)
            east_in, south_in, west_in, north_in, lateral_started = lax.optimization_barrier(
                (east_in, south_in, west_in, north_in, lateral_started)
            )
        outs = step_call(not last)(
            flags, depth, flux_east, flux_south, bed_level, roughness, land_mask,
            east_in, south_in, west_in, north_in,
        )
        depth, flux_east, flux_south = outs[:3]
        if not last:
            tile_parts.append(outs[3])
            edges = outs[4:]

    got = lax.all_to_all(lateral_started, ("gy", "gx"), 0, 0, tiled=True)
    got_ids = got[:, STEPS * slot_cap:].reshape(device_count, -1)[:, :slot_cap].reshape(-1)
    targets = lax.iota(f32, block_rows)
    scatter_onehot = (targets[:, None] == got_ids[None, :]).astype(f32)
    laterals = [
        jnp.dot(
            scatter_onehot,
            got[:, step * slot_cap:(step + 1) * slot_cap].reshape(-1, reach_width),
            precision=lax.Precision.HIGHEST,
        )
        for step in range(STEPS)
    ]

    for step in range(STEPS):
        ratio = reach_rate * jnp.power(storage, 2.0 / 3.0)
        outflow = storage * ratio / (1.0 + ratio)
        own_part = block_term(downstream, outflow, first_block, block_rows)
        ahead_part = block_term(downstream, outflow, first_block + block_rows, block_rows)
        upstream = own_part + shifted(ahead_part, ("gy", "gx"), 1)
        storage = storage - outflow + upstream + lateral_gain * laterals[step]
    return (depth, flux_east, flux_south, storage)


def solution(mesh):
    placed = (
        P("gy", "gx"),
        P("gy", "gx"),
        P("gy", "gx"),
        P("gy", "gx"),
        P("gy", "gx"),
        P("gy", "gx"),
        P(("gy", "gx")),
        P(("gy", "gx"), None),
        P(("gy", "gx"), None),
        P(("gy", "gx")),
    )
    return jax.shard_map(
        body,
        mesh=mesh,
        in_specs=placed,
        out_specs=(P("gy", "gx"), P("gy", "gx"), P("gy", "gx"), P(("gy", "gx"), None)),
        check_vma=False,
    )
```

```python
import functools

import jax
import jax.numpy as jnp
from jax import lax
from jax.experimental import pallas as pl
from jax.experimental.pallas import tpu as pltpu
from jax.sharding import PartitionSpec as P

STRIP = 8
STEPS = 2


rim_depth = 0.1
slope_gain = 0.1
friction_gain = 1.0
mass_gain = 0.05
drain_rate = 0.05
lateral_gain = 0.125


def shifted(value, axis, steps):
    count = lax.axis_size(axis)
    first, last = (max(0, -steps), min(count, count - steps))
    return lax.ppermute(value, axis, [(source, source + steps) for source in range(first, last)])


def face_update(flux, level, level_next, depth, depth_next, roughness, active):
    face_depth = rim_depth + 0.5 * (jnp.abs(depth) + jnp.abs(depth_next))
    drive = flux - slope_gain * face_depth * (level_next - level)
    damping = 1.0 + friction_gain * roughness * jnp.abs(flux) / jnp.power(face_depth, 7.0 / 3.0)
    return active * drive / damping


def block_term(target_ids, values, start, count):
    targets = start + lax.iota(jnp.int32, count)
    onehot = (target_ids[:, None] == targets[None, :]).astype(jnp.float32)
    return jnp.einsum("tb,tc->bc", onehot, values, precision=lax.Precision.HIGHEST)


def first_col_row(x):
    return jnp.transpose(x[:, :128])[0:1, :]


def last_col_row(x):
    return jnp.transpose(x[:, -128:])[127:128, :]


def rows_as_cols(msg):
    count, length = msg.shape
    pad = jnp.zeros((128 - count, length), jnp.float32)
    return jnp.transpose(jnp.concatenate([msg, pad], axis=0))


def write_edges(level, depth, flux_e, flux_s, rough, eopen, sopen, to_west, to_north, to_east,
                to_south):
    to_west[0:1, :] = first_col_row(level)
    to_west[1:2, :] = first_col_row(depth)
    to_north[0:1, :] = level[0:1, :]
    to_north[1:2, :] = depth[0:1, :]
    to_east[0:1, :] = last_col_row(flux_e)
    to_east[1:2, :] = last_col_row(level)
    to_east[2:3, :] = last_col_row(depth)
    to_east[3:4, :] = last_col_row(rough)
    to_east[4:5, :] = last_col_row(eopen)
    to_south[0:1, :] = flux_s[-1:, :]
    to_south[1:2, :] = level[-1:, :]
    to_south[2:3, :] = depth[-1:, :]
    to_south[3:4, :] = rough[-1:, :]
    to_south[4:5, :] = sopen[-1:, :]


def open_masks(flags_ref, land):
    ny, nx = land.shape
    col = lax.broadcasted_iota(jnp.int32, (ny, nx), 1)
    row = lax.broadcasted_iota(jnp.int32, (ny, nx), 0)
    eopen = jnp.where((col == nx - 1) & (flags_ref[0] == 1), 0.0, land)
    sopen = jnp.where((row == ny - 1) & (flags_ref[1] == 1), 0.0, land)
    return col, row, eopen, sopen


def edge_kernel(flags_ref, d_ref, land_ref, bed_first_col, bed_last_col, bed_first_row,
                bed_last_row, e_ref, s_ref, r_col, r_row,
                tile_out, to_west, to_north, to_east, to_south):
    ny, nx = d_ref.shape
    depth = d_ref[...]
    land = land_ref[...].astype(jnp.float32)
    drained = drain_rate * land * jnp.abs(depth)
    tile_out[...] = drained.reshape(ny // STRIP, STRIP, nx).sum(axis=1)
    _, _, eopen, sopen = open_masks(flags_ref, land)
    to_west[0:1, :] = first_col_row(bed_first_col[...] + depth[:, :128])
    to_west[1:2, :] = first_col_row(depth)
    to_north[0:1, :] = bed_first_row[0:1, :] + depth[0:1, :]
    to_north[1:2, :] = depth[0:1, :]
    to_east[0:1, :] = last_col_row(e_ref[...])
    to_east[1:2, :] = last_col_row(bed_last_col[...] + depth[:, -128:])
    to_east[2:3, :] = last_col_row(depth)
    to_east[3:4, :] = last_col_row(r_col[...])
    to_east[4:5, :] = last_col_row(eopen)
    to_south[0:1, :] = s_ref[-1:, :]
    to_south[1:2, :] = bed_last_row[-1:, :] + depth[-1:, :]
    to_south[2:3, :] = depth[-1:, :]
    to_south[3:4, :] = r_row[-1:, :]
    to_south[4:5, :] = sopen[-1:, :]


def step_kernel(with_edges, flags_ref, d_ref, e_ref, s_ref, bed_ref, r_ref, land_ref,
                east_ref, south_ref, west_ref, north_ref,
                d_out, e_out, s_out, *more):
    ny, nx = d_ref.shape
    depth = d_ref[...]
    bed = bed_ref[...]
    land = land_ref[...].astype(jnp.float32)
    rough = r_ref[...]
    level = bed + depth
    col, row, eopen, sopen = open_masks(flags_ref, land)
    east = rows_as_cols(east_ref[...])
    west = rows_as_cols(west_ref[...])
    level_e = jnp.where(col == nx - 1, east[:, 0:1], pltpu.roll(level, nx - 1, 1))
    depth_e = jnp.where(col == nx - 1, east[:, 1:2], pltpu.roll(depth, nx - 1, 1))
    level_s = jnp.where(row == ny - 1, south_ref[0:1, :], pltpu.roll(level, ny - 1, 0))
    depth_s = jnp.where(row == ny - 1, south_ref[1:2, :], pltpu.roll(depth, ny - 1, 0))
    flux_e = face_update(e_ref[...], level, level_e, depth, depth_e, rough, eopen)
    flux_s = face_update(s_ref[...], level, level_s, depth, depth_s, rough, sopen)
    west_edge = face_update(
        west[:, 0:1], west[:, 1:2], level[:, 0:1], west[:, 2:3], depth[:, 0:1],
        west[:, 3:4], west[:, 4:5],
    )
    north_edge = face_update(
        north_ref[0:1, :], north_ref[1:2, :], level[0:1, :], north_ref[2:3, :], depth[0:1, :],
        north_ref[3:4, :], north_ref[4:5, :],
    )
    west_flux = jnp.where(col == 0, west_edge, pltpu.roll(flux_e, 1, 1))
    north_flux = jnp.where(row == 0, north_edge, pltpu.roll(flux_s, 1, 0))
    drained = drain_rate * land * jnp.abs(depth)
    new_depth = depth - mass_gain * (flux_e - west_flux + (flux_s - north_flux)) - drained
    d_out[...] = new_depth
    e_out[...] = flux_e
    s_out[...] = flux_s
    if with_edges:
        tile_out, to_west, to_north, to_east, to_south = more
        next_drained = drain_rate * land * jnp.abs(new_depth)
        tile_out[...] = next_drained.reshape(ny // STRIP, STRIP, nx).sum(axis=1)
        write_edges(bed + new_depth, new_depth, flux_e, flux_s, rough, eopen, sopen,
                    to_west, to_north, to_east, to_south)


def edge_shapes(ny, nx):
    f32 = jnp.float32
    return (
        jax.ShapeDtypeStruct((2, ny), f32),
        jax.ShapeDtypeStruct((2, nx), f32),
        jax.ShapeDtypeStruct((5, ny), f32),
        jax.ShapeDtypeStruct((5, nx), f32),
    )


def vmem_specs(count):
    return [pl.BlockSpec(memory_space=pltpu.VMEM) for _ in range(count)]


def body(
    water_depth,
    flux_east,
    flux_south,
    bed_level,
    roughness,
    land_mask,
    tile_block,
    storage,
    reach_rate,
    downstream,
):
    cell_rows, cell_cols = water_depth.shape
    block_rows, reach_width = storage.shape
    row_count = lax.axis_size("gy")
    col_count = lax.axis_size("gx")
    row_index = lax.axis_index("gy")
    col_index = lax.axis_index("gx")
    device_count = row_count * col_count
    tile_count = tile_block.shape[0]
    slot_cap = max(2, 2 * tile_count // device_count)
    flags = jnp.stack(
        [(col_index == col_count - 1).astype(jnp.int32), (row_index == row_count - 1).astype(jnp.int32)]
    )
    device_index = row_index * col_count + col_index
    first_block = device_index * block_rows
    f32 = jnp.float32
    grid_shape = jax.ShapeDtypeStruct((cell_rows, cell_cols), f32)
    smem_spec = pl.BlockSpec(memory_space=pltpu.SMEM)

    col_blocks = cell_cols // 128
    row_blocks = cell_rows // 8
    col_spec = lambda k: pl.BlockSpec((cell_rows, 128), lambda i: (0, k))
    row_spec = lambda k: pl.BlockSpec((8, cell_cols), lambda i: (k, 0))
    tile_shape = jax.ShapeDtypeStruct((cell_rows // STRIP, cell_cols), f32)
    tiles, *edges = pl.pallas_call(
        edge_kernel,
        grid=(1,),
        out_shape=(tile_shape,) + edge_shapes(cell_rows, cell_cols),
        in_specs=[smem_spec] + vmem_specs(2)
        + [col_spec(0), col_spec(col_blocks - 1), row_spec(0), row_spec(row_blocks - 1),
           col_spec(col_blocks - 1), row_spec(row_blocks - 1),
           col_spec(col_blocks - 1), row_spec(row_blocks - 1)],
        out_specs=vmem_specs(5),
    )(flags, water_depth, land_mask, bed_level, bed_level, bed_level, bed_level,
      flux_east, flux_south, roughness, roughness)
    tile_parts = [tiles]

    def step_call(with_edges):
        outs = (grid_shape, grid_shape, grid_shape)
        if with_edges:
            outs = outs + (tile_shape,) + edge_shapes(cell_rows, cell_cols)
        return pl.pallas_call(
            functools.partial(step_kernel, with_edges),
            out_shape=outs,
            in_specs=[smem_spec] + vmem_specs(10),
            out_specs=vmem_specs(len(outs)),
        )

    tile_owner = tile_block // block_rows
    owner_hits = (tile_owner[:, None] == lax.iota(jnp.int32, device_count)[None, :]).astype(
        jnp.int32
    )
    earlier = jnp.sum((jnp.cumsum(owner_hits, axis=0) - owner_hits) * owner_hits, axis=1)
    send_pos = tile_owner * slot_cap + earlier
    local_ids = (tile_block % block_rows).astype(f32)
    send_ids = jnp.full((device_count * slot_cap,), -1.0, f32).at[send_pos].set(local_ids)
    id_rows = -(-slot_cap // reach_width)
    send_ids = jnp.pad(
        send_ids.reshape(device_count, slot_cap),
        ((0, 0), (0, id_rows * reach_width - slot_cap)),
        constant_values=-1.0,
    ).reshape(device_count, id_rows, reach_width)
    gather_onehot = (
        lax.iota(jnp.int32, device_count * slot_cap)[:, None] == send_pos[None, :]
    ).astype(f32)
    def start_lateral(parts):
        parts = [
            part.reshape(cell_rows // STRIP, cell_cols // reach_width, reach_width).reshape(
                -1, reach_width
            )
            for part in parts
        ]
        packed = [
            jnp.dot(gather_onehot, part, precision=lax.Precision.HIGHEST).reshape(
                device_count, slot_cap, reach_width
            )
            for part in parts
        ]
        return jnp.concatenate(packed + [send_ids], axis=1)

    depth = water_depth
    for step in range(STEPS):
        to_west, to_north, to_east, to_south = edges
        east_in = shifted(to_west, "gx", -1)
        south_in = shifted(to_north, "gy", -1)
        west_in = shifted(to_east, "gx", 1)
        north_in = shifted(to_south, "gy", 1)
        last = step == STEPS - 1
        if last:
            lateral_started = start_lateral(tile_parts)
            east_in, south_in, west_in, north_in, lateral_started = lax.optimization_barrier(
                (east_in, south_in, west_in, north_in, lateral_started)
            )
        outs = step_call(not last)(
            flags, depth, flux_east, flux_south, bed_level, roughness, land_mask,
            east_in, south_in, west_in, north_in,
        )
        depth, flux_east, flux_south = outs[:3]
        if not last:
            tile_parts.append(outs[3])
            edges = outs[4:]

    got = lax.all_to_all(lateral_started, ("gy", "gx"), 0, 0, tiled=True)
    got_ids = got[:, STEPS * slot_cap:].reshape(device_count, -1)[:, :slot_cap].reshape(-1)
    targets = lax.iota(f32, block_rows)
    scatter_onehot = (targets[:, None] == got_ids[None, :]).astype(f32)
    laterals = [
        jnp.dot(
            scatter_onehot,
            got[:, step * slot_cap:(step + 1) * slot_cap].reshape(-1, reach_width),
            precision=lax.Precision.HIGHEST,
        )
        for step in range(STEPS)
    ]

    for step in range(STEPS):
        ratio = reach_rate * jnp.power(storage, 2.0 / 3.0)
        outflow = storage * ratio / (1.0 + ratio)
        own_part = block_term(downstream, outflow, first_block, block_rows)
        ahead_part = block_term(downstream, outflow, first_block + block_rows, block_rows)
        upstream = own_part + shifted(ahead_part, ("gy", "gx"), 1)
        storage = storage - outflow + upstream + lateral_gain * laterals[step]
    return (depth, flux_east, flux_south, storage)


def solution(mesh):
    placed = (
        P("gy", "gx"),
        P("gy", "gx"),
        P("gy", "gx"),
        P("gy", "gx"),
        P("gy", "gx"),
        P("gy", "gx"),
        P(("gy", "gx")),
        P(("gy", "gx"), None),
        P(("gy", "gx"), None),
        P(("gy", "gx")),
    )
    return jax.shard_map(
        body,
        mesh=mesh,
        in_specs=placed,
        out_specs=(P("gy", "gx"), P("gy", "gx"), P("gy", "gx"), P(("gy", "gx"), None)),
        check_vma=False,
    )
```

```python
import functools

import jax
import jax.numpy as jnp
from jax import lax
from jax.experimental import pallas as pl
from jax.experimental.pallas import tpu as pltpu
from jax.sharding import PartitionSpec as P

STRIP = 8
STEPS = 2


rim_depth = 0.1
slope_gain = 0.1
friction_gain = 1.0
mass_gain = 0.05
drain_rate = 0.05
lateral_gain = 0.125


def shifted(value, axis, steps):
    count = lax.axis_size(axis)
    first, last = (max(0, -steps), min(count, count - steps))
    return lax.ppermute(value, axis, [(source, source + steps) for source in range(first, last)])


def face_update(flux, level, level_next, depth, depth_next, roughness, active):
    face_depth = rim_depth + 0.5 * (jnp.abs(depth) + jnp.abs(depth_next))
    drive = flux - slope_gain * face_depth * (level_next - level)
    damping = 1.0 + friction_gain * roughness * jnp.abs(flux) / jnp.power(face_depth, 7.0 / 3.0)
    return active * drive / damping


def block_term(target_ids, values, start, count):
    targets = start + lax.iota(jnp.int32, count)
    onehot = (target_ids[:, None] == targets[None, :]).astype(jnp.float32)
    return jnp.einsum("tb,tc->bc", onehot, values, precision=lax.Precision.HIGHEST)


def first_col_row(x):
    return jnp.transpose(x[:, :128])[0:1, :]


def last_col_row(x):
    return jnp.transpose(x[:, -128:])[127:128, :]


def rows_as_cols(msg):
    count, length = msg.shape
    pad = jnp.zeros((128 - count, length), jnp.float32)
    return jnp.transpose(jnp.concatenate([msg, pad], axis=0))


def write_edges(level, depth, flux_e, flux_s, rough, eopen, sopen, to_west, to_north, to_east,
                to_south):
    to_west[0:1, :] = first_col_row(level)
    to_west[1:2, :] = first_col_row(depth)
    to_north[0:1, :] = level[0:1, :]
    to_north[1:2, :] = depth[0:1, :]
    to_east[0:1, :] = last_col_row(flux_e)
    to_east[1:2, :] = last_col_row(level)
    to_east[2:3, :] = last_col_row(depth)
    to_east[3:4, :] = last_col_row(rough)
    to_east[4:5, :] = last_col_row(eopen)
    to_south[0:1, :] = flux_s[-1:, :]
    to_south[1:2, :] = level[-1:, :]
    to_south[2:3, :] = depth[-1:, :]
    to_south[3:4, :] = rough[-1:, :]
    to_south[4:5, :] = sopen[-1:, :]


def open_masks(flags_ref, land):
    ny, nx = land.shape
    col = lax.broadcasted_iota(jnp.int32, (ny, nx), 1)
    row = lax.broadcasted_iota(jnp.int32, (ny, nx), 0)
    eopen = jnp.where((col == nx - 1) & (flags_ref[0] == 1), 0.0, land)
    sopen = jnp.where((row == ny - 1) & (flags_ref[1] == 1), 0.0, land)
    return col, row, eopen, sopen


def edge_kernel(flags_ref, d_ref, land_ref, bed_first_col, bed_last_col, bed_first_row,
                bed_last_row, e_ref, s_ref, r_col, r_row,
                tile_out, to_west, to_north, to_east, to_south):
    ny, nx = d_ref.shape
    depth = d_ref[...]
    land = land_ref[...].astype(jnp.float32)
    drained = drain_rate * land * jnp.abs(depth)
    tile_out[...] = drained.reshape(ny // STRIP, STRIP, nx).sum(axis=1)
    _, _, eopen, sopen = open_masks(flags_ref, land)
    to_west[0:1, :] = first_col_row(bed_first_col[...] + depth[:, :128])
    to_west[1:2, :] = first_col_row(depth)
    to_north[0:1, :] = bed_first_row[0:1, :] + depth[0:1, :]
    to_north[1:2, :] = depth[0:1, :]
    to_east[0:1, :] = last_col_row(e_ref[...])
    to_east[1:2, :] = last_col_row(bed_last_col[...] + depth[:, -128:])
    to_east[2:3, :] = last_col_row(depth)
    to_east[3:4, :] = last_col_row(r_col[...])
    to_east[4:5, :] = last_col_row(eopen)
    to_south[0:1, :] = s_ref[-1:, :]
    to_south[1:2, :] = bed_last_row[-1:, :] + depth[-1:, :]
    to_south[2:3, :] = depth[-1:, :]
    to_south[3:4, :] = r_row[-1:, :]
    to_south[4:5, :] = sopen[-1:, :]


def step_kernel(with_edges, flags_ref, d_ref, e_ref, s_ref, bed_ref, r_ref, land_ref,
                east_ref, south_ref, west_ref, north_ref,
                d_out, e_out, s_out, *more):
    ny, nx = d_ref.shape
    depth = d_ref[...]
    bed = bed_ref[...]
    land = land_ref[...].astype(jnp.float32)
    rough = r_ref[...]
    level = bed + depth
    col, row, eopen, sopen = open_masks(flags_ref, land)
    east = rows_as_cols(east_ref[...])
    west = rows_as_cols(west_ref[...])
    level_e = jnp.where(col == nx - 1, east[:, 0:1], pltpu.roll(level, nx - 1, 1))
    depth_e = jnp.where(col == nx - 1, east[:, 1:2], pltpu.roll(depth, nx - 1, 1))
    level_s = jnp.where(row == ny - 1, south_ref[0:1, :], pltpu.roll(level, ny - 1, 0))
    depth_s = jnp.where(row == ny - 1, south_ref[1:2, :], pltpu.roll(depth, ny - 1, 0))
    flux_e = face_update(e_ref[...], level, level_e, depth, depth_e, rough, eopen)
    flux_s = face_update(s_ref[...], level, level_s, depth, depth_s, rough, sopen)
    west_edge = face_update(
        west[:, 0:1], west[:, 1:2], level[:, 0:1], west[:, 2:3], depth[:, 0:1],
        west[:, 3:4], west[:, 4:5],
    )
    north_edge = face_update(
        north_ref[0:1, :], north_ref[1:2, :], level[0:1, :], north_ref[2:3, :], depth[0:1, :],
        north_ref[3:4, :], north_ref[4:5, :],
    )
    west_flux = jnp.where(col == 0, west_edge, pltpu.roll(flux_e, 1, 1))
    north_flux = jnp.where(row == 0, north_edge, pltpu.roll(flux_s, 1, 0))
    drained = drain_rate * land * jnp.abs(depth)
    new_depth = depth - mass_gain * (flux_e - west_flux + (flux_s - north_flux)) - drained
    d_out[...] = new_depth
    e_out[...] = flux_e
    s_out[...] = flux_s
    if with_edges:
        tile_out, to_west, to_north, to_east, to_south = more
        next_drained = drain_rate * land * jnp.abs(new_depth)
        tile_out[...] = next_drained.reshape(ny // STRIP, STRIP, nx).sum(axis=1)
        write_edges(bed + new_depth, new_depth, flux_e, flux_s, rough, eopen, sopen,
                    to_west, to_north, to_east, to_south)


def edge_shapes(ny, nx):
    f32 = jnp.float32
    return (
        jax.ShapeDtypeStruct((2, ny), f32),
        jax.ShapeDtypeStruct((2, nx), f32),
        jax.ShapeDtypeStruct((5, ny), f32),
        jax.ShapeDtypeStruct((5, nx), f32),
    )


def vmem_specs(count):
    return [pl.BlockSpec(memory_space=pltpu.VMEM) for _ in range(count)]


def body(
    water_depth,
    flux_east,
    flux_south,
    bed_level,
    roughness,
    land_mask,
    tile_block,
    storage,
    reach_rate,
    downstream,
):
    cell_rows, cell_cols = water_depth.shape
    block_rows, reach_width = storage.shape
    row_count = lax.axis_size("gy")
    col_count = lax.axis_size("gx")
    row_index = lax.axis_index("gy")
    col_index = lax.axis_index("gx")
    device_count = row_count * col_count
    tile_count = tile_block.shape[0]
    slot_cap = max(2, 2 * tile_count // device_count)
    flags = jnp.stack(
        [(col_index == col_count - 1).astype(jnp.int32), (row_index == row_count - 1).astype(jnp.int32)]
    )
    device_index = row_index * col_count + col_index
    first_block = device_index * block_rows
    f32 = jnp.float32
    grid_shape = jax.ShapeDtypeStruct((cell_rows, cell_cols), f32)
    smem_spec = pl.BlockSpec(memory_space=pltpu.SMEM)

    col_blocks = cell_cols // 128
    row_blocks = cell_rows // 8
    col_spec = lambda k: pl.BlockSpec((cell_rows, 128), lambda i: (0, k))
    row_spec = lambda k: pl.BlockSpec((8, cell_cols), lambda i: (k, 0))
    tile_shape = jax.ShapeDtypeStruct((cell_rows // STRIP, cell_cols), f32)
    tiles, *edges = pl.pallas_call(
        edge_kernel,
        grid=(1,),
        out_shape=(tile_shape,) + edge_shapes(cell_rows, cell_cols),
        in_specs=[smem_spec] + vmem_specs(2)
        + [col_spec(0), col_spec(col_blocks - 1), row_spec(0), row_spec(row_blocks - 1),
           col_spec(col_blocks - 1), row_spec(row_blocks - 1),
           col_spec(col_blocks - 1), row_spec(row_blocks - 1)],
        out_specs=vmem_specs(5),
    )(flags, water_depth, land_mask, bed_level, bed_level, bed_level, bed_level,
      flux_east, flux_south, roughness, roughness)
    tile_parts = [tiles]

    def step_call(with_edges):
        outs = (grid_shape, grid_shape, grid_shape)
        if with_edges:
            outs = outs + (tile_shape,) + edge_shapes(cell_rows, cell_cols)
        return pl.pallas_call(
            functools.partial(step_kernel, with_edges),
            out_shape=outs,
            in_specs=[smem_spec] + vmem_specs(10),
            out_specs=vmem_specs(len(outs)),
        )

    tile_owner = tile_block // block_rows
    owner_hits = (tile_owner[:, None] == lax.iota(jnp.int32, device_count)[None, :]).astype(
        jnp.int32
    )
    earlier = jnp.sum((jnp.cumsum(owner_hits, axis=0) - owner_hits) * owner_hits, axis=1)
    send_pos = tile_owner * slot_cap + earlier
    local_ids = (tile_block % block_rows).astype(f32)
    send_ids = jnp.full((device_count * slot_cap,), -1.0, f32).at[send_pos].set(local_ids)
    id_rows = -(-slot_cap // reach_width)
    send_ids = jnp.pad(
        send_ids.reshape(device_count, slot_cap),
        ((0, 0), (0, id_rows * reach_width - slot_cap)),
        constant_values=-1.0,
    ).reshape(device_count, id_rows, reach_width)
    gather_onehot = (
        lax.iota(jnp.int32, device_count * slot_cap)[:, None] == send_pos[None, :]
    ).astype(f32)
    def start_lateral(parts, with_ids=True):
        parts = [
            part.reshape(cell_rows // STRIP, cell_cols // reach_width, reach_width).reshape(
                -1, reach_width
            )
            for part in parts
        ]
        packed = [
            jnp.dot(gather_onehot, part, precision=lax.Precision.HIGHEST).reshape(
                device_count, slot_cap, reach_width
            )
            for part in parts
        ]
        return jnp.concatenate(packed + ([send_ids] if with_ids else []), axis=1)

    got_first = lax.all_to_all(start_lateral(tile_parts), ("gy", "gx"), 0, 0, tiled=True)
    depth = water_depth
    for step in range(STEPS):
        to_west, to_north, to_east, to_south = edges
        east_in = shifted(to_west, "gx", -1)
        south_in = shifted(to_north, "gy", -1)
        west_in = shifted(to_east, "gx", 1)
        north_in = shifted(to_south, "gy", 1)
        last = step == STEPS - 1
        if last:
            lateral_started = start_lateral(tile_parts[1:], False)
            east_in, south_in, west_in, north_in, lateral_started, got_first = (
                lax.optimization_barrier(
                    (east_in, south_in, west_in, north_in, lateral_started, got_first)
                )
            )
        outs = step_call(not last)(
            flags, depth, flux_east, flux_south, bed_level, roughness, land_mask,
            east_in, south_in, west_in, north_in,
        )
        depth, flux_east, flux_south = outs[:3]
        if not last:
            tile_parts.append(outs[3])
            edges = outs[4:]

    got_second = lax.all_to_all(lateral_started, ("gy", "gx"), 0, 0, tiled=True)
    got_ids = got_first[:, slot_cap:].reshape(device_count, -1)[:, :slot_cap].reshape(-1)
    targets = lax.iota(f32, block_rows)
    scatter_onehot = (targets[:, None] == got_ids[None, :]).astype(f32)
    laterals = [
        jnp.dot(
            scatter_onehot,
            got[:, :slot_cap].reshape(-1, reach_width),
            precision=lax.Precision.HIGHEST,
        )
        for got in (got_first, got_second)
    ]

    for step in range(STEPS):
        ratio = reach_rate * jnp.power(storage, 2.0 / 3.0)
        outflow = storage * ratio / (1.0 + ratio)
        own_part = block_term(downstream, outflow, first_block, block_rows)
        ahead_part = block_term(downstream, outflow, first_block + block_rows, block_rows)
        upstream = own_part + shifted(ahead_part, ("gy", "gx"), 1)
        storage = storage - outflow + upstream + lateral_gain * laterals[step]
    return (depth, flux_east, flux_south, storage)


def solution(mesh):
    placed = (
        P("gy", "gx"),
        P("gy", "gx"),
        P("gy", "gx"),
        P("gy", "gx"),
        P("gy", "gx"),
        P("gy", "gx"),
        P(("gy", "gx")),
        P(("gy", "gx"), None),
        P(("gy", "gx"), None),
        P(("gy", "gx")),
    )
    return jax.shard_map(
        body,
        mesh=mesh,
        in_specs=placed,
        out_specs=(P("gy", "gx"), P("gy", "gx"), P("gy", "gx"), P(("gy", "gx"), None)),
        check_vma=False,
    )
```

```python
import functools

import jax
import jax.numpy as jnp
from jax import lax
from jax.experimental import pallas as pl
from jax.experimental.pallas import tpu as pltpu
from jax.sharding import PartitionSpec as P

STRIP = 8
STEPS = 2


rim_depth = 0.1
slope_gain = 0.1
friction_gain = 1.0
mass_gain = 0.05
drain_rate = 0.05
lateral_gain = 0.125


def shifted(value, axis, steps):
    count = lax.axis_size(axis)
    first, last = (max(0, -steps), min(count, count - steps))
    return lax.ppermute(value, axis, [(source, source + steps) for source in range(first, last)])


def face_update(flux, level, level_next, depth, depth_next, roughness, active):
    face_depth = rim_depth + 0.5 * (jnp.abs(depth) + jnp.abs(depth_next))
    drive = flux - slope_gain * face_depth * (level_next - level)
    inverse_power = jnp.exp((-7.0 / 3.0) * jnp.log(face_depth))
    damping = 1.0 + friction_gain * roughness * jnp.abs(flux) * inverse_power
    return active * drive / damping


def block_term(target_ids, values, start, count):
    targets = start + lax.iota(jnp.int32, count)
    onehot = (target_ids[:, None] == targets[None, :]).astype(jnp.float32)
    return jnp.einsum("tb,tc->bc", onehot, values, precision=lax.Precision.HIGHEST)


def first_col_row(x):
    return jnp.transpose(x[:, :128])[0:1, :]


def last_col_row(x):
    return jnp.transpose(x[:, -128:])[127:128, :]


def rows_as_cols(msg):
    count, length = msg.shape
    pad = jnp.zeros((128 - count, length), jnp.float32)
    return jnp.transpose(jnp.concatenate([msg, pad], axis=0))


def write_edges(level, depth, flux_e, flux_s, rough, eopen, sopen, to_west, to_north, to_east,
                to_south):
    to_west[0:1, :] = first_col_row(level)
    to_west[1:2, :] = first_col_row(depth)
    to_north[0:1, :] = level[0:1, :]
    to_north[1:2, :] = depth[0:1, :]
    to_east[0:1, :] = last_col_row(flux_e)
    to_east[1:2, :] = last_col_row(level)
    to_east[2:3, :] = last_col_row(depth)
    to_east[3:4, :] = last_col_row(rough)
    to_east[4:5, :] = last_col_row(eopen)
    to_south[0:1, :] = flux_s[-1:, :]
    to_south[1:2, :] = level[-1:, :]
    to_south[2:3, :] = depth[-1:, :]
    to_south[3:4, :] = rough[-1:, :]
    to_south[4:5, :] = sopen[-1:, :]


def open_masks(flags_ref, land):
    ny, nx = land.shape
    col = lax.broadcasted_iota(jnp.int32, (ny, nx), 1)
    row = lax.broadcasted_iota(jnp.int32, (ny, nx), 0)
    eopen = jnp.where((col == nx - 1) & (flags_ref[0] == 1), 0.0, land)
    sopen = jnp.where((row == ny - 1) & (flags_ref[1] == 1), 0.0, land)
    return col, row, eopen, sopen


def edge_kernel(flags_ref, d_ref, land_ref, bed_first_col, bed_last_col, bed_first_row,
                bed_last_row, e_ref, s_ref, r_col, r_row,
                tile_out, to_west, to_north, to_east, to_south):
    ny, nx = d_ref.shape
    depth = d_ref[...]
    land = land_ref[...].astype(jnp.float32)
    drained = drain_rate * land * jnp.abs(depth)
    tile_out[...] = drained.reshape(ny // STRIP, STRIP, nx).sum(axis=1)
    _, _, eopen, sopen = open_masks(flags_ref, land)
    to_west[0:1, :] = first_col_row(bed_first_col[...] + depth[:, :128])
    to_west[1:2, :] = first_col_row(depth)
    to_north[0:1, :] = bed_first_row[0:1, :] + depth[0:1, :]
    to_north[1:2, :] = depth[0:1, :]
    to_east[0:1, :] = last_col_row(e_ref[...])
    to_east[1:2, :] = last_col_row(bed_last_col[...] + depth[:, -128:])
    to_east[2:3, :] = last_col_row(depth)
    to_east[3:4, :] = last_col_row(r_col[...])
    to_east[4:5, :] = last_col_row(eopen)
    to_south[0:1, :] = s_ref[-1:, :]
    to_south[1:2, :] = bed_last_row[-1:, :] + depth[-1:, :]
    to_south[2:3, :] = depth[-1:, :]
    to_south[3:4, :] = r_row[-1:, :]
    to_south[4:5, :] = sopen[-1:, :]


def step_kernel(with_edges, flags_ref, d_ref, e_ref, s_ref, bed_ref, r_ref, land_ref,
                east_ref, south_ref, west_ref, north_ref,
                d_out, e_out, s_out, *more):
    ny, nx = d_ref.shape
    depth = d_ref[...]
    bed = bed_ref[...]
    land = land_ref[...].astype(jnp.float32)
    rough = r_ref[...]
    level = bed + depth
    col, row, eopen, sopen = open_masks(flags_ref, land)
    east = rows_as_cols(east_ref[...])
    west = rows_as_cols(west_ref[...])
    level_e = jnp.where(col == nx - 1, east[:, 0:1], pltpu.roll(level, nx - 1, 1))
    depth_e = jnp.where(col == nx - 1, east[:, 1:2], pltpu.roll(depth, nx - 1, 1))
    level_s = jnp.where(row == ny - 1, south_ref[0:1, :], pltpu.roll(level, ny - 1, 0))
    depth_s = jnp.where(row == ny - 1, south_ref[1:2, :], pltpu.roll(depth, ny - 1, 0))
    flux_e = face_update(e_ref[...], level, level_e, depth, depth_e, rough, eopen)
    flux_s = face_update(s_ref[...], level, level_s, depth, depth_s, rough, sopen)
    west_edge = face_update(
        west[:, 0:1], west[:, 1:2], level[:, 0:1], west[:, 2:3], depth[:, 0:1],
        west[:, 3:4], west[:, 4:5],
    )
    north_edge = face_update(
        north_ref[0:1, :], north_ref[1:2, :], level[0:1, :], north_ref[2:3, :], depth[0:1, :],
        north_ref[3:4, :], north_ref[4:5, :],
    )
    west_flux = jnp.where(col == 0, west_edge, pltpu.roll(flux_e, 1, 1))
    north_flux = jnp.where(row == 0, north_edge, pltpu.roll(flux_s, 1, 0))
    drained = drain_rate * land * jnp.abs(depth)
    new_depth = depth - mass_gain * (flux_e - west_flux + (flux_s - north_flux)) - drained
    d_out[...] = new_depth
    e_out[...] = flux_e
    s_out[...] = flux_s
    if with_edges:
        tile_out, to_west, to_north, to_east, to_south = more
        next_drained = drain_rate * land * jnp.abs(new_depth)
        tile_out[...] = next_drained.reshape(ny // STRIP, STRIP, nx).sum(axis=1)
        write_edges(bed + new_depth, new_depth, flux_e, flux_s, rough, eopen, sopen,
                    to_west, to_north, to_east, to_south)


def edge_shapes(ny, nx):
    f32 = jnp.float32
    return (
        jax.ShapeDtypeStruct((2, ny), f32),
        jax.ShapeDtypeStruct((2, nx), f32),
        jax.ShapeDtypeStruct((5, ny), f32),
        jax.ShapeDtypeStruct((5, nx), f32),
    )


def vmem_specs(count):
    return [pl.BlockSpec(memory_space=pltpu.VMEM) for _ in range(count)]


def body(
    water_depth,
    flux_east,
    flux_south,
    bed_level,
    roughness,
    land_mask,
    tile_block,
    storage,
    reach_rate,
    downstream,
):
    cell_rows, cell_cols = water_depth.shape
    block_rows, reach_width = storage.shape
    row_count = lax.axis_size("gy")
    col_count = lax.axis_size("gx")
    row_index = lax.axis_index("gy")
    col_index = lax.axis_index("gx")
    device_count = row_count * col_count
    tile_count = tile_block.shape[0]
    slot_cap = max(2, 2 * tile_count // device_count)
    flags = jnp.stack(
        [(col_index == col_count - 1).astype(jnp.int32), (row_index == row_count - 1).astype(jnp.int32)]
    )
    device_index = row_index * col_count + col_index
    first_block = device_index * block_rows
    f32 = jnp.float32
    grid_shape = jax.ShapeDtypeStruct((cell_rows, cell_cols), f32)
    smem_spec = pl.BlockSpec(memory_space=pltpu.SMEM)

    col_blocks = cell_cols // 128
    row_blocks = cell_rows // 8
    col_spec = lambda k: pl.BlockSpec((cell_rows, 128), lambda i: (0, k))
    row_spec = lambda k: pl.BlockSpec((8, cell_cols), lambda i: (k, 0))
    tile_shape = jax.ShapeDtypeStruct((cell_rows // STRIP, cell_cols), f32)
    tiles, *edges = pl.pallas_call(
        edge_kernel,
        grid=(1,),
        out_shape=(tile_shape,) + edge_shapes(cell_rows, cell_cols),
        in_specs=[smem_spec] + vmem_specs(2)
        + [col_spec(0), col_spec(col_blocks - 1), row_spec(0), row_spec(row_blocks - 1),
           col_spec(col_blocks - 1), row_spec(row_blocks - 1),
           col_spec(col_blocks - 1), row_spec(row_blocks - 1)],
        out_specs=vmem_specs(5),
    )(flags, water_depth, land_mask, bed_level, bed_level, bed_level, bed_level,
      flux_east, flux_south, roughness, roughness)
    tile_parts = [tiles]

    def step_call(with_edges):
        outs = (grid_shape, grid_shape, grid_shape)
        if with_edges:
            outs = outs + (tile_shape,) + edge_shapes(cell_rows, cell_cols)
        return pl.pallas_call(
            functools.partial(step_kernel, with_edges),
            out_shape=outs,
            in_specs=[smem_spec] + vmem_specs(10),
            out_specs=vmem_specs(len(outs)),
        )

    tile_owner = tile_block // block_rows
    owner_hits = (tile_owner[:, None] == lax.iota(jnp.int32, device_count)[None, :]).astype(
        jnp.int32
    )
    earlier = jnp.sum((jnp.cumsum(owner_hits, axis=0) - owner_hits) * owner_hits, axis=1)
    send_pos = tile_owner * slot_cap + earlier
    local_ids = (tile_block % block_rows).astype(f32)
    gather_onehot = (
        lax.iota(jnp.int32, device_count * slot_cap)[:, None] == send_pos[None, :]
    ).astype(f32)
    send_ids = jnp.dot(gather_onehot, local_ids + 1.0, precision=lax.Precision.HIGHEST) - 1.0
    id_rows = -(-slot_cap // reach_width)
    send_ids = jnp.pad(
        send_ids.reshape(device_count, slot_cap),
        ((0, 0), (0, id_rows * reach_width - slot_cap)),
        constant_values=-1.0,
    ).reshape(device_count, id_rows, reach_width)
    def start_lateral(parts, with_ids=True):
        parts = [
            part.reshape(cell_rows // STRIP, cell_cols // reach_width, reach_width).reshape(
                -1, reach_width
            )
            for part in parts
        ]
        packed = [
            jnp.dot(gather_onehot, part, precision=lax.Precision.HIGHEST).reshape(
                device_count, slot_cap, reach_width
            )
            for part in parts
        ]
        return jnp.concatenate(packed + ([send_ids] if with_ids else []), axis=1)

    got_first = lax.all_to_all(start_lateral(tile_parts), ("gy", "gx"), 0, 0, tiled=True)
    depth = water_depth
    for step in range(STEPS):
        to_west, to_north, to_east, to_south = edges
        east_in = shifted(to_west, "gx", -1)
        south_in = shifted(to_north, "gy", -1)
        west_in = shifted(to_east, "gx", 1)
        north_in = shifted(to_south, "gy", 1)
        last = step == STEPS - 1
        if last:
            lateral_started = start_lateral(tile_parts[1:], False)
            east_in, south_in, west_in, north_in, lateral_started, got_first = (
                lax.optimization_barrier(
                    (east_in, south_in, west_in, north_in, lateral_started, got_first)
                )
            )
        outs = step_call(not last)(
            flags, depth, flux_east, flux_south, bed_level, roughness, land_mask,
            east_in, south_in, west_in, north_in,
        )
        depth, flux_east, flux_south = outs[:3]
        if not last:
            tile_parts.append(outs[3])
            edges = outs[4:]

    got_second = lax.all_to_all(lateral_started, ("gy", "gx"), 0, 0, tiled=True)
    got_ids = got_first[:, slot_cap:].reshape(device_count, -1)[:, :slot_cap].reshape(-1)
    targets = lax.iota(f32, block_rows)
    scatter_onehot = (targets[:, None] == got_ids[None, :]).astype(f32)
    laterals = [
        jnp.dot(
            scatter_onehot,
            got[:, :slot_cap].reshape(-1, reach_width),
            precision=lax.Precision.HIGHEST,
        )
        for got in (got_first, got_second)
    ]

    for step in range(STEPS):
        ratio = reach_rate * jnp.power(storage, 2.0 / 3.0)
        outflow = storage * ratio / (1.0 + ratio)
        own_part = block_term(downstream, outflow, first_block, block_rows)
        ahead_part = block_term(downstream, outflow, first_block + block_rows, block_rows)
        upstream = own_part + shifted(ahead_part, ("gy", "gx"), 1)
        storage = storage - outflow + upstream + lateral_gain * laterals[step]
    return (depth, flux_east, flux_south, storage)


def solution(mesh):
    placed = (
        P("gy", "gx"),
        P("gy", "gx"),
        P("gy", "gx"),
        P("gy", "gx"),
        P("gy", "gx"),
        P("gy", "gx"),
        P(("gy", "gx")),
        P(("gy", "gx"), None),
        P(("gy", "gx"), None),
        P(("gy", "gx")),
    )
    return jax.shard_map(
        body,
        mesh=mesh,
        in_specs=placed,
        out_specs=(P("gy", "gx"), P("gy", "gx"), P("gy", "gx"), P(("gy", "gx"), None)),
        check_vma=False,
    )
```

```python
import functools

import jax
import jax.numpy as jnp
from jax import lax
from jax.experimental import pallas as pl
from jax.experimental.pallas import tpu as pltpu
from jax.sharding import PartitionSpec as P

STRIP = 8
STEPS = 2
SPAN = 8


rim_depth = 0.1
slope_gain = 0.1
friction_gain = 1.0
mass_gain = 0.05
drain_rate = 0.05
lateral_gain = 0.125


def shifted(value, axis, steps):
    count = lax.axis_size(axis)
    first, last = (max(0, -steps), min(count, count - steps))
    return lax.ppermute(value, axis, [(source, source + steps) for source in range(first, last)])


def face_update(flux, level, level_next, depth, depth_next, roughness, active):
    face_depth = rim_depth + 0.5 * (jnp.abs(depth) + jnp.abs(depth_next))
    drive = flux - slope_gain * face_depth * (level_next - level)
    inverse_power = jnp.exp((-7.0 / 3.0) * jnp.log(face_depth))
    damping = 1.0 + friction_gain * roughness * jnp.abs(flux) * inverse_power
    return active * drive / damping


def block_term(target_ids, values, start, count):
    targets = start + lax.iota(jnp.int32, count)
    onehot = (target_ids[:, None] == targets[None, :]).astype(jnp.float32)
    return jnp.einsum("tb,tc->bc", onehot, values, precision=lax.Precision.HIGHEST)


def first_col_row(x):
    return jnp.transpose(x[:, :128])[0:1, :]


def last_col_row(x):
    return jnp.transpose(x[:, -128:])[127:128, :]


def rows_as_cols(msg):
    count, length = msg.shape
    pad = jnp.zeros((128 - count, length), jnp.float32)
    return jnp.transpose(jnp.concatenate([msg, pad], axis=0))


def write_edges(level, depth, flux_e, flux_s, rough, eopen, sopen, to_west, to_north, to_east,
                to_south):
    to_west[0:1, :] = first_col_row(level)
    to_west[1:2, :] = first_col_row(depth)
    to_north[0:1, :] = level[0:1, :]
    to_north[1:2, :] = depth[0:1, :]
    to_east[0:1, :] = last_col_row(flux_e)
    to_east[1:2, :] = last_col_row(level)
    to_east[2:3, :] = last_col_row(depth)
    to_east[3:4, :] = last_col_row(rough)
    to_east[4:5, :] = last_col_row(eopen)
    to_south[0:1, :] = flux_s[-1:, :]
    to_south[1:2, :] = level[-1:, :]
    to_south[2:3, :] = depth[-1:, :]
    to_south[3:4, :] = rough[-1:, :]
    to_south[4:5, :] = sopen[-1:, :]


def open_masks(flags_ref, land):
    ny, nx = land.shape
    col = lax.broadcasted_iota(jnp.int32, (ny, nx), 1)
    row = lax.broadcasted_iota(jnp.int32, (ny, nx), 0)
    eopen = jnp.where((col == nx - 1) & (flags_ref[0] == 1), 0.0, land)
    sopen = jnp.where((row == ny - 1) & (flags_ref[1] == 1), 0.0, land)
    return col, row, eopen, sopen


def edge_kernel(flags_ref, d_ref, land_ref, bed_first_col, bed_last_col, bed_first_row,
                bed_last_row, e_ref, s_ref, r_col, r_row,
                tile_out, to_west, to_north, to_east, to_south):
    ny, nx = d_ref.shape
    depth = d_ref[...]
    land = land_ref[...].astype(jnp.float32)
    drained = drain_rate * land * jnp.abs(depth)
    tile_out[...] = drained.reshape(ny // STRIP, STRIP, nx).sum(axis=1)
    _, _, eopen, sopen = open_masks(flags_ref, land)
    to_west[0:1, :] = first_col_row(bed_first_col[...] + depth[:, :128])
    to_west[1:2, :] = first_col_row(depth)
    to_north[0:1, :] = bed_first_row[0:1, :] + depth[0:1, :]
    to_north[1:2, :] = depth[0:1, :]
    to_east[0:1, :] = last_col_row(e_ref[...])
    to_east[1:2, :] = last_col_row(bed_last_col[...] + depth[:, -128:])
    to_east[2:3, :] = last_col_row(depth)
    to_east[3:4, :] = last_col_row(r_col[...])
    to_east[4:5, :] = last_col_row(eopen)
    to_south[0:1, :] = s_ref[-1:, :]
    to_south[1:2, :] = bed_last_row[-1:, :] + depth[-1:, :]
    to_south[2:3, :] = depth[-1:, :]
    to_south[3:4, :] = r_row[-1:, :]
    to_south[4:5, :] = sopen[-1:, :]


def step_kernel(with_edges, flags_ref, d_ref, e_ref, s_ref, bed_ref, r_ref, land_ref,
                east_ref, south_ref, west_ref, north_ref,
                d_out, e_out, s_out, *more):
    ny, nx = d_ref.shape
    depth = d_ref[...]
    bed = bed_ref[...]
    land = land_ref[...].astype(jnp.float32)
    rough = r_ref[...]
    level = bed + depth
    col, row, eopen, sopen = open_masks(flags_ref, land)
    east = rows_as_cols(east_ref[...])
    west = rows_as_cols(west_ref[...])
    level_e = jnp.where(col == nx - 1, east[:, 0:1], pltpu.roll(level, nx - 1, 1))
    depth_e = jnp.where(col == nx - 1, east[:, 1:2], pltpu.roll(depth, nx - 1, 1))
    level_s = jnp.where(row == ny - 1, south_ref[0:1, :], pltpu.roll(level, ny - 1, 0))
    depth_s = jnp.where(row == ny - 1, south_ref[1:2, :], pltpu.roll(depth, ny - 1, 0))
    flux_e = face_update(e_ref[...], level, level_e, depth, depth_e, rough, eopen)
    flux_s = face_update(s_ref[...], level, level_s, depth, depth_s, rough, sopen)
    west_edge = face_update(
        west[:, 0:1], west[:, 1:2], level[:, 0:1], west[:, 2:3], depth[:, 0:1],
        west[:, 3:4], west[:, 4:5],
    )
    north_edge = face_update(
        north_ref[0:1, :], north_ref[1:2, :], level[0:1, :], north_ref[2:3, :], depth[0:1, :],
        north_ref[3:4, :], north_ref[4:5, :],
    )
    west_edge = jnp.where(flags_ref[2] == 1, 0.0, west_edge)
    west_flux = jnp.where(col == 0, west_edge, pltpu.roll(flux_e, 1, 1))
    north_flux = jnp.where(row == 0, north_edge, pltpu.roll(flux_s, 1, 0))
    drained = drain_rate * land * jnp.abs(depth)
    new_depth = depth - mass_gain * (flux_e - west_flux + (flux_s - north_flux)) - drained
    d_out[...] = new_depth
    e_out[...] = flux_e
    s_out[...] = flux_s
    if with_edges:
        tile_out, to_west, to_north, to_east, to_south = more
        next_drained = drain_rate * land * jnp.abs(new_depth)
        tile_out[...] = next_drained.reshape(ny // STRIP, STRIP, nx).sum(axis=1)
        write_edges(bed + new_depth, new_depth, flux_e, flux_s, rough, eopen, sopen,
                    to_west, to_north, to_east, to_south)


def edge_shapes(ny, nx):
    f32 = jnp.float32
    return (
        jax.ShapeDtypeStruct((2, ny), f32),
        jax.ShapeDtypeStruct((2, nx), f32),
        jax.ShapeDtypeStruct((5, ny), f32),
        jax.ShapeDtypeStruct((5, nx), f32),
    )


def vmem_specs(count):
    return [pl.BlockSpec(memory_space=pltpu.VMEM) for _ in range(count)]


def body(
    water_depth,
    flux_east,
    flux_south,
    bed_level,
    roughness,
    land_mask,
    tile_block,
    storage,
    reach_rate,
    downstream,
):
    cell_rows, cell_cols = water_depth.shape
    block_rows, reach_width = storage.shape
    row_count = lax.axis_size("gy")
    col_count = lax.axis_size("gx")
    row_index = lax.axis_index("gy")
    col_index = lax.axis_index("gx")
    device_count = row_count * col_count
    tile_count = tile_block.shape[0]
    slot_cap = max(2, 2 * tile_count // device_count)
    flags = jnp.stack(
        [
            (col_index == col_count - 1).astype(jnp.int32),
            (row_index == row_count - 1).astype(jnp.int32),
            (col_index == 0).astype(jnp.int32),
        ]
    )
    device_index = row_index * col_count + col_index
    first_block = device_index * block_rows
    f32 = jnp.float32
    grid_shape = jax.ShapeDtypeStruct((cell_rows, cell_cols), f32)
    smem_spec = pl.BlockSpec(memory_space=pltpu.SMEM)

    col_blocks = cell_cols // 128
    row_blocks = cell_rows // 8
    col_spec = lambda k: pl.BlockSpec((cell_rows, 128), lambda i: (0, k))
    row_spec = lambda k: pl.BlockSpec((8, cell_cols), lambda i: (k, 0))
    tile_shape = jax.ShapeDtypeStruct((cell_rows // STRIP, cell_cols), f32)
    tiles, *edges = pl.pallas_call(
        edge_kernel,
        grid=(1,),
        out_shape=(tile_shape,) + edge_shapes(cell_rows, cell_cols),
        in_specs=[smem_spec] + vmem_specs(2)
        + [col_spec(0), col_spec(col_blocks - 1), row_spec(0), row_spec(row_blocks - 1),
           col_spec(col_blocks - 1), row_spec(row_blocks - 1),
           col_spec(col_blocks - 1), row_spec(row_blocks - 1)],
        out_specs=vmem_specs(5),
    )(flags, water_depth, land_mask, bed_level, bed_level, bed_level, bed_level,
      flux_east, flux_south, roughness, roughness)
    tile_parts = [tiles]

    def step_call(with_edges):
        outs = (grid_shape, grid_shape, grid_shape)
        if with_edges:
            outs = outs + (tile_shape,) + edge_shapes(cell_rows, cell_cols)
        return pl.pallas_call(
            functools.partial(step_kernel, with_edges),
            out_shape=outs,
            in_specs=[smem_spec] + vmem_specs(10),
            out_specs=vmem_specs(len(outs)),
        )

    tile_owner = tile_block // block_rows
    owner_hits = (tile_owner[:, None] == lax.iota(jnp.int32, device_count)[None, :]).astype(
        jnp.int32
    )
    earlier = jnp.sum((jnp.cumsum(owner_hits, axis=0) - owner_hits) * owner_hits, axis=1)
    send_pos = tile_owner * slot_cap + earlier
    local_ids = (tile_block % block_rows).astype(f32)
    gather_onehot = (
        lax.iota(jnp.int32, device_count * slot_cap)[:, None] == send_pos[None, :]
    ).astype(f32)
    send_ids = jnp.dot(gather_onehot, local_ids + 1.0, precision=lax.Precision.HIGHEST) - 1.0
    id_rows = -(-slot_cap // reach_width)
    send_ids = jnp.pad(
        send_ids.reshape(device_count, slot_cap),
        ((0, 0), (0, id_rows * reach_width - slot_cap)),
        constant_values=-1.0,
    ).reshape(device_count, id_rows, reach_width)
    def start_lateral(parts, with_ids=True):
        parts = [
            part.reshape(cell_rows // STRIP, cell_cols // reach_width, reach_width).reshape(
                -1, reach_width
            )
            for part in parts
        ]
        packed = [
            jnp.dot(gather_onehot, part, precision=lax.Precision.HIGHEST).reshape(
                device_count, slot_cap, reach_width
            )
            for part in parts
        ]
        return jnp.concatenate(packed + ([send_ids] if with_ids else []), axis=1)

    first_rows = slot_cap + id_rows
    got_first = lax.all_to_all(
        start_lateral(tile_parts).reshape(device_count, first_rows * reach_width),
        ("gy", "gx"), 0, 0, tiled=True,
    ).reshape(device_count, first_rows, reach_width)

    def reach_outflow(storage):
        ratio = reach_rate * jnp.power(storage, 2.0 / 3.0)
        outflow = storage * ratio / (1.0 + ratio)
        own_part = block_term(downstream, outflow, first_block, block_rows)
        ahead_part = block_term(downstream, outflow, first_block + block_rows, SPAN)
        return outflow, own_part, ahead_part

    first_outflow = reach_outflow(storage)
    ahead_rows = SPAN * reach_width // cell_cols
    depth = water_depth
    for step in range(STEPS):
        to_west, to_north, to_east, to_south = edges
        east_in = shifted(to_west, "gx", -1)
        south_in = shifted(to_north, "gy", -1)
        if step == 0:
            joined = shifted(
                jnp.concatenate(
                    [to_east, first_outflow[2].reshape(ahead_rows, cell_cols)], axis=0
                ),
                ("gy", "gx"),
                1,
            )
            west_in = joined[: to_east.shape[0]]
            first_ahead = joined[to_east.shape[0]:].reshape(SPAN, reach_width)
        else:
            west_in = shifted(to_east, "gx", 1)
        north_in = shifted(to_south, "gy", 1)
        last = step == STEPS - 1
        if last:
            lateral_started = start_lateral(tile_parts[1:], False)
            east_in, south_in, west_in, north_in, lateral_started, got_first = (
                lax.optimization_barrier(
                    (east_in, south_in, west_in, north_in, lateral_started, got_first)
                )
            )
        outs = step_call(not last)(
            flags, depth, flux_east, flux_south, bed_level, roughness, land_mask,
            east_in, south_in, west_in, north_in,
        )
        depth, flux_east, flux_south = outs[:3]
        if not last:
            tile_parts.append(outs[3])
            edges = outs[4:]

    got_second = lax.all_to_all(lateral_started, ("gy", "gx"), 0, 0, tiled=True)
    got_ids = got_first[:, slot_cap:].reshape(device_count, -1)[:, :slot_cap].reshape(-1)
    targets = lax.iota(f32, block_rows)
    scatter_onehot = (targets[:, None] == got_ids[None, :]).astype(f32)
    laterals = [
        jnp.dot(
            scatter_onehot,
            got[:, :slot_cap].reshape(-1, reach_width),
            precision=lax.Precision.HIGHEST,
        )
        for got in (got_first, got_second)
    ]

    for step in range(STEPS):
        if step == 0:
            outflow, own_part, _ = first_outflow
            upstream = own_part + jnp.pad(first_ahead, ((0, block_rows - SPAN), (0, 0)))
        else:
            outflow, own_part, ahead_part = reach_outflow(storage)
            upstream = own_part + jnp.pad(
                shifted(ahead_part, ("gy", "gx"), 1), ((0, block_rows - SPAN), (0, 0))
            )
        storage = storage - outflow + upstream + lateral_gain * laterals[step]
    return (depth, flux_east, flux_south, storage)


def solution(mesh):
    placed = (
        P("gy", "gx"),
        P("gy", "gx"),
        P("gy", "gx"),
        P("gy", "gx"),
        P("gy", "gx"),
        P("gy", "gx"),
        P(("gy", "gx")),
        P(("gy", "gx"), None),
        P(("gy", "gx"), None),
        P(("gy", "gx")),
    )
    return jax.shard_map(
        body,
        mesh=mesh,
        in_specs=placed,
        out_specs=(P("gy", "gx"), P("gy", "gx"), P("gy", "gx"), P(("gy", "gx"), None)),
        check_vma=False,
    )
```

```python
import functools

import jax
import jax.numpy as jnp
from jax import lax
from jax.experimental import pallas as pl
from jax.experimental.pallas import tpu as pltpu
from jax.sharding import PartitionSpec as P

STRIP = 8
STEPS = 2
SPAN = 8


rim_depth = 0.1
slope_gain = 0.1
friction_gain = 1.0
mass_gain = 0.05
drain_rate = 0.05
lateral_gain = 0.125


def shifted(value, axis, steps):
    count = lax.axis_size(axis)
    first, last = (max(0, -steps), min(count, count - steps))
    return lax.ppermute(value, axis, [(source, source + steps) for source in range(first, last)])


def face_update(flux, level, level_next, depth, depth_next, roughness, active):
    face_depth = rim_depth + 0.5 * (jnp.abs(depth) + jnp.abs(depth_next))
    drive = flux - slope_gain * face_depth * (level_next - level)
    inverse_power = jnp.exp((-7.0 / 3.0) * jnp.log(face_depth))
    damping = 1.0 + friction_gain * roughness * jnp.abs(flux) * inverse_power
    return active * drive / damping


def block_term(target_ids, values, start, count):
    targets = start + lax.iota(jnp.int32, count)
    onehot = (target_ids[:, None] == targets[None, :]).astype(jnp.float32)
    return jnp.einsum("tb,tc->bc", onehot, values, precision=lax.Precision.HIGHEST)


def first_col_row(x):
    return jnp.transpose(x[:, :128])[0:1, :]


def last_col_row(x):
    return jnp.transpose(x[:, -128:])[127:128, :]


def rows_as_cols(msg):
    count, length = msg.shape
    pad = jnp.zeros((128 - count, length), jnp.float32)
    return jnp.transpose(jnp.concatenate([msg, pad], axis=0))


def write_edges(level, depth, flux_e, flux_s, rough, eopen, sopen, to_west, to_north, to_east,
                to_south):
    to_west[0:1, :] = first_col_row(level)
    to_west[1:2, :] = first_col_row(depth)
    to_north[0:1, :] = level[0:1, :]
    to_north[1:2, :] = depth[0:1, :]
    to_east[0:1, :] = last_col_row(flux_e)
    to_east[1:2, :] = last_col_row(level)
    to_east[2:3, :] = last_col_row(depth)
    to_east[3:4, :] = last_col_row(rough)
    to_east[4:5, :] = last_col_row(eopen)
    to_south[0:1, :] = flux_s[-1:, :]
    to_south[1:2, :] = level[-1:, :]
    to_south[2:3, :] = depth[-1:, :]
    to_south[3:4, :] = rough[-1:, :]
    to_south[4:5, :] = sopen[-1:, :]


def open_masks(flags_ref, land):
    ny, nx = land.shape
    col = lax.broadcasted_iota(jnp.int32, (ny, nx), 1)
    row = lax.broadcasted_iota(jnp.int32, (ny, nx), 0)
    eopen = jnp.where((col == nx - 1) & (flags_ref[0] == 1), 0.0, land)
    sopen = jnp.where((row == ny - 1) & (flags_ref[1] == 1), 0.0, land)
    return col, row, eopen, sopen


def edge_kernel(flags_ref, d_ref, land_ref, bed_first_col, bed_last_col, bed_first_row,
                bed_last_row, e_ref, s_ref, r_col, r_row,
                tile_out, to_west, to_north, to_east, to_south):
    ny, nx = d_ref.shape
    depth = d_ref[...]
    land = land_ref[...].astype(jnp.float32)
    drained = drain_rate * land * jnp.abs(depth)
    tile_out[...] = drained.reshape(ny // STRIP, STRIP, nx).sum(axis=1)
    _, _, eopen, sopen = open_masks(flags_ref, land)
    to_west[0:1, :] = first_col_row(bed_first_col[...] + depth[:, :128])
    to_west[1:2, :] = first_col_row(depth)
    to_north[0:1, :] = bed_first_row[0:1, :] + depth[0:1, :]
    to_north[1:2, :] = depth[0:1, :]
    to_east[0:1, :] = last_col_row(e_ref[...])
    to_east[1:2, :] = last_col_row(bed_last_col[...] + depth[:, -128:])
    to_east[2:3, :] = last_col_row(depth)
    to_east[3:4, :] = last_col_row(r_col[...])
    to_east[4:5, :] = last_col_row(eopen)
    to_south[0:1, :] = s_ref[-1:, :]
    to_south[1:2, :] = bed_last_row[-1:, :] + depth[-1:, :]
    to_south[2:3, :] = depth[-1:, :]
    to_south[3:4, :] = r_row[-1:, :]
    to_south[4:5, :] = sopen[-1:, :]


def step_kernel(with_edges, flags_ref, d_ref, e_ref, s_ref, bed_ref, r_ref, land_ref,
                east_ref, south_ref, west_ref, north_ref,
                d_out, e_out, s_out, *more):
    ny, nx = d_ref.shape
    depth = d_ref[...]
    bed = bed_ref[...]
    land = land_ref[...].astype(jnp.float32)
    rough = r_ref[...]
    level = bed + depth
    col, row, eopen, sopen = open_masks(flags_ref, land)
    east = rows_as_cols(east_ref[...])
    west = rows_as_cols(west_ref[...])
    level_e = jnp.where(col == nx - 1, east[:, 0:1], pltpu.roll(level, nx - 1, 1))
    depth_e = jnp.where(col == nx - 1, east[:, 1:2], pltpu.roll(depth, nx - 1, 1))
    level_s = jnp.where(row == ny - 1, south_ref[0:1, :], pltpu.roll(level, ny - 1, 0))
    depth_s = jnp.where(row == ny - 1, south_ref[1:2, :], pltpu.roll(depth, ny - 1, 0))
    flux_e = face_update(e_ref[...], level, level_e, depth, depth_e, rough, eopen)
    flux_s = face_update(s_ref[...], level, level_s, depth, depth_s, rough, sopen)
    west_edge = face_update(
        west[:, 0:1], west[:, 1:2], level[:, 0:1], west[:, 2:3], depth[:, 0:1],
        west[:, 3:4], west[:, 4:5],
    )
    north_edge = face_update(
        north_ref[0:1, :], north_ref[1:2, :], level[0:1, :], north_ref[2:3, :], depth[0:1, :],
        north_ref[3:4, :], north_ref[4:5, :],
    )
    west_edge = jnp.where(flags_ref[2] == 1, 0.0, west_edge)
    west_flux = jnp.where(col == 0, west_edge, pltpu.roll(flux_e, 1, 1))
    north_flux = jnp.where(row == 0, north_edge, pltpu.roll(flux_s, 1, 0))
    drained = drain_rate * land * jnp.abs(depth)
    new_depth = depth - mass_gain * (flux_e - west_flux + (flux_s - north_flux)) - drained
    d_out[...] = new_depth
    e_out[...] = flux_e
    s_out[...] = flux_s
    if with_edges:
        tile_out, to_west, to_north, to_east, to_south = more
        next_drained = drain_rate * land * jnp.abs(new_depth)
        tile_out[...] = next_drained.reshape(ny // STRIP, STRIP, nx).sum(axis=1)
        write_edges(bed + new_depth, new_depth, flux_e, flux_s, rough, eopen, sopen,
                    to_west, to_north, to_east, to_south)


def edge_shapes(ny, nx):
    f32 = jnp.float32
    return (
        jax.ShapeDtypeStruct((2, ny), f32),
        jax.ShapeDtypeStruct((2, nx), f32),
        jax.ShapeDtypeStruct((5, ny), f32),
        jax.ShapeDtypeStruct((5, nx), f32),
    )


def vmem_specs(count):
    return [pl.BlockSpec(memory_space=pltpu.VMEM) for _ in range(count)]


def body(
    water_depth,
    flux_east,
    flux_south,
    bed_level,
    roughness,
    land_mask,
    tile_block,
    storage,
    reach_rate,
    downstream,
):
    cell_rows, cell_cols = water_depth.shape
    block_rows, reach_width = storage.shape
    row_count = lax.axis_size("gy")
    col_count = lax.axis_size("gx")
    row_index = lax.axis_index("gy")
    col_index = lax.axis_index("gx")
    device_count = row_count * col_count
    tile_count = tile_block.shape[0]
    slot_cap = max(2, 2 * tile_count // device_count)
    flags = jnp.stack(
        [
            (col_index == col_count - 1).astype(jnp.int32),
            (row_index == row_count - 1).astype(jnp.int32),
            (col_index == 0).astype(jnp.int32),
        ]
    )
    device_index = row_index * col_count + col_index
    first_block = device_index * block_rows
    f32 = jnp.float32
    grid_shape = jax.ShapeDtypeStruct((cell_rows, cell_cols), f32)
    smem_spec = pl.BlockSpec(memory_space=pltpu.SMEM)

    col_blocks = cell_cols // 128
    row_blocks = cell_rows // 8
    col_spec = lambda k: pl.BlockSpec((cell_rows, 128), lambda i: (0, k))
    row_spec = lambda k: pl.BlockSpec((8, cell_cols), lambda i: (k, 0))
    tile_shape = jax.ShapeDtypeStruct((cell_rows // STRIP, cell_cols), f32)
    tiles, *edges = pl.pallas_call(
        edge_kernel,
        grid=(1,),
        out_shape=(tile_shape,) + edge_shapes(cell_rows, cell_cols),
        in_specs=[smem_spec] + vmem_specs(2)
        + [col_spec(0), col_spec(col_blocks - 1), row_spec(0), row_spec(row_blocks - 1),
           col_spec(col_blocks - 1), row_spec(row_blocks - 1),
           col_spec(col_blocks - 1), row_spec(row_blocks - 1)],
        out_specs=vmem_specs(5),
    )(flags, water_depth, land_mask, bed_level, bed_level, bed_level, bed_level,
      flux_east, flux_south, roughness, roughness)
    tile_parts = [tiles]

    def step_call(with_edges):
        outs = (grid_shape, grid_shape, grid_shape)
        if with_edges:
            outs = outs + (tile_shape,) + edge_shapes(cell_rows, cell_cols)
        return pl.pallas_call(
            functools.partial(step_kernel, with_edges),
            out_shape=outs,
            in_specs=[smem_spec] + vmem_specs(10),
            out_specs=vmem_specs(len(outs)),
        )

    tile_owner = tile_block // block_rows
    owner_hits = (tile_owner[:, None] == lax.iota(jnp.int32, device_count)[None, :]).astype(
        jnp.int32
    )
    earlier = jnp.sum((jnp.cumsum(owner_hits, axis=0) - owner_hits) * owner_hits, axis=1)
    send_pos = tile_owner * slot_cap + earlier
    local_ids = (tile_block % block_rows).astype(f32)
    gather_onehot = (
        lax.iota(jnp.int32, device_count * slot_cap)[:, None] == send_pos[None, :]
    ).astype(f32)
    send_ids = jnp.dot(gather_onehot, local_ids + 1.0, precision=lax.Precision.HIGHEST) - 1.0
    id_rows = -(-slot_cap // reach_width)
    send_ids = jnp.pad(
        send_ids.reshape(device_count, slot_cap),
        ((0, 0), (0, id_rows * reach_width - slot_cap)),
        constant_values=-1.0,
    ).reshape(device_count, id_rows, reach_width)
    def start_lateral(parts, with_ids=True):
        parts = [
            part.reshape(cell_rows // STRIP, cell_cols // reach_width, reach_width).reshape(
                -1, reach_width
            )
            for part in parts
        ]
        packed = [
            jnp.dot(gather_onehot, part, precision=lax.Precision.HIGHEST).reshape(
                device_count, slot_cap, reach_width
            )
            for part in parts
        ]
        return jnp.concatenate(packed + ([send_ids] if with_ids else []), axis=1)

    message_rows = STEPS * slot_cap + id_rows

    def reach_outflow(storage):
        ratio = reach_rate * jnp.power(storage, 2.0 / 3.0)
        outflow = storage * ratio / (1.0 + ratio)
        own_part = block_term(downstream, outflow, first_block, block_rows)
        ahead_part = block_term(downstream, outflow, first_block + block_rows, SPAN)
        return outflow, own_part, ahead_part

    first_outflow = reach_outflow(storage)
    ahead_rows = SPAN * reach_width // cell_cols
    depth = water_depth
    for step in range(STEPS):
        to_west, to_north, to_east, to_south = edges
        east_in = shifted(to_west, "gx", -1)
        south_in = shifted(to_north, "gy", -1)
        if step == 0:
            joined = shifted(
                jnp.concatenate(
                    [to_east, first_outflow[2].reshape(ahead_rows, cell_cols)], axis=0
                ),
                ("gy", "gx"),
                1,
            )
            west_in = joined[: to_east.shape[0]]
            first_ahead = joined[to_east.shape[0]:].reshape(SPAN, reach_width)
        else:
            west_in = shifted(to_east, "gx", 1)
        north_in = shifted(to_south, "gy", 1)
        last = step == STEPS - 1
        if last:
            lateral_started = start_lateral(tile_parts).reshape(
                device_count, message_rows * reach_width
            )
            east_in, south_in, west_in, north_in, lateral_started = lax.optimization_barrier(
                (east_in, south_in, west_in, north_in, lateral_started)
            )
        outs = step_call(not last)(
            flags, depth, flux_east, flux_south, bed_level, roughness, land_mask,
            east_in, south_in, west_in, north_in,
        )
        depth, flux_east, flux_south = outs[:3]
        if not last:
            tile_parts.append(outs[3])
            edges = outs[4:]

    got = lax.all_to_all(lateral_started, ("gy", "gx"), 0, 0, tiled=True).reshape(
        device_count, message_rows, reach_width
    )
    got_ids = got[:, STEPS * slot_cap:].reshape(device_count, -1)[:, :slot_cap].reshape(-1)
    targets = lax.iota(f32, block_rows)
    scatter_onehot = (targets[:, None] == got_ids[None, :]).astype(f32)
    laterals = [
        jnp.dot(
            scatter_onehot,
            got[:, step * slot_cap:(step + 1) * slot_cap].reshape(-1, reach_width),
            precision=lax.Precision.HIGHEST,
        )
        for step in range(STEPS)
    ]

    for step in range(STEPS):
        if step == 0:
            outflow, own_part, _ = first_outflow
            upstream = own_part + jnp.pad(first_ahead, ((0, block_rows - SPAN), (0, 0)))
        else:
            outflow, own_part, ahead_part = reach_outflow(storage)
            upstream = own_part + jnp.pad(
                shifted(ahead_part, ("gy", "gx"), 1), ((0, block_rows - SPAN), (0, 0))
            )
        storage = storage - outflow + upstream + lateral_gain * laterals[step]
    return (depth, flux_east, flux_south, storage)


def solution(mesh):
    placed = (
        P("gy", "gx"),
        P("gy", "gx"),
        P("gy", "gx"),
        P("gy", "gx"),
        P("gy", "gx"),
        P("gy", "gx"),
        P(("gy", "gx")),
        P(("gy", "gx"), None),
        P(("gy", "gx"), None),
        P(("gy", "gx")),
    )
    return jax.shard_map(
        body,
        mesh=mesh,
        in_specs=placed,
        out_specs=(P("gy", "gx"), P("gy", "gx"), P("gy", "gx"), P(("gy", "gx"), None)),
        check_vma=False,
    )
```

```python
import functools

import jax
import jax.numpy as jnp
from jax import lax
from jax.experimental import pallas as pl
from jax.experimental.pallas import tpu as pltpu
from jax.sharding import PartitionSpec as P

STRIP = 8
STEPS = 2
SPAN = 8


rim_depth = 0.1
slope_gain = 0.1
friction_gain = 1.0
mass_gain = 0.05
drain_rate = 0.05
lateral_gain = 0.125


def shifted(value, axis, steps):
    count = lax.axis_size(axis)
    first, last = (max(0, -steps), min(count, count - steps))
    return lax.ppermute(value, axis, [(source, source + steps) for source in range(first, last)])


def face_update(flux, level, level_next, depth, depth_next, roughness, active):
    face_depth = rim_depth + 0.5 * (jnp.abs(depth) + jnp.abs(depth_next))
    drive = flux - slope_gain * face_depth * (level_next - level)
    inverse_power = jnp.exp((-7.0 / 3.0) * jnp.log(face_depth))
    damping = 1.0 + friction_gain * roughness * jnp.abs(flux) * inverse_power
    return active * drive / damping


def block_term(target_ids, values, start, count):
    targets = start + lax.iota(jnp.int32, count)
    onehot = (target_ids[:, None] == targets[None, :]).astype(jnp.float32)
    return jnp.einsum("tb,tc->bc", onehot, values, precision=lax.Precision.HIGHEST)


def first_col_row(x):
    return jnp.transpose(x[:, :128])[0:1, :]


def last_col_row(x):
    return jnp.transpose(x[:, -128:])[127:128, :]


def rows_as_cols(msg):
    count, length = msg.shape
    pad = jnp.zeros((128 - count, length), jnp.float32)
    return jnp.transpose(jnp.concatenate([msg, pad], axis=0))


def write_edges(level, depth, flux_e, flux_s, rough, eopen, sopen, to_west, to_north, to_east,
                to_south):
    to_west[0:1, :] = first_col_row(level)
    to_west[1:2, :] = first_col_row(depth)
    to_north[0:1, :] = level[0:1, :]
    to_north[1:2, :] = depth[0:1, :]
    to_east[0:1, :] = last_col_row(flux_e)
    to_east[1:2, :] = last_col_row(level)
    to_east[2:3, :] = last_col_row(depth)
    to_east[3:4, :] = last_col_row(rough)
    to_east[4:5, :] = last_col_row(eopen)
    to_south[0:1, :] = flux_s[-1:, :]
    to_south[1:2, :] = level[-1:, :]
    to_south[2:3, :] = depth[-1:, :]
    to_south[3:4, :] = rough[-1:, :]
    to_south[4:5, :] = sopen[-1:, :]


def tile_rows(drained):
    ny, nx = drained.shape
    strips = drained.reshape(ny // STRIP, STRIP, nx).sum(axis=1)
    return jnp.concatenate([strips[:, k * 128:(k + 1) * 128] for k in range(nx // 128)], axis=0)


def open_masks(flags_ref, land):
    ny, nx = land.shape
    col = lax.broadcasted_iota(jnp.int32, (ny, nx), 1)
    row = lax.broadcasted_iota(jnp.int32, (ny, nx), 0)
    eopen = jnp.where((col == nx - 1) & (flags_ref[0] == 1), 0.0, land)
    sopen = jnp.where((row == ny - 1) & (flags_ref[1] == 1), 0.0, land)
    return col, row, eopen, sopen


def edge_kernel(flags_ref, d_ref, land_ref, bed_first_col, bed_last_col, bed_first_row,
                bed_last_row, e_ref, s_ref, r_col, r_row,
                tile_out, to_west, to_north, to_east, to_south):
    ny, nx = d_ref.shape
    depth = d_ref[...]
    land = land_ref[...].astype(jnp.float32)
    drained = drain_rate * land * jnp.abs(depth)
    tile_out[...] = tile_rows(drained)
    _, _, eopen, sopen = open_masks(flags_ref, land)
    to_west[0:1, :] = first_col_row(bed_first_col[...] + depth[:, :128])
    to_west[1:2, :] = first_col_row(depth)
    to_north[0:1, :] = bed_first_row[0:1, :] + depth[0:1, :]
    to_north[1:2, :] = depth[0:1, :]
    to_east[0:1, :] = last_col_row(e_ref[...])
    to_east[1:2, :] = last_col_row(bed_last_col[...] + depth[:, -128:])
    to_east[2:3, :] = last_col_row(depth)
    to_east[3:4, :] = last_col_row(r_col[...])
    to_east[4:5, :] = last_col_row(eopen)
    to_south[0:1, :] = s_ref[-1:, :]
    to_south[1:2, :] = bed_last_row[-1:, :] + depth[-1:, :]
    to_south[2:3, :] = depth[-1:, :]
    to_south[3:4, :] = r_row[-1:, :]
    to_south[4:5, :] = sopen[-1:, :]


def step_kernel(with_edges, flags_ref, d_ref, e_ref, s_ref, bed_ref, r_ref, land_ref,
                east_ref, south_ref, west_ref, north_ref,
                d_out, e_out, s_out, *more):
    ny, nx = d_ref.shape
    depth = d_ref[...]
    bed = bed_ref[...]
    land = land_ref[...].astype(jnp.float32)
    rough = r_ref[...]
    level = bed + depth
    col, row, eopen, sopen = open_masks(flags_ref, land)
    east = rows_as_cols(east_ref[...])
    west = rows_as_cols(west_ref[...])
    level_e = jnp.where(col == nx - 1, east[:, 0:1], pltpu.roll(level, nx - 1, 1))
    depth_e = jnp.where(col == nx - 1, east[:, 1:2], pltpu.roll(depth, nx - 1, 1))
    level_s = jnp.where(row == ny - 1, south_ref[0:1, :], pltpu.roll(level, ny - 1, 0))
    depth_s = jnp.where(row == ny - 1, south_ref[1:2, :], pltpu.roll(depth, ny - 1, 0))
    flux_e = face_update(e_ref[...], level, level_e, depth, depth_e, rough, eopen)
    flux_s = face_update(s_ref[...], level, level_s, depth, depth_s, rough, sopen)
    west_edge = face_update(
        west[:, 0:1], west[:, 1:2], level[:, 0:1], west[:, 2:3], depth[:, 0:1],
        west[:, 3:4], west[:, 4:5],
    )
    north_edge = face_update(
        north_ref[0:1, :], north_ref[1:2, :], level[0:1, :], north_ref[2:3, :], depth[0:1, :],
        north_ref[3:4, :], north_ref[4:5, :],
    )
    west_edge = jnp.where(flags_ref[2] == 1, 0.0, west_edge)
    west_flux = jnp.where(col == 0, west_edge, pltpu.roll(flux_e, 1, 1))
    north_flux = jnp.where(row == 0, north_edge, pltpu.roll(flux_s, 1, 0))
    drained = drain_rate * land * jnp.abs(depth)
    new_depth = depth - mass_gain * (flux_e - west_flux + (flux_s - north_flux)) - drained
    d_out[...] = new_depth
    e_out[...] = flux_e
    s_out[...] = flux_s
    if with_edges:
        tile_out, to_west, to_north, to_east, to_south = more
        next_drained = drain_rate * land * jnp.abs(new_depth)
        tile_out[...] = tile_rows(next_drained)
        write_edges(bed + new_depth, new_depth, flux_e, flux_s, rough, eopen, sopen,
                    to_west, to_north, to_east, to_south)


def edge_shapes(ny, nx):
    f32 = jnp.float32
    return (
        jax.ShapeDtypeStruct((2, ny), f32),
        jax.ShapeDtypeStruct((2, nx), f32),
        jax.ShapeDtypeStruct((5, ny), f32),
        jax.ShapeDtypeStruct((5, nx), f32),
    )


def vmem_specs(count):
    return [pl.BlockSpec(memory_space=pltpu.VMEM) for _ in range(count)]


def body(
    water_depth,
    flux_east,
    flux_south,
    bed_level,
    roughness,
    land_mask,
    tile_block,
    storage,
    reach_rate,
    downstream,
):
    cell_rows, cell_cols = water_depth.shape
    block_rows, reach_width = storage.shape
    row_count = lax.axis_size("gy")
    col_count = lax.axis_size("gx")
    row_index = lax.axis_index("gy")
    col_index = lax.axis_index("gx")
    device_count = row_count * col_count
    tile_count = tile_block.shape[0]
    slot_cap = max(2, 2 * tile_count // device_count)
    flags = jnp.stack(
        [
            (col_index == col_count - 1).astype(jnp.int32),
            (row_index == row_count - 1).astype(jnp.int32),
            (col_index == 0).astype(jnp.int32),
        ]
    )
    device_index = row_index * col_count + col_index
    first_block = device_index * block_rows
    f32 = jnp.float32
    grid_shape = jax.ShapeDtypeStruct((cell_rows, cell_cols), f32)
    smem_spec = pl.BlockSpec(memory_space=pltpu.SMEM)

    col_blocks = cell_cols // 128
    row_blocks = cell_rows // 8
    col_spec = lambda k: pl.BlockSpec((cell_rows, 128), lambda i: (0, k))
    row_spec = lambda k: pl.BlockSpec((8, cell_cols), lambda i: (k, 0))
    tile_shape = jax.ShapeDtypeStruct((cell_rows // STRIP * cell_cols // 128, 128), f32)
    tiles, *edges = pl.pallas_call(
        edge_kernel,
        grid=(1,),
        out_shape=(tile_shape,) + edge_shapes(cell_rows, cell_cols),
        in_specs=[smem_spec] + vmem_specs(2)
        + [col_spec(0), col_spec(col_blocks - 1), row_spec(0), row_spec(row_blocks - 1),
           col_spec(col_blocks - 1), row_spec(row_blocks - 1),
           col_spec(col_blocks - 1), row_spec(row_blocks - 1)],
        out_specs=vmem_specs(5),
    )(flags, water_depth, land_mask, bed_level, bed_level, bed_level, bed_level,
      flux_east, flux_south, roughness, roughness)
    tile_parts = [tiles]

    def step_call(with_edges):
        outs = (grid_shape, grid_shape, grid_shape)
        if with_edges:
            outs = outs + (tile_shape,) + edge_shapes(cell_rows, cell_cols)
        return pl.pallas_call(
            functools.partial(step_kernel, with_edges),
            out_shape=outs,
            in_specs=[smem_spec] + vmem_specs(10),
            out_specs=vmem_specs(len(outs)),
        )

    tile_owner = tile_block // block_rows
    owner_hits = (tile_owner[:, None] == lax.iota(jnp.int32, device_count)[None, :]).astype(
        jnp.int32
    )
    earlier = jnp.sum((jnp.cumsum(owner_hits, axis=0) - owner_hits) * owner_hits, axis=1)
    send_pos = tile_owner * slot_cap + earlier
    local_ids = (tile_block % block_rows).astype(f32)
    gather_onehot = (
        lax.iota(jnp.int32, device_count * slot_cap)[:, None] == send_pos[None, :]
    ).astype(f32)
    send_ids = jnp.dot(gather_onehot, local_ids + 1.0, precision=lax.Precision.HIGHEST) - 1.0
    lane_blocks = cell_cols // 128
    row_pos = send_pos.reshape(cell_rows // STRIP, lane_blocks).T.reshape(-1)
    row_onehot = (
        lax.iota(jnp.int32, device_count * slot_cap)[:, None] == row_pos[None, :]
    ).astype(f32)
    id_rows = -(-slot_cap // reach_width)
    send_ids = jnp.pad(
        send_ids.reshape(device_count, slot_cap),
        ((0, 0), (0, id_rows * reach_width - slot_cap)),
        constant_values=-1.0,
    ).reshape(device_count, id_rows, reach_width)
    def start_lateral(parts, with_ids=True):
        packed = [
            jnp.dot(row_onehot, part, precision=lax.Precision.HIGHEST).reshape(
                device_count, slot_cap, reach_width
            )
            for part in parts
        ]
        return jnp.concatenate(packed + ([send_ids] if with_ids else []), axis=1)

    first_rows = slot_cap + id_rows
    got_first = lax.all_to_all(
        start_lateral(tile_parts).reshape(device_count, first_rows * reach_width),
        ("gy", "gx"), 0, 0, tiled=True,
    ).reshape(device_count, first_rows, reach_width)

    def reach_outflow(storage):
        ratio = reach_rate * jnp.power(storage, 2.0 / 3.0)
        outflow = storage * ratio / (1.0 + ratio)
        own_part = block_term(downstream, outflow, first_block, block_rows)
        ahead_part = block_term(downstream, outflow, first_block + block_rows, SPAN)
        return outflow, own_part, ahead_part

    first_outflow = reach_outflow(storage)
    ahead_rows = SPAN * reach_width // cell_cols
    depth = water_depth
    for step in range(STEPS):
        to_west, to_north, to_east, to_south = edges
        east_in = shifted(to_west, "gx", -1)
        south_in = shifted(to_north, "gy", -1)
        if step == 0:
            joined = shifted(
                jnp.concatenate(
                    [to_east, first_outflow[2].reshape(ahead_rows, cell_cols)], axis=0
                ),
                ("gy", "gx"),
                1,
            )
            west_in = joined[: to_east.shape[0]]
            first_ahead = joined[to_east.shape[0]:].reshape(SPAN, reach_width)
        else:
            west_in = shifted(to_east, "gx", 1)
        north_in = shifted(to_south, "gy", 1)
        last = step == STEPS - 1
        if last:
            lateral_started = start_lateral(tile_parts[1:], False)
            east_in, south_in, west_in, north_in, lateral_started, got_first = (
                lax.optimization_barrier(
                    (east_in, south_in, west_in, north_in, lateral_started, got_first)
                )
            )
        outs = step_call(not last)(
            flags, depth, flux_east, flux_south, bed_level, roughness, land_mask,
            east_in, south_in, west_in, north_in,
        )
        depth, flux_east, flux_south = outs[:3]
        if not last:
            tile_parts.append(outs[3])
            edges = outs[4:]

    got_second = lax.all_to_all(lateral_started, ("gy", "gx"), 0, 0, tiled=True)
    got_ids = got_first[:, slot_cap:].reshape(device_count, -1)[:, :slot_cap].reshape(-1)
    targets = lax.iota(f32, block_rows)
    scatter_onehot = (targets[:, None] == got_ids[None, :]).astype(f32)
    laterals = [
        jnp.dot(
            scatter_onehot,
            got[:, :slot_cap].reshape(-1, reach_width),
            precision=lax.Precision.HIGHEST,
        )
        for got in (got_first, got_second)
    ]

    for step in range(STEPS):
        if step == 0:
            outflow, own_part, _ = first_outflow
            upstream = own_part + jnp.pad(first_ahead, ((0, block_rows - SPAN), (0, 0)))
        else:
            outflow, own_part, ahead_part = reach_outflow(storage)
            upstream = own_part + jnp.pad(
                shifted(ahead_part, ("gy", "gx"), 1), ((0, block_rows - SPAN), (0, 0))
            )
        storage = storage - outflow + upstream + lateral_gain * laterals[step]
    return (depth, flux_east, flux_south, storage)


def solution(mesh):
    placed = (
        P("gy", "gx"),
        P("gy", "gx"),
        P("gy", "gx"),
        P("gy", "gx"),
        P("gy", "gx"),
        P("gy", "gx"),
        P(("gy", "gx")),
        P(("gy", "gx"), None),
        P(("gy", "gx"), None),
        P(("gy", "gx")),
    )
    return jax.shard_map(
        body,
        mesh=mesh,
        in_specs=placed,
        out_specs=(P("gy", "gx"), P("gy", "gx"), P("gy", "gx"), P(("gy", "gx"), None)),
        check_vma=False,
    )
```

```python
import functools

import jax
import jax.numpy as jnp
from jax import lax
from jax.experimental import pallas as pl
from jax.experimental.pallas import tpu as pltpu
from jax.sharding import PartitionSpec as P

STRIP = 8
STEPS = 2
SPAN = 8


rim_depth = 0.1
slope_gain = 0.1
friction_gain = 1.0
mass_gain = 0.05
drain_rate = 0.05
lateral_gain = 0.125


def shifted(value, axis, steps):
    count = lax.axis_size(axis)
    first, last = (max(0, -steps), min(count, count - steps))
    return lax.ppermute(value, axis, [(source, source + steps) for source in range(first, last)])


def face_update(flux, level, level_next, depth, depth_next, roughness, active):
    face_depth = rim_depth + 0.5 * (jnp.abs(depth) + jnp.abs(depth_next))
    drive = flux - slope_gain * face_depth * (level_next - level)
    inverse_power = jnp.exp((-7.0 / 3.0) * jnp.log(face_depth))
    damping = 1.0 + friction_gain * roughness * jnp.abs(flux) * inverse_power
    return active * drive / damping


def block_term(target_ids, values, start, count):
    targets = start + lax.iota(jnp.int32, count)
    onehot = (target_ids[:, None] == targets[None, :]).astype(jnp.float32)
    return jnp.einsum("tb,tc->bc", onehot, values, precision=lax.Precision.HIGHEST)


def first_col_row(x):
    return jnp.transpose(x[:, :128])[0:1, :]


def last_col_row(x):
    return jnp.transpose(x[:, -128:])[127:128, :]


def rows_as_cols(msg):
    count, length = msg.shape
    pad = jnp.zeros((128 - count, length), jnp.float32)
    return jnp.transpose(jnp.concatenate([msg, pad], axis=0))


def write_edges(level, depth, flux_e, flux_s, rough, eopen, sopen, to_west, to_north, to_east,
                to_south):
    to_west[0:1, :] = first_col_row(level)
    to_west[1:2, :] = first_col_row(depth)
    to_north[0:1, :] = level[0:1, :]
    to_north[1:2, :] = depth[0:1, :]
    to_east[0:1, :] = last_col_row(flux_e)
    to_east[1:2, :] = last_col_row(level)
    to_east[2:3, :] = last_col_row(depth)
    to_east[3:4, :] = last_col_row(rough)
    to_east[4:5, :] = last_col_row(eopen)
    to_south[0:1, :] = flux_s[-1:, :]
    to_south[1:2, :] = level[-1:, :]
    to_south[2:3, :] = depth[-1:, :]
    to_south[3:4, :] = rough[-1:, :]
    to_south[4:5, :] = sopen[-1:, :]


def tile_rows(drained):
    ny, nx = drained.shape
    strips = drained.reshape(ny // STRIP, STRIP, nx).sum(axis=1)
    return jnp.concatenate([strips[:, k * 128:(k + 1) * 128] for k in range(nx // 128)], axis=0)


def pack_slots(slot_ref, tile_out, packed_out):
    packed_out[...] = jnp.zeros(packed_out.shape, jnp.float32)

    def place(row, carry):
        packed_out[pl.ds(slot_ref[row], 1), :] = tile_out[pl.ds(row, 1), :]
        return carry

    lax.fori_loop(0, tile_out.shape[0], place, 0)


def open_masks(flags_ref, land):
    ny, nx = land.shape
    col = lax.broadcasted_iota(jnp.int32, (ny, nx), 1)
    row = lax.broadcasted_iota(jnp.int32, (ny, nx), 0)
    eopen = jnp.where((col == nx - 1) & (flags_ref[0] == 1), 0.0, land)
    sopen = jnp.where((row == ny - 1) & (flags_ref[1] == 1), 0.0, land)
    return col, row, eopen, sopen


def edge_kernel(flags_ref, slot_ref, d_ref, land_ref, bed_first_col, bed_last_col, bed_first_row,
                bed_last_row, e_ref, s_ref, r_col, r_row,
                tile_out, packed_out, to_west, to_north, to_east, to_south):
    ny, nx = d_ref.shape
    depth = d_ref[...]
    land = land_ref[...].astype(jnp.float32)
    drained = drain_rate * land * jnp.abs(depth)
    tile_out[...] = tile_rows(drained)
    pack_slots(slot_ref, tile_out, packed_out)
    _, _, eopen, sopen = open_masks(flags_ref, land)
    to_west[0:1, :] = first_col_row(bed_first_col[...] + depth[:, :128])
    to_west[1:2, :] = first_col_row(depth)
    to_north[0:1, :] = bed_first_row[0:1, :] + depth[0:1, :]
    to_north[1:2, :] = depth[0:1, :]
    to_east[0:1, :] = last_col_row(e_ref[...])
    to_east[1:2, :] = last_col_row(bed_last_col[...] + depth[:, -128:])
    to_east[2:3, :] = last_col_row(depth)
    to_east[3:4, :] = last_col_row(r_col[...])
    to_east[4:5, :] = last_col_row(eopen)
    to_south[0:1, :] = s_ref[-1:, :]
    to_south[1:2, :] = bed_last_row[-1:, :] + depth[-1:, :]
    to_south[2:3, :] = depth[-1:, :]
    to_south[3:4, :] = r_row[-1:, :]
    to_south[4:5, :] = sopen[-1:, :]


def step_kernel(with_edges, flags_ref, slot_ref, d_ref, e_ref, s_ref, bed_ref, r_ref, land_ref,
                east_ref, south_ref, west_ref, north_ref,
                d_out, e_out, s_out, *more):
    ny, nx = d_ref.shape
    depth = d_ref[...]
    bed = bed_ref[...]
    land = land_ref[...].astype(jnp.float32)
    rough = r_ref[...]
    level = bed + depth
    col, row, eopen, sopen = open_masks(flags_ref, land)
    east = rows_as_cols(east_ref[...])
    west = rows_as_cols(west_ref[...])
    level_e = jnp.where(col == nx - 1, east[:, 0:1], pltpu.roll(level, nx - 1, 1))
    depth_e = jnp.where(col == nx - 1, east[:, 1:2], pltpu.roll(depth, nx - 1, 1))
    level_s = jnp.where(row == ny - 1, south_ref[0:1, :], pltpu.roll(level, ny - 1, 0))
    depth_s = jnp.where(row == ny - 1, south_ref[1:2, :], pltpu.roll(depth, ny - 1, 0))
    flux_e = face_update(e_ref[...], level, level_e, depth, depth_e, rough, eopen)
    flux_s = face_update(s_ref[...], level, level_s, depth, depth_s, rough, sopen)
    west_edge = face_update(
        west[:, 0:1], west[:, 1:2], level[:, 0:1], west[:, 2:3], depth[:, 0:1],
        west[:, 3:4], west[:, 4:5],
    )
    north_edge = face_update(
        north_ref[0:1, :], north_ref[1:2, :], level[0:1, :], north_ref[2:3, :], depth[0:1, :],
        north_ref[3:4, :], north_ref[4:5, :],
    )
    west_edge = jnp.where(flags_ref[2] == 1, 0.0, west_edge)
    west_flux = jnp.where(col == 0, west_edge, pltpu.roll(flux_e, 1, 1))
    north_flux = jnp.where(row == 0, north_edge, pltpu.roll(flux_s, 1, 0))
    drained = drain_rate * land * jnp.abs(depth)
    new_depth = depth - mass_gain * (flux_e - west_flux + (flux_s - north_flux)) - drained
    d_out[...] = new_depth
    e_out[...] = flux_e
    s_out[...] = flux_s
    if with_edges:
        tile_out, packed_out, to_west, to_north, to_east, to_south = more
        next_drained = drain_rate * land * jnp.abs(new_depth)
        tile_out[...] = tile_rows(next_drained)
        pack_slots(slot_ref, tile_out, packed_out)
        write_edges(bed + new_depth, new_depth, flux_e, flux_s, rough, eopen, sopen,
                    to_west, to_north, to_east, to_south)


def edge_shapes(ny, nx):
    f32 = jnp.float32
    return (
        jax.ShapeDtypeStruct((2, ny), f32),
        jax.ShapeDtypeStruct((2, nx), f32),
        jax.ShapeDtypeStruct((5, ny), f32),
        jax.ShapeDtypeStruct((5, nx), f32),
    )


def vmem_specs(count):
    return [pl.BlockSpec(memory_space=pltpu.VMEM) for _ in range(count)]


def body(
    water_depth,
    flux_east,
    flux_south,
    bed_level,
    roughness,
    land_mask,
    tile_block,
    storage,
    reach_rate,
    downstream,
):
    cell_rows, cell_cols = water_depth.shape
    block_rows, reach_width = storage.shape
    row_count = lax.axis_size("gy")
    col_count = lax.axis_size("gx")
    row_index = lax.axis_index("gy")
    col_index = lax.axis_index("gx")
    device_count = row_count * col_count
    tile_count = tile_block.shape[0]
    slot_cap = max(2, 2 * tile_count // device_count)
    flags = jnp.stack(
        [
            (col_index == col_count - 1).astype(jnp.int32),
            (row_index == row_count - 1).astype(jnp.int32),
            (col_index == 0).astype(jnp.int32),
        ]
    )
    device_index = row_index * col_count + col_index
    first_block = device_index * block_rows
    f32 = jnp.float32
    grid_shape = jax.ShapeDtypeStruct((cell_rows, cell_cols), f32)
    smem_spec = pl.BlockSpec(memory_space=pltpu.SMEM)

    tile_owner = tile_block // block_rows
    owner_hits = (tile_owner[:, None] == lax.iota(jnp.int32, device_count)[None, :]).astype(
        jnp.int32
    )
    earlier = jnp.sum((jnp.cumsum(owner_hits, axis=0) - owner_hits) * owner_hits, axis=1)
    send_pos = tile_owner * slot_cap + earlier
    local_ids = (tile_block % block_rows).astype(f32)
    gather_onehot = (
        lax.iota(jnp.int32, device_count * slot_cap)[:, None] == send_pos[None, :]
    ).astype(f32)
    send_ids = jnp.dot(gather_onehot, local_ids + 1.0, precision=lax.Precision.HIGHEST) - 1.0
    lane_blocks = cell_cols // 128
    row_pos = send_pos.reshape(cell_rows // STRIP, lane_blocks).T.reshape(-1)
    id_rows = -(-slot_cap // reach_width)
    send_ids = jnp.pad(
        send_ids.reshape(device_count, slot_cap),
        ((0, 0), (0, id_rows * reach_width - slot_cap)),
        constant_values=-1.0,
    ).reshape(device_count, id_rows, reach_width)
    col_blocks = cell_cols // 128
    row_blocks = cell_rows // 8
    col_spec = lambda k: pl.BlockSpec((cell_rows, 128), lambda i: (0, k))
    row_spec = lambda k: pl.BlockSpec((8, cell_cols), lambda i: (k, 0))
    tile_shape = jax.ShapeDtypeStruct((cell_rows // STRIP * cell_cols // 128, 128), f32)
    slot_shape = jax.ShapeDtypeStruct((device_count * slot_cap, reach_width), f32)
    _, slots, *edges = pl.pallas_call(
        edge_kernel,
        grid=(1,),
        out_shape=(tile_shape, slot_shape) + edge_shapes(cell_rows, cell_cols),
        in_specs=[smem_spec, smem_spec] + vmem_specs(2)
        + [col_spec(0), col_spec(col_blocks - 1), row_spec(0), row_spec(row_blocks - 1),
           col_spec(col_blocks - 1), row_spec(row_blocks - 1),
           col_spec(col_blocks - 1), row_spec(row_blocks - 1)],
        out_specs=vmem_specs(6),
    )(flags, row_pos, water_depth, land_mask, bed_level, bed_level, bed_level, bed_level,
      flux_east, flux_south, roughness, roughness)
    tile_parts = [slots]

    def step_call(with_edges):
        outs = (grid_shape, grid_shape, grid_shape)
        if with_edges:
            outs = outs + (tile_shape, slot_shape) + edge_shapes(cell_rows, cell_cols)
        return pl.pallas_call(
            functools.partial(step_kernel, with_edges),
            out_shape=outs,
            in_specs=[smem_spec, smem_spec] + vmem_specs(10),
            out_specs=vmem_specs(len(outs)),
        )

    def start_lateral(parts, with_ids=True):
        packed = [
            part.reshape(device_count, slot_cap, reach_width)
            for part in parts
        ]
        return jnp.concatenate(packed + ([send_ids] if with_ids else []), axis=1)

    first_rows = slot_cap + id_rows
    got_first = lax.all_to_all(
        start_lateral(tile_parts).reshape(device_count, first_rows * reach_width),
        ("gy", "gx"), 0, 0, tiled=True,
    ).reshape(device_count, first_rows, reach_width)

    def reach_outflow(storage):
        ratio = reach_rate * jnp.power(storage, 2.0 / 3.0)
        outflow = storage * ratio / (1.0 + ratio)
        own_part = block_term(downstream, outflow, first_block, block_rows)
        ahead_part = block_term(downstream, outflow, first_block + block_rows, SPAN)
        return outflow, own_part, ahead_part

    first_outflow = reach_outflow(storage)
    ahead_rows = SPAN * reach_width // cell_cols
    depth = water_depth
    for step in range(STEPS):
        to_west, to_north, to_east, to_south = edges
        east_in = shifted(to_west, "gx", -1)
        south_in = shifted(to_north, "gy", -1)
        if step == 0:
            joined = shifted(
                jnp.concatenate(
                    [to_east, first_outflow[2].reshape(ahead_rows, cell_cols)], axis=0
                ),
                ("gy", "gx"),
                1,
            )
            west_in = joined[: to_east.shape[0]]
            first_ahead = joined[to_east.shape[0]:].reshape(SPAN, reach_width)
        else:
            west_in = shifted(to_east, "gx", 1)
        north_in = shifted(to_south, "gy", 1)
        last = step == STEPS - 1
        if last:
            lateral_started = start_lateral(tile_parts[1:], False)
            east_in, south_in, west_in, north_in, lateral_started, got_first = (
                lax.optimization_barrier(
                    (east_in, south_in, west_in, north_in, lateral_started, got_first)
                )
            )
        outs = step_call(not last)(
            flags, row_pos, depth, flux_east, flux_south, bed_level, roughness, land_mask,
            east_in, south_in, west_in, north_in,
        )
        depth, flux_east, flux_south = outs[:3]
        if not last:
            tile_parts.append(outs[4])
            edges = outs[5:]

    got_second = lax.all_to_all(lateral_started, ("gy", "gx"), 0, 0, tiled=True)
    got_ids = got_first[:, slot_cap:].reshape(device_count, -1)[:, :slot_cap].reshape(-1)
    targets = lax.iota(f32, block_rows)
    scatter_onehot = (targets[:, None] == got_ids[None, :]).astype(f32)
    laterals = [
        jnp.dot(
            scatter_onehot,
            got[:, :slot_cap].reshape(-1, reach_width),
            precision=lax.Precision.HIGHEST,
        )
        for got in (got_first, got_second)
    ]

    for step in range(STEPS):
        if step == 0:
            outflow, own_part, _ = first_outflow
            upstream = own_part + jnp.pad(first_ahead, ((0, block_rows - SPAN), (0, 0)))
        else:
            outflow, own_part, ahead_part = reach_outflow(storage)
            upstream = own_part + jnp.pad(
                shifted(ahead_part, ("gy", "gx"), 1), ((0, block_rows - SPAN), (0, 0))
            )
        storage = storage - outflow + upstream + lateral_gain * laterals[step]
    return (depth, flux_east, flux_south, storage)


def solution(mesh):
    placed = (
        P("gy", "gx"),
        P("gy", "gx"),
        P("gy", "gx"),
        P("gy", "gx"),
        P("gy", "gx"),
        P("gy", "gx"),
        P(("gy", "gx")),
        P(("gy", "gx"), None),
        P(("gy", "gx"), None),
        P(("gy", "gx")),
    )
    return jax.shard_map(
        body,
        mesh=mesh,
        in_specs=placed,
        out_specs=(P("gy", "gx"), P("gy", "gx"), P("gy", "gx"), P(("gy", "gx"), None)),
        check_vma=False,
    )
```

```python
import functools

import jax
import jax.numpy as jnp
from jax import lax
from jax.experimental import pallas as pl
from jax.experimental.pallas import tpu as pltpu
from jax.sharding import PartitionSpec as P

STRIP = 8
STEPS = 2
SPAN = 8


rim_depth = 0.1
slope_gain = 0.1
friction_gain = 1.0
mass_gain = 0.05
drain_rate = 0.05
lateral_gain = 0.125


def shifted(value, axis, steps):
    count = lax.axis_size(axis)
    first, last = (max(0, -steps), min(count, count - steps))
    return lax.ppermute(value, axis, [(source, source + steps) for source in range(first, last)])


def face_update(flux, level, level_next, depth, depth_next, roughness, active):
    face_depth = rim_depth + 0.5 * (jnp.abs(depth) + jnp.abs(depth_next))
    drive = flux - slope_gain * face_depth * (level_next - level)
    inverse_power = jnp.exp((-7.0 / 3.0) * jnp.log(face_depth))
    damping = 1.0 + friction_gain * roughness * jnp.abs(flux) * inverse_power
    return active * drive / damping


def block_term(target_ids, values, start, count):
    targets = start + lax.iota(jnp.int32, count)
    onehot = (target_ids[:, None] == targets[None, :]).astype(jnp.float32)
    return jnp.einsum("tb,tc->bc", onehot, values, precision=lax.Precision.HIGHEST)


def first_col_row(x):
    return jnp.transpose(x[:, :128])[0:1, :]


def last_col_row(x):
    return jnp.transpose(x[:, -128:])[127:128, :]


def rows_as_cols(msg):
    count, length = msg.shape
    pad = jnp.zeros((128 - count, length), jnp.float32)
    return jnp.transpose(jnp.concatenate([msg, pad], axis=0))


def write_edges(level, depth, flux_e, flux_s, rough, eopen, sopen, to_west, to_north, to_east,
                to_south):
    to_west[0:1, :] = first_col_row(level)
    to_west[1:2, :] = first_col_row(depth)
    to_north[0:1, :] = level[0:1, :]
    to_north[1:2, :] = depth[0:1, :]
    to_east[0:1, :] = last_col_row(flux_e)
    to_east[1:2, :] = last_col_row(level)
    to_east[2:3, :] = last_col_row(depth)
    to_east[3:4, :] = last_col_row(rough)
    to_east[4:5, :] = last_col_row(eopen)
    to_south[0:1, :] = flux_s[-1:, :]
    to_south[1:2, :] = level[-1:, :]
    to_south[2:3, :] = depth[-1:, :]
    to_south[3:4, :] = rough[-1:, :]
    to_south[4:5, :] = sopen[-1:, :]


def tile_rows(drained):
    ny, nx = drained.shape
    strips = drained.reshape(ny // STRIP, STRIP, nx).sum(axis=1)
    return jnp.concatenate([strips[:, k * 128:(k + 1) * 128] for k in range(nx // 128)], axis=0)


def open_masks(flags_ref, land):
    ny, nx = land.shape
    col = lax.broadcasted_iota(jnp.int32, (ny, nx), 1)
    row = lax.broadcasted_iota(jnp.int32, (ny, nx), 0)
    eopen = jnp.where((col == nx - 1) & (flags_ref[0] == 1), 0.0, land)
    sopen = jnp.where((row == ny - 1) & (flags_ref[1] == 1), 0.0, land)
    return col, row, eopen, sopen


def edge_kernel(flags_ref, d_ref, land_ref, bed_first_col, bed_last_col, bed_first_row,
                bed_last_row, e_ref, s_ref, r_col, r_row,
                tile_out, to_west, to_north, to_east, to_south):
    ny, nx = d_ref.shape
    depth = d_ref[...]
    land = land_ref[...].astype(jnp.float32)
    drained = drain_rate * land * jnp.abs(depth)
    tile_out[...] = tile_rows(drained)
    _, _, eopen, sopen = open_masks(flags_ref, land)
    to_west[0:1, :] = first_col_row(bed_first_col[...] + depth[:, :128])
    to_west[1:2, :] = first_col_row(depth)
    to_north[0:1, :] = bed_first_row[0:1, :] + depth[0:1, :]
    to_north[1:2, :] = depth[0:1, :]
    to_east[0:1, :] = last_col_row(e_ref[...])
    to_east[1:2, :] = last_col_row(bed_last_col[...] + depth[:, -128:])
    to_east[2:3, :] = last_col_row(depth)
    to_east[3:4, :] = last_col_row(r_col[...])
    to_east[4:5, :] = last_col_row(eopen)
    to_south[0:1, :] = s_ref[-1:, :]
    to_south[1:2, :] = bed_last_row[-1:, :] + depth[-1:, :]
    to_south[2:3, :] = depth[-1:, :]
    to_south[3:4, :] = r_row[-1:, :]
    to_south[4:5, :] = sopen[-1:, :]


def step_kernel(with_edges, flags_ref, d_ref, e_ref, s_ref, bed_ref, r_ref, land_ref,
                east_ref, south_ref, west_ref, north_ref,
                d_out, e_out, s_out, *more):
    ny, nx = d_ref.shape
    depth = d_ref[...]
    bed = bed_ref[...]
    land = land_ref[...].astype(jnp.float32)
    rough = r_ref[...]
    level = bed + depth
    col, row, eopen, sopen = open_masks(flags_ref, land)
    east = rows_as_cols(east_ref[...])
    west = rows_as_cols(west_ref[...])
    level_e = jnp.where(col == nx - 1, east[:, 0:1], pltpu.roll(level, nx - 1, 1))
    depth_e = jnp.where(col == nx - 1, east[:, 1:2], pltpu.roll(depth, nx - 1, 1))
    level_s = jnp.where(row == ny - 1, south_ref[0:1, :], pltpu.roll(level, ny - 1, 0))
    depth_s = jnp.where(row == ny - 1, south_ref[1:2, :], pltpu.roll(depth, ny - 1, 0))
    flux_e = face_update(e_ref[...], level, level_e, depth, depth_e, rough, eopen)
    flux_s = face_update(s_ref[...], level, level_s, depth, depth_s, rough, sopen)
    west_edge = face_update(
        west[:, 0:1], west[:, 1:2], level[:, 0:1], west[:, 2:3], depth[:, 0:1],
        west[:, 3:4], west[:, 4:5],
    )
    north_edge = face_update(
        north_ref[0:1, :], north_ref[1:2, :], level[0:1, :], north_ref[2:3, :], depth[0:1, :],
        north_ref[3:4, :], north_ref[4:5, :],
    )
    west_edge = jnp.where(flags_ref[2] == 1, 0.0, west_edge)
    west_flux = jnp.where(col == 0, west_edge, pltpu.roll(flux_e, 1, 1))
    north_flux = jnp.where(row == 0, north_edge, pltpu.roll(flux_s, 1, 0))
    drained = drain_rate * land * jnp.abs(depth)
    new_depth = depth - mass_gain * (flux_e - west_flux + (flux_s - north_flux)) - drained
    d_out[...] = new_depth
    e_out[...] = flux_e
    s_out[...] = flux_s
    if with_edges:
        tile_out, to_west, to_north, to_east, to_south = more
        next_drained = drain_rate * land * jnp.abs(new_depth)
        tile_out[...] = tile_rows(next_drained)
        write_edges(bed + new_depth, new_depth, flux_e, flux_s, rough, eopen, sopen,
                    to_west, to_north, to_east, to_south)


def edge_shapes(ny, nx):
    f32 = jnp.float32
    return (
        jax.ShapeDtypeStruct((2, ny), f32),
        jax.ShapeDtypeStruct((2, nx), f32),
        jax.ShapeDtypeStruct((5, ny), f32),
        jax.ShapeDtypeStruct((5, nx), f32),
    )


def vmem_specs(count):
    return [pl.BlockSpec(memory_space=pltpu.VMEM) for _ in range(count)]


def body(
    water_depth,
    flux_east,
    flux_south,
    bed_level,
    roughness,
    land_mask,
    tile_block,
    storage,
    reach_rate,
    downstream,
):
    cell_rows, cell_cols = water_depth.shape
    block_rows, reach_width = storage.shape
    row_count = lax.axis_size("gy")
    col_count = lax.axis_size("gx")
    row_index = lax.axis_index("gy")
    col_index = lax.axis_index("gx")
    device_count = row_count * col_count
    tile_count = tile_block.shape[0]
    slot_cap = max(2, 2 * tile_count // device_count)
    flags = jnp.stack(
        [
            (col_index == col_count - 1).astype(jnp.int32),
            (row_index == row_count - 1).astype(jnp.int32),
            (col_index == 0).astype(jnp.int32),
        ]
    )
    device_index = row_index * col_count + col_index
    first_block = device_index * block_rows
    f32 = jnp.float32
    grid_shape = jax.ShapeDtypeStruct((cell_rows, cell_cols), f32)
    smem_spec = pl.BlockSpec(memory_space=pltpu.SMEM)

    col_blocks = cell_cols // 128
    row_blocks = cell_rows // 8
    col_spec = lambda k: pl.BlockSpec((cell_rows, 128), lambda i: (0, k))
    row_spec = lambda k: pl.BlockSpec((8, cell_cols), lambda i: (k, 0))
    tile_shape = jax.ShapeDtypeStruct((cell_rows // STRIP * cell_cols // 128, 128), f32)
    tiles, *edges = pl.pallas_call(
        edge_kernel,
        grid=(1,),
        out_shape=(tile_shape,) + edge_shapes(cell_rows, cell_cols),
        in_specs=[smem_spec] + vmem_specs(2)
        + [col_spec(0), col_spec(col_blocks - 1), row_spec(0), row_spec(row_blocks - 1),
           col_spec(col_blocks - 1), row_spec(row_blocks - 1),
           col_spec(col_blocks - 1), row_spec(row_blocks - 1)],
        out_specs=vmem_specs(5),
    )(flags, water_depth, land_mask, bed_level, bed_level, bed_level, bed_level,
      flux_east, flux_south, roughness, roughness)
    tile_parts = [tiles]

    def step_call(with_edges):
        outs = (grid_shape, grid_shape, grid_shape)
        if with_edges:
            outs = outs + (tile_shape,) + edge_shapes(cell_rows, cell_cols)
        return pl.pallas_call(
            functools.partial(step_kernel, with_edges),
            out_shape=outs,
            in_specs=[smem_spec] + vmem_specs(10),
            out_specs=vmem_specs(len(outs)),
        )

    tile_owner = tile_block // block_rows
    owner_hits = (tile_owner[:, None] == lax.iota(jnp.int32, device_count)[None, :]).astype(
        jnp.int32
    )
    earlier = jnp.sum((jnp.cumsum(owner_hits, axis=0) - owner_hits) * owner_hits, axis=1)
    send_pos = tile_owner * slot_cap + earlier
    local_ids = (tile_block % block_rows).astype(f32)
    gather_onehot = (
        lax.iota(jnp.int32, device_count * slot_cap)[:, None] == send_pos[None, :]
    ).astype(f32)
    send_ids = jnp.dot(gather_onehot, local_ids + 1.0, precision=lax.Precision.DEFAULT) - 1.0
    lane_blocks = cell_cols // 128
    row_pos = send_pos.reshape(cell_rows // STRIP, lane_blocks).T.reshape(-1)
    row_onehot = (
        lax.iota(jnp.int32, device_count * slot_cap)[:, None] == row_pos[None, :]
    ).astype(f32)
    id_rows = -(-slot_cap // reach_width)
    send_ids = jnp.pad(
        send_ids.reshape(device_count, slot_cap),
        ((0, 0), (0, id_rows * reach_width - slot_cap)),
        constant_values=-1.0,
    ).reshape(device_count, id_rows, reach_width)
    def start_lateral(parts, with_ids=True):
        packed = [
            jnp.dot(row_onehot, part, precision=lax.Precision.HIGH).reshape(
                device_count, slot_cap, reach_width
            )
            for part in parts
        ]
        return jnp.concatenate(packed + ([send_ids] if with_ids else []), axis=1)

    first_rows = slot_cap + id_rows
    got_first = lax.all_to_all(
        start_lateral(tile_parts).reshape(device_count, first_rows * reach_width),
        ("gy", "gx"), 0, 0, tiled=True,
    ).reshape(device_count, first_rows, reach_width)

    def reach_outflow(storage):
        ratio = reach_rate * jnp.power(storage, 2.0 / 3.0)
        outflow = storage * ratio / (1.0 + ratio)
        own_part = block_term(downstream, outflow, first_block, block_rows)
        ahead_part = block_term(downstream, outflow, first_block + block_rows, SPAN)
        return outflow, own_part, ahead_part

    first_outflow = reach_outflow(storage)
    ahead_rows = SPAN * reach_width // cell_cols
    depth = water_depth
    for step in range(STEPS):
        to_west, to_north, to_east, to_south = edges
        east_in = shifted(to_west, "gx", -1)
        south_in = shifted(to_north, "gy", -1)
        if step == 0:
            joined = shifted(
                jnp.concatenate(
                    [to_east, first_outflow[2].reshape(ahead_rows, cell_cols)], axis=0
                ),
                ("gy", "gx"),
                1,
            )
            west_in = joined[: to_east.shape[0]]
            first_ahead = joined[to_east.shape[0]:].reshape(SPAN, reach_width)
        else:
            west_in = shifted(to_east, "gx", 1)
        north_in = shifted(to_south, "gy", 1)
        last = step == STEPS - 1
        if last:
            lateral_started = start_lateral(tile_parts[1:], False)
            east_in, south_in, west_in, north_in, lateral_started, got_first = (
                lax.optimization_barrier(
                    (east_in, south_in, west_in, north_in, lateral_started, got_first)
                )
            )
        outs = step_call(not last)(
            flags, depth, flux_east, flux_south, bed_level, roughness, land_mask,
            east_in, south_in, west_in, north_in,
        )
        depth, flux_east, flux_south = outs[:3]
        if not last:
            tile_parts.append(outs[3])
            edges = outs[4:]

    got_second = lax.all_to_all(lateral_started, ("gy", "gx"), 0, 0, tiled=True)
    got_ids = got_first[:, slot_cap:].reshape(device_count, -1)[:, :slot_cap].reshape(-1)
    targets = lax.iota(f32, block_rows)
    scatter_onehot = (targets[:, None] == got_ids[None, :]).astype(f32)
    laterals = [
        jnp.dot(
            scatter_onehot,
            got[:, :slot_cap].reshape(-1, reach_width),
            precision=lax.Precision.HIGHEST,
        )
        for got in (got_first, got_second)
    ]

    for step in range(STEPS):
        if step == 0:
            outflow, own_part, _ = first_outflow
            upstream = own_part + jnp.pad(first_ahead, ((0, block_rows - SPAN), (0, 0)))
        else:
            outflow, own_part, ahead_part = reach_outflow(storage)
            upstream = own_part + jnp.pad(
                shifted(ahead_part, ("gy", "gx"), 1), ((0, block_rows - SPAN), (0, 0))
            )
        storage = storage - outflow + upstream + lateral_gain * laterals[step]
    return (depth, flux_east, flux_south, storage)


def solution(mesh):
    placed = (
        P("gy", "gx"),
        P("gy", "gx"),
        P("gy", "gx"),
        P("gy", "gx"),
        P("gy", "gx"),
        P("gy", "gx"),
        P(("gy", "gx")),
        P(("gy", "gx"), None),
        P(("gy", "gx"), None),
        P(("gy", "gx")),
    )
    return jax.shard_map(
        body,
        mesh=mesh,
        in_specs=placed,
        out_specs=(P("gy", "gx"), P("gy", "gx"), P("gy", "gx"), P(("gy", "gx"), None)),
        check_vma=False,
    )
```

```python
import functools

import jax
import jax.numpy as jnp
from jax import lax
from jax.experimental import pallas as pl
from jax.experimental.pallas import tpu as pltpu
from jax.sharding import PartitionSpec as P

STRIP = 8
STEPS = 2
SPAN = 8


rim_depth = 0.1
slope_gain = 0.1
friction_gain = 1.0
mass_gain = 0.05
drain_rate = 0.05
lateral_gain = 0.125


def shifted(value, axis, steps):
    count = lax.axis_size(axis)
    first, last = (max(0, -steps), min(count, count - steps))
    return lax.ppermute(value, axis, [(source, source + steps) for source in range(first, last)])


def face_update(flux, level, level_next, depth, depth_next, roughness, active):
    face_depth = rim_depth + 0.5 * (jnp.abs(depth) + jnp.abs(depth_next))
    drive = flux - slope_gain * face_depth * (level_next - level)
    inverse_power = jnp.exp((-7.0 / 3.0) * jnp.log(face_depth))
    damping = 1.0 + friction_gain * roughness * jnp.abs(flux) * inverse_power
    return active * drive / damping


def block_term(target_ids, values, start, count):
    targets = start + lax.iota(jnp.int32, count)
    onehot = (target_ids[:, None] == targets[None, :]).astype(jnp.float32)
    return jnp.einsum("tb,tc->bc", onehot, values, precision=lax.Precision.HIGHEST)


def first_col_row(x):
    return jnp.transpose(x[:, :128])[0:1, :]


def last_col_row(x):
    return jnp.transpose(x[:, -128:])[127:128, :]


def rows_as_cols(msg):
    count, length = msg.shape
    pad = jnp.zeros((128 - count, length), jnp.float32)
    return jnp.transpose(jnp.concatenate([msg, pad], axis=0))


def write_edges(level, depth, flux_e, flux_s, rough, eopen, sopen, to_west, to_north, to_east,
                to_south):
    to_west[0:1, :] = first_col_row(level)
    to_west[1:2, :] = first_col_row(depth)
    to_north[0:1, :] = level[0:1, :]
    to_north[1:2, :] = depth[0:1, :]
    to_east[0:1, :] = last_col_row(flux_e)
    to_east[1:2, :] = last_col_row(level)
    to_east[2:3, :] = last_col_row(depth)
    to_east[3:4, :] = last_col_row(rough)
    to_east[4:5, :] = last_col_row(eopen)
    to_south[0:1, :] = flux_s[-1:, :]
    to_south[1:2, :] = level[-1:, :]
    to_south[2:3, :] = depth[-1:, :]
    to_south[3:4, :] = rough[-1:, :]
    to_south[4:5, :] = sopen[-1:, :]


def tile_rows(drained):
    ny, nx = drained.shape
    strips = drained.reshape(ny // STRIP, STRIP, nx).sum(axis=1)
    return jnp.concatenate([strips[:, k * 128:(k + 1) * 128] for k in range(nx // 128)], axis=0)


def open_masks(flags_ref, land):
    ny, nx = land.shape
    col = lax.broadcasted_iota(jnp.int32, (ny, nx), 1)
    row = lax.broadcasted_iota(jnp.int32, (ny, nx), 0)
    eopen = jnp.where((col == nx - 1) & (flags_ref[0] == 1), 0.0, land)
    sopen = jnp.where((row == ny - 1) & (flags_ref[1] == 1), 0.0, land)
    return col, row, eopen, sopen


def edge_kernel(flags_ref, d_ref, land_ref, bed_first_col, bed_last_col, bed_first_row,
                bed_last_row, e_ref, s_ref, r_col, r_row, ahead_ref,
                tile_out, to_west, to_north, to_east, to_south):
    ny, nx = d_ref.shape
    depth = d_ref[...]
    land = land_ref[...].astype(jnp.float32)
    drained = drain_rate * land * jnp.abs(depth)
    tile_out[...] = tile_rows(drained)
    _, _, eopen, sopen = open_masks(flags_ref, land)
    to_west[0:1, :] = first_col_row(bed_first_col[...] + depth[:, :128])
    to_west[1:2, :] = first_col_row(depth)
    to_north[0:1, :] = bed_first_row[0:1, :] + depth[0:1, :]
    to_north[1:2, :] = depth[0:1, :]
    to_east[0:1, :] = last_col_row(e_ref[...])
    to_east[1:2, :] = last_col_row(bed_last_col[...] + depth[:, -128:])
    to_east[2:3, :] = last_col_row(depth)
    to_east[3:4, :] = last_col_row(r_col[...])
    to_east[4:5, :] = last_col_row(eopen)
    ahead = ahead_ref[...]
    per_row = ny // ahead.shape[1]
    for j in range(ahead.shape[0] // per_row):
        to_east[5 + j:6 + j, :] = jnp.concatenate(
            [ahead[j * per_row + m:j * per_row + m + 1, :] for m in range(per_row)], axis=1
        )
    to_south[0:1, :] = s_ref[-1:, :]
    to_south[1:2, :] = bed_last_row[-1:, :] + depth[-1:, :]
    to_south[2:3, :] = depth[-1:, :]
    to_south[3:4, :] = r_row[-1:, :]
    to_south[4:5, :] = sopen[-1:, :]


def step_kernel(with_edges, flags_ref, d_ref, e_ref, s_ref, bed_ref, r_ref, land_ref,
                east_ref, south_ref, west_ref, north_ref,
                d_out, e_out, s_out, *more):
    ny, nx = d_ref.shape
    depth = d_ref[...]
    bed = bed_ref[...]
    land = land_ref[...].astype(jnp.float32)
    rough = r_ref[...]
    level = bed + depth
    col, row, eopen, sopen = open_masks(flags_ref, land)
    east = rows_as_cols(east_ref[...])
    west = rows_as_cols(west_ref[...])
    level_e = jnp.where(col == nx - 1, east[:, 0:1], pltpu.roll(level, nx - 1, 1))
    depth_e = jnp.where(col == nx - 1, east[:, 1:2], pltpu.roll(depth, nx - 1, 1))
    level_s = jnp.where(row == ny - 1, south_ref[0:1, :], pltpu.roll(level, ny - 1, 0))
    depth_s = jnp.where(row == ny - 1, south_ref[1:2, :], pltpu.roll(depth, ny - 1, 0))
    flux_e = face_update(e_ref[...], level, level_e, depth, depth_e, rough, eopen)
    flux_s = face_update(s_ref[...], level, level_s, depth, depth_s, rough, sopen)
    west_edge = face_update(
        west[:, 0:1], west[:, 1:2], level[:, 0:1], west[:, 2:3], depth[:, 0:1],
        west[:, 3:4], west[:, 4:5],
    )
    north_edge = face_update(
        north_ref[0:1, :], north_ref[1:2, :], level[0:1, :], north_ref[2:3, :], depth[0:1, :],
        north_ref[3:4, :], north_ref[4:5, :],
    )
    west_edge = jnp.where(flags_ref[2] == 1, 0.0, west_edge)
    west_flux = jnp.where(col == 0, west_edge, pltpu.roll(flux_e, 1, 1))
    north_flux = jnp.where(row == 0, north_edge, pltpu.roll(flux_s, 1, 0))
    drained = drain_rate * land * jnp.abs(depth)
    new_depth = depth - mass_gain * (flux_e - west_flux + (flux_s - north_flux)) - drained
    d_out[...] = new_depth
    e_out[...] = flux_e
    s_out[...] = flux_s
    if with_edges:
        tile_out, to_west, to_north, to_east, to_south = more
        next_drained = drain_rate * land * jnp.abs(new_depth)
        tile_out[...] = tile_rows(next_drained)
        write_edges(bed + new_depth, new_depth, flux_e, flux_s, rough, eopen, sopen,
                    to_west, to_north, to_east, to_south)


def edge_shapes(ny, nx):
    f32 = jnp.float32
    return (
        jax.ShapeDtypeStruct((2, ny), f32),
        jax.ShapeDtypeStruct((2, nx), f32),
        jax.ShapeDtypeStruct((5, ny), f32),
        jax.ShapeDtypeStruct((5, nx), f32),
    )


def vmem_specs(count):
    return [pl.BlockSpec(memory_space=pltpu.VMEM) for _ in range(count)]


def body(
    water_depth,
    flux_east,
    flux_south,
    bed_level,
    roughness,
    land_mask,
    tile_block,
    storage,
    reach_rate,
    downstream,
):
    cell_rows, cell_cols = water_depth.shape
    block_rows, reach_width = storage.shape
    row_count = lax.axis_size("gy")
    col_count = lax.axis_size("gx")
    row_index = lax.axis_index("gy")
    col_index = lax.axis_index("gx")
    device_count = row_count * col_count
    tile_count = tile_block.shape[0]
    slot_cap = max(2, 2 * tile_count // device_count)
    flags = jnp.stack(
        [
            (col_index == col_count - 1).astype(jnp.int32),
            (row_index == row_count - 1).astype(jnp.int32),
            (col_index == 0).astype(jnp.int32),
        ]
    )
    device_index = row_index * col_count + col_index
    first_block = device_index * block_rows
    f32 = jnp.float32
    grid_shape = jax.ShapeDtypeStruct((cell_rows, cell_cols), f32)
    smem_spec = pl.BlockSpec(memory_space=pltpu.SMEM)

    def reach_outflow(storage):
        ratio = reach_rate * jnp.power(storage, 2.0 / 3.0)
        outflow = storage * ratio / (1.0 + ratio)
        own_part = block_term(downstream, outflow, first_block, block_rows)
        ahead_part = block_term(downstream, outflow, first_block + block_rows, SPAN)
        return outflow, own_part, ahead_part

    first_outflow = reach_outflow(storage)
    ahead_rows = SPAN * reach_width // cell_cols
    col_blocks = cell_cols // 128
    row_blocks = cell_rows // 8
    col_spec = lambda k: pl.BlockSpec((cell_rows, 128), lambda i: (0, k))
    row_spec = lambda k: pl.BlockSpec((8, cell_cols), lambda i: (k, 0))
    tile_shape = jax.ShapeDtypeStruct((cell_rows // STRIP * cell_cols // 128, 128), f32)
    first_shapes = list(edge_shapes(cell_rows, cell_cols))
    first_shapes[2] = jax.ShapeDtypeStruct((5 + ahead_rows, cell_rows), f32)
    tiles, *edges = pl.pallas_call(
        edge_kernel,
        grid=(1,),
        out_shape=(tile_shape,) + tuple(first_shapes),
        in_specs=[smem_spec] + vmem_specs(2)
        + [col_spec(0), col_spec(col_blocks - 1), row_spec(0), row_spec(row_blocks - 1),
           col_spec(col_blocks - 1), row_spec(row_blocks - 1),
           col_spec(col_blocks - 1), row_spec(row_blocks - 1)] + vmem_specs(1),
        out_specs=vmem_specs(5),
    )(flags, water_depth, land_mask, bed_level, bed_level, bed_level, bed_level,
      flux_east, flux_south, roughness, roughness, first_outflow[2])
    tile_parts = [tiles]

    def step_call(with_edges):
        outs = (grid_shape, grid_shape, grid_shape)
        if with_edges:
            outs = outs + (tile_shape,) + edge_shapes(cell_rows, cell_cols)
        return pl.pallas_call(
            functools.partial(step_kernel, with_edges),
            out_shape=outs,
            in_specs=[smem_spec] + vmem_specs(10),
            out_specs=vmem_specs(len(outs)),
        )

    tile_owner = tile_block // block_rows
    owner_hits = (tile_owner[:, None] == lax.iota(jnp.int32, device_count)[None, :]).astype(
        jnp.int32
    )
    earlier = jnp.sum((jnp.cumsum(owner_hits, axis=0) - owner_hits) * owner_hits, axis=1)
    send_pos = tile_owner * slot_cap + earlier
    local_ids = (tile_block % block_rows).astype(f32)
    gather_onehot = (
        lax.iota(jnp.int32, device_count * slot_cap)[:, None] == send_pos[None, :]
    ).astype(f32)
    send_ids = jnp.dot(gather_onehot, local_ids + 1.0, precision=lax.Precision.DEFAULT) - 1.0
    lane_blocks = cell_cols // 128
    row_pos = send_pos.reshape(cell_rows // STRIP, lane_blocks).T.reshape(-1)
    row_onehot = (
        lax.iota(jnp.int32, device_count * slot_cap)[:, None] == row_pos[None, :]
    ).astype(f32)
    id_rows = -(-slot_cap // reach_width)
    send_ids = jnp.pad(
        send_ids.reshape(device_count, slot_cap),
        ((0, 0), (0, id_rows * reach_width - slot_cap)),
        constant_values=-1.0,
    ).reshape(device_count, id_rows, reach_width)
    def start_lateral(parts, with_ids=True):
        packed = [
            jnp.dot(row_onehot, part, precision=lax.Precision.HIGH).reshape(
                device_count, slot_cap, reach_width
            )
            for part in parts
        ]
        return jnp.concatenate(packed + ([send_ids] if with_ids else []), axis=1)

    first_rows = slot_cap + id_rows
    got_first = lax.all_to_all(
        start_lateral(tile_parts).reshape(device_count, first_rows * reach_width),
        ("gy", "gx"), 0, 0, tiled=True,
    ).reshape(device_count, first_rows, reach_width)

    depth = water_depth
    for step in range(STEPS):
        to_west, to_north, to_east, to_south = edges
        east_in = shifted(to_west, "gx", -1)
        south_in = shifted(to_north, "gy", -1)
        if step == 0:
            west_in = shifted(to_east, ("gy", "gx"), 1)
            first_ahead = west_in[5:].reshape(SPAN, reach_width)
        else:
            west_in = shifted(to_east, "gx", 1)
        north_in = shifted(to_south, "gy", 1)
        last = step == STEPS - 1
        if last:
            lateral_started = start_lateral(tile_parts[1:], False)
            east_in, south_in, west_in, north_in, lateral_started, got_first = (
                lax.optimization_barrier(
                    (east_in, south_in, west_in, north_in, lateral_started, got_first)
                )
            )
        outs = step_call(not last)(
            flags, depth, flux_east, flux_south, bed_level, roughness, land_mask,
            east_in, south_in, west_in, north_in,
        )
        depth, flux_east, flux_south = outs[:3]
        if not last:
            tile_parts.append(outs[3])
            edges = outs[4:]

    got_second = lax.all_to_all(lateral_started, ("gy", "gx"), 0, 0, tiled=True)
    got_ids = got_first[:, slot_cap:].reshape(device_count, -1)[:, :slot_cap].reshape(-1)
    targets = lax.iota(f32, block_rows)
    scatter_onehot = (targets[:, None] == got_ids[None, :]).astype(f32)
    laterals = [
        jnp.dot(
            scatter_onehot,
            got[:, :slot_cap].reshape(-1, reach_width),
            precision=lax.Precision.HIGHEST,
        )
        for got in (got_first, got_second)
    ]

    for step in range(STEPS):
        if step == 0:
            outflow, own_part, _ = first_outflow
            upstream = own_part + jnp.pad(first_ahead, ((0, block_rows - SPAN), (0, 0)))
        else:
            outflow, own_part, ahead_part = reach_outflow(storage)
            upstream = own_part + jnp.pad(
                shifted(ahead_part, ("gy", "gx"), 1), ((0, block_rows - SPAN), (0, 0))
            )
        storage = storage - outflow + upstream + lateral_gain * laterals[step]
    return (depth, flux_east, flux_south, storage)


def solution(mesh):
    placed = (
        P("gy", "gx"),
        P("gy", "gx"),
        P("gy", "gx"),
        P("gy", "gx"),
        P("gy", "gx"),
        P("gy", "gx"),
        P(("gy", "gx")),
        P(("gy", "gx"), None),
        P(("gy", "gx"), None),
        P(("gy", "gx")),
    )
    return jax.shard_map(
        body,
        mesh=mesh,
        in_specs=placed,
        out_specs=(P("gy", "gx"), P("gy", "gx"), P("gy", "gx"), P(("gy", "gx"), None)),
        check_vma=False,
    )
```

```python
import functools

import jax
import jax.numpy as jnp
from jax import lax
from jax.experimental import pallas as pl
from jax.experimental.pallas import tpu as pltpu
from jax.sharding import PartitionSpec as P

STRIP = 8
STEPS = 2
SPAN = 8


rim_depth = 0.1
slope_gain = 0.1
friction_gain = 1.0
mass_gain = 0.05
drain_rate = 0.05
lateral_gain = 0.125


def shifted(value, axis, steps):
    count = lax.axis_size(axis)
    first, last = (max(0, -steps), min(count, count - steps))
    return lax.ppermute(value, axis, [(source, source + steps) for source in range(first, last)])


def face_update(flux, level, level_next, depth, depth_next, roughness, active):
    face_depth = rim_depth + 0.5 * (jnp.abs(depth) + jnp.abs(depth_next))
    drive = flux - slope_gain * face_depth * (level_next - level)
    inverse_power = jnp.exp((-7.0 / 3.0) * jnp.log(face_depth))
    damping = 1.0 + friction_gain * roughness * jnp.abs(flux) * inverse_power
    return active * drive / damping


def block_term(target_ids, values, start, count):
    targets = start + lax.iota(jnp.int32, count)
    onehot = (target_ids[:, None] == targets[None, :]).astype(jnp.float32)
    return jnp.einsum("tb,tc->bc", onehot, values, precision=lax.Precision.HIGHEST)


def first_col_row(x):
    return jnp.transpose(x[:, :128])[0:1, :]


def last_col_row(x):
    return jnp.transpose(x[:, -128:])[127:128, :]


def rows_as_cols(msg):
    count, length = msg.shape
    pad = jnp.zeros((128 - count, length), jnp.float32)
    return jnp.transpose(jnp.concatenate([msg, pad], axis=0))


def write_edges(level, depth, flux_e, flux_s, rough, eopen, sopen, to_west, to_north, to_east,
                to_south):
    to_west[0:1, :] = first_col_row(level)
    to_west[1:2, :] = first_col_row(depth)
    to_north[0:1, :] = level[0:1, :]
    to_north[1:2, :] = depth[0:1, :]
    to_east[0:1, :] = last_col_row(flux_e)
    to_east[1:2, :] = last_col_row(level)
    to_east[2:3, :] = last_col_row(depth)
    to_east[3:4, :] = last_col_row(rough)
    to_east[4:5, :] = last_col_row(eopen)
    to_south[0:1, :] = flux_s[-1:, :]
    to_south[1:2, :] = level[-1:, :]
    to_south[2:3, :] = depth[-1:, :]
    to_south[3:4, :] = rough[-1:, :]
    to_south[4:5, :] = sopen[-1:, :]


def tile_rows(drained):
    ny, nx = drained.shape
    strips = drained.reshape(ny // STRIP, STRIP, nx).sum(axis=1)
    return jnp.concatenate([strips[:, k * 128:(k + 1) * 128] for k in range(nx // 128)], axis=0)


def write_ahead(ahead_ref, to_east):
    ahead = ahead_ref[...]
    per_row = to_east.shape[1] // ahead.shape[1]
    for j in range(ahead.shape[0] // per_row):
        to_east[5 + j:6 + j, :] = jnp.concatenate(
            [ahead[j * per_row + m:j * per_row + m + 1, :] for m in range(per_row)], axis=1
        )


def open_masks(flags_ref, land):
    ny, nx = land.shape
    col = lax.broadcasted_iota(jnp.int32, (ny, nx), 1)
    row = lax.broadcasted_iota(jnp.int32, (ny, nx), 0)
    eopen = jnp.where((col == nx - 1) & (flags_ref[0] == 1), 0.0, land)
    sopen = jnp.where((row == ny - 1) & (flags_ref[1] == 1), 0.0, land)
    return col, row, eopen, sopen


def edge_kernel(flags_ref, d_ref, land_ref, bed_first_col, bed_last_col, bed_first_row,
                bed_last_row, e_ref, s_ref, r_col, r_row, ahead_ref,
                tile_out, to_west, to_north, to_east, to_south):
    ny, nx = d_ref.shape
    depth = d_ref[...]
    land = land_ref[...].astype(jnp.float32)
    drained = drain_rate * land * jnp.abs(depth)
    tile_out[...] = tile_rows(drained)
    _, _, eopen, sopen = open_masks(flags_ref, land)
    to_west[0:1, :] = first_col_row(bed_first_col[...] + depth[:, :128])
    to_west[1:2, :] = first_col_row(depth)
    to_north[0:1, :] = bed_first_row[0:1, :] + depth[0:1, :]
    to_north[1:2, :] = depth[0:1, :]
    to_east[0:1, :] = last_col_row(e_ref[...])
    to_east[1:2, :] = last_col_row(bed_last_col[...] + depth[:, -128:])
    to_east[2:3, :] = last_col_row(depth)
    to_east[3:4, :] = last_col_row(r_col[...])
    to_east[4:5, :] = last_col_row(eopen)
    write_ahead(ahead_ref, to_east)
    to_south[0:1, :] = s_ref[-1:, :]
    to_south[1:2, :] = bed_last_row[-1:, :] + depth[-1:, :]
    to_south[2:3, :] = depth[-1:, :]
    to_south[3:4, :] = r_row[-1:, :]
    to_south[4:5, :] = sopen[-1:, :]


def step_kernel(with_edges, flags_ref, d_ref, e_ref, s_ref, bed_ref, r_ref, land_ref,
                east_ref, south_ref, west_ref, north_ref, *rest):
    if with_edges:
        ahead_ref, d_out, e_out, s_out, tile_out, to_west, to_north, to_east, to_south = rest
    else:
        d_out, e_out, s_out = rest
    ny, nx = d_ref.shape
    depth = d_ref[...]
    bed = bed_ref[...]
    land = land_ref[...].astype(jnp.float32)
    rough = r_ref[...]
    level = bed + depth
    col, row, eopen, sopen = open_masks(flags_ref, land)
    east = rows_as_cols(east_ref[...])
    west = rows_as_cols(west_ref[...])
    level_e = jnp.where(col == nx - 1, east[:, 0:1], pltpu.roll(level, nx - 1, 1))
    depth_e = jnp.where(col == nx - 1, east[:, 1:2], pltpu.roll(depth, nx - 1, 1))
    level_s = jnp.where(row == ny - 1, south_ref[0:1, :], pltpu.roll(level, ny - 1, 0))
    depth_s = jnp.where(row == ny - 1, south_ref[1:2, :], pltpu.roll(depth, ny - 1, 0))
    flux_e = face_update(e_ref[...], level, level_e, depth, depth_e, rough, eopen)
    flux_s = face_update(s_ref[...], level, level_s, depth, depth_s, rough, sopen)
    west_edge = face_update(
        west[:, 0:1], west[:, 1:2], level[:, 0:1], west[:, 2:3], depth[:, 0:1],
        west[:, 3:4], west[:, 4:5],
    )
    north_edge = face_update(
        north_ref[0:1, :], north_ref[1:2, :], level[0:1, :], north_ref[2:3, :], depth[0:1, :],
        north_ref[3:4, :], north_ref[4:5, :],
    )
    west_edge = jnp.where(flags_ref[2] == 1, 0.0, west_edge)
    west_flux = jnp.where(col == 0, west_edge, pltpu.roll(flux_e, 1, 1))
    north_flux = jnp.where(row == 0, north_edge, pltpu.roll(flux_s, 1, 0))
    drained = drain_rate * land * jnp.abs(depth)
    new_depth = depth - mass_gain * (flux_e - west_flux + (flux_s - north_flux)) - drained
    d_out[...] = new_depth
    e_out[...] = flux_e
    s_out[...] = flux_s
    if with_edges:
        write_ahead(ahead_ref, to_east)
        next_drained = drain_rate * land * jnp.abs(new_depth)
        tile_out[...] = tile_rows(next_drained)
        write_edges(bed + new_depth, new_depth, flux_e, flux_s, rough, eopen, sopen,
                    to_west, to_north, to_east, to_south)


def edge_shapes(ny, nx):
    f32 = jnp.float32
    return (
        jax.ShapeDtypeStruct((2, ny), f32),
        jax.ShapeDtypeStruct((2, nx), f32),
        jax.ShapeDtypeStruct((5, ny), f32),
        jax.ShapeDtypeStruct((5, nx), f32),
    )


def vmem_specs(count):
    return [pl.BlockSpec(memory_space=pltpu.VMEM) for _ in range(count)]


def body(
    water_depth,
    flux_east,
    flux_south,
    bed_level,
    roughness,
    land_mask,
    tile_block,
    storage,
    reach_rate,
    downstream,
):
    cell_rows, cell_cols = water_depth.shape
    block_rows, reach_width = storage.shape
    row_count = lax.axis_size("gy")
    col_count = lax.axis_size("gx")
    row_index = lax.axis_index("gy")
    col_index = lax.axis_index("gx")
    device_count = row_count * col_count
    tile_count = tile_block.shape[0]
    slot_cap = max(2, 2 * tile_count // device_count)
    flags = jnp.stack(
        [
            (col_index == col_count - 1).astype(jnp.int32),
            (row_index == row_count - 1).astype(jnp.int32),
            (col_index == 0).astype(jnp.int32),
        ]
    )
    device_index = row_index * col_count + col_index
    first_block = device_index * block_rows
    f32 = jnp.float32
    grid_shape = jax.ShapeDtypeStruct((cell_rows, cell_cols), f32)
    smem_spec = pl.BlockSpec(memory_space=pltpu.SMEM)

    def reach_outflow(storage):
        ratio = reach_rate * jnp.power(storage, 2.0 / 3.0)
        outflow = storage * ratio / (1.0 + ratio)
        own_part = block_term(downstream, outflow, first_block, block_rows)
        ahead_part = block_term(downstream, outflow, first_block + block_rows, SPAN)
        return outflow, own_part, ahead_part

    first_outflow = reach_outflow(storage)
    ahead_rows = SPAN * reach_width // cell_cols
    col_blocks = cell_cols // 128
    row_blocks = cell_rows // 8
    col_spec = lambda k: pl.BlockSpec((cell_rows, 128), lambda i: (0, k))
    row_spec = lambda k: pl.BlockSpec((8, cell_cols), lambda i: (k, 0))
    tile_shape = jax.ShapeDtypeStruct((cell_rows // STRIP * cell_cols // 128, 128), f32)
    first_shapes = list(edge_shapes(cell_rows, cell_cols))
    first_shapes[2] = jax.ShapeDtypeStruct((5 + ahead_rows, cell_rows), f32)
    tiles, *edges = pl.pallas_call(
        edge_kernel,
        grid=(1,),
        out_shape=(tile_shape,) + tuple(first_shapes),
        in_specs=[smem_spec] + vmem_specs(2)
        + [col_spec(0), col_spec(col_blocks - 1), row_spec(0), row_spec(row_blocks - 1),
           col_spec(col_blocks - 1), row_spec(row_blocks - 1),
           col_spec(col_blocks - 1), row_spec(row_blocks - 1)] + vmem_specs(1),
        out_specs=vmem_specs(5),
    )(flags, water_depth, land_mask, bed_level, bed_level, bed_level, bed_level,
      flux_east, flux_south, roughness, roughness, first_outflow[2])
    tile_parts = [tiles]

    def step_call(with_edges):
        outs = (grid_shape, grid_shape, grid_shape)
        if with_edges:
            outs = outs + (tile_shape,) + tuple(first_shapes)
        return pl.pallas_call(
            functools.partial(step_kernel, with_edges),
            out_shape=outs,
            in_specs=[smem_spec] + vmem_specs(11 if with_edges else 10),
            out_specs=vmem_specs(len(outs)),
        )

    tile_owner = tile_block // block_rows
    owner_hits = (tile_owner[:, None] == lax.iota(jnp.int32, device_count)[None, :]).astype(
        jnp.int32
    )
    earlier = jnp.sum((jnp.cumsum(owner_hits, axis=0) - owner_hits) * owner_hits, axis=1)
    send_pos = tile_owner * slot_cap + earlier
    local_ids = (tile_block % block_rows).astype(f32)
    gather_onehot = (
        lax.iota(jnp.int32, device_count * slot_cap)[:, None] == send_pos[None, :]
    ).astype(f32)
    send_ids = jnp.dot(gather_onehot, local_ids + 1.0, precision=lax.Precision.DEFAULT) - 1.0
    lane_blocks = cell_cols // 128
    row_pos = send_pos.reshape(cell_rows // STRIP, lane_blocks).T.reshape(-1)
    row_onehot = (
        lax.iota(jnp.int32, device_count * slot_cap)[:, None] == row_pos[None, :]
    ).astype(f32)
    id_rows = -(-slot_cap // reach_width)
    send_ids = jnp.pad(
        send_ids.reshape(device_count, slot_cap),
        ((0, 0), (0, id_rows * reach_width - slot_cap)),
        constant_values=-1.0,
    ).reshape(device_count, id_rows, reach_width)
    def start_lateral(parts, with_ids=True):
        packed = [
            jnp.dot(row_onehot, part, precision=lax.Precision.HIGH).reshape(
                device_count, slot_cap, reach_width
            )
            for part in parts
        ]
        return jnp.concatenate(packed + ([send_ids] if with_ids else []), axis=1)

    first_rows = slot_cap + id_rows
    got_first = lax.all_to_all(
        start_lateral(tile_parts).reshape(device_count, first_rows * reach_width),
        ("gy", "gx"), 0, 0, tiled=True,
    ).reshape(device_count, first_rows, reach_width)

    got_ids = got_first[:, slot_cap:].reshape(device_count, -1)[:, :slot_cap].reshape(-1)
    targets = lax.iota(f32, block_rows)
    scatter_onehot = (targets[:, None] == got_ids[None, :]).astype(f32)

    def lateral_from(got):
        return jnp.dot(
            scatter_onehot,
            got[:, :slot_cap].reshape(-1, reach_width),
            precision=lax.Precision.HIGHEST,
        )

    def with_upstream(storage, outflow_parts, ahead, lateral):
        outflow, own_part, _ = outflow_parts
        upstream = own_part + jnp.pad(ahead, ((0, block_rows - SPAN), (0, 0)))
        return storage - outflow + upstream + lateral_gain * lateral

    depth = water_depth
    for step in range(STEPS):
        to_west, to_north, to_east, to_south = edges
        east_in = shifted(to_west, "gx", -1)
        south_in = shifted(to_north, "gy", -1)
        west_in = shifted(to_east, ("gy", "gx"), 1)
        ahead_in = west_in[5:].reshape(SPAN, reach_width)
        north_in = shifted(to_south, "gy", 1)
        last = step == STEPS - 1
        extra = ()
        if step == 0:
            storage = with_upstream(storage, first_outflow, ahead_in, lateral_from(got_first))
            second_outflow = reach_outflow(storage)
            extra = (second_outflow[2],)
        if last:
            second_ahead = ahead_in
            lateral_started = start_lateral(tile_parts[1:], False)
            east_in, south_in, west_in, north_in, lateral_started = lax.optimization_barrier(
                (east_in, south_in, west_in, north_in, lateral_started)
            )
        outs = step_call(not last)(
            flags, depth, flux_east, flux_south, bed_level, roughness, land_mask,
            east_in, south_in, west_in, north_in, *extra,
        )
        depth, flux_east, flux_south = outs[:3]
        if not last:
            tile_parts.append(outs[3])
            edges = outs[4:]

    got_second = lax.all_to_all(lateral_started, ("gy", "gx"), 0, 0, tiled=True)
    storage = with_upstream(storage, second_outflow, second_ahead, lateral_from(got_second))
    return (depth, flux_east, flux_south, storage)


def solution(mesh):
    placed = (
        P("gy", "gx"),
        P("gy", "gx"),
        P("gy", "gx"),
        P("gy", "gx"),
        P("gy", "gx"),
        P("gy", "gx"),
        P(("gy", "gx")),
        P(("gy", "gx"), None),
        P(("gy", "gx"), None),
        P(("gy", "gx")),
    )
    return jax.shard_map(
        body,
        mesh=mesh,
        in_specs=placed,
        out_specs=(P("gy", "gx"), P("gy", "gx"), P("gy", "gx"), P(("gy", "gx"), None)),
        check_vma=False,
    )
```

```python
import functools

import jax
import jax.numpy as jnp
from jax import lax
from jax.experimental import pallas as pl
from jax.experimental.pallas import tpu as pltpu
from jax.sharding import PartitionSpec as P

STRIP = 8
STEPS = 2
SPAN = 8


rim_depth = 0.1
slope_gain = 0.1
friction_gain = 1.0
mass_gain = 0.05
drain_rate = 0.05
lateral_gain = 0.125


def shifted(value, axis, steps):
    count = lax.axis_size(axis)
    first, last = (max(0, -steps), min(count, count - steps))
    return lax.ppermute(value, axis, [(source, source + steps) for source in range(first, last)])


def face_update(flux, level, level_next, depth, depth_next, roughness, active):
    face_depth = rim_depth + 0.5 * (jnp.abs(depth) + jnp.abs(depth_next))
    drive = flux - slope_gain * face_depth * (level_next - level)
    inverse_power = jnp.exp((-7.0 / 3.0) * jnp.log(face_depth))
    damping = 1.0 + friction_gain * roughness * jnp.abs(flux) * inverse_power
    return active * drive / damping


def block_term(target_ids, values, start, count):
    targets = start + lax.iota(jnp.int32, count)
    onehot = (target_ids[:, None] == targets[None, :]).astype(jnp.float32)
    return jnp.einsum("tb,tc->bc", onehot, values, precision=lax.Precision.HIGHEST)


def first_col_row(x):
    return jnp.transpose(x[:, :128])[0:1, :]


def last_col_row(x):
    return jnp.transpose(x[:, -128:])[127:128, :]


def rows_as_cols(msg):
    count, length = msg.shape
    pad = jnp.zeros((128 - count, length), jnp.float32)
    return jnp.transpose(jnp.concatenate([msg, pad], axis=0))


def write_edges(level, depth, flux_e, flux_s, rough, eopen, sopen, to_west, to_north, to_east,
                to_south):
    to_west[0:1, :] = first_col_row(level)
    to_west[1:2, :] = first_col_row(depth)
    to_north[0:1, :] = level[0:1, :]
    to_north[1:2, :] = depth[0:1, :]
    to_east[0:1, :] = last_col_row(flux_e)
    to_east[1:2, :] = last_col_row(level)
    to_east[2:3, :] = last_col_row(depth)
    to_east[3:4, :] = last_col_row(rough)
    to_east[4:5, :] = last_col_row(eopen)
    to_south[0:1, :] = flux_s[-1:, :]
    to_south[1:2, :] = level[-1:, :]
    to_south[2:3, :] = depth[-1:, :]
    to_south[3:4, :] = rough[-1:, :]
    to_south[4:5, :] = sopen[-1:, :]


def tile_rows(drained):
    ny, nx = drained.shape
    strips = drained.reshape(ny // STRIP, STRIP, nx).sum(axis=1)
    return jnp.concatenate([strips[:, k * 128:(k + 1) * 128] for k in range(nx // 128)], axis=0)


def write_ahead(ahead_ref, to_east):
    ahead = ahead_ref[...]
    per_row = to_east.shape[1] // ahead.shape[1]
    for j in range(ahead.shape[0] // per_row):
        to_east[5 + j:6 + j, :] = jnp.concatenate(
            [ahead[j * per_row + m:j * per_row + m + 1, :] for m in range(per_row)], axis=1
        )


def open_masks(flags_ref, land):
    ny, nx = land.shape
    col = lax.broadcasted_iota(jnp.int32, (ny, nx), 1)
    row = lax.broadcasted_iota(jnp.int32, (ny, nx), 0)
    eopen = jnp.where((col == nx - 1) & (flags_ref[0] == 1), 0.0, land)
    sopen = jnp.where((row == ny - 1) & (flags_ref[1] == 1), 0.0, land)
    return col, row, eopen, sopen


def edge_kernel(flags_ref, d_ref, land_ref, bed_first_col, bed_last_col, bed_first_row,
                bed_last_row, e_ref, s_ref, r_col, r_row, ahead_ref,
                tile_out, to_west, to_north, to_east, to_south):
    ny, nx = d_ref.shape
    depth = d_ref[...]
    land = land_ref[...].astype(jnp.float32)
    drained = drain_rate * land * jnp.abs(depth)
    tile_out[...] = tile_rows(drained)
    _, _, eopen, sopen = open_masks(flags_ref, land)
    to_west[0:1, :] = first_col_row(bed_first_col[...] + depth[:, :128])
    to_west[1:2, :] = first_col_row(depth)
    to_north[0:1, :] = bed_first_row[0:1, :] + depth[0:1, :]
    to_north[1:2, :] = depth[0:1, :]
    to_east[0:1, :] = last_col_row(e_ref[...])
    to_east[1:2, :] = last_col_row(bed_last_col[...] + depth[:, -128:])
    to_east[2:3, :] = last_col_row(depth)
    to_east[3:4, :] = last_col_row(r_col[...])
    to_east[4:5, :] = last_col_row(eopen)
    write_ahead(ahead_ref, to_east)
    to_south[0:1, :] = s_ref[-1:, :]
    to_south[1:2, :] = bed_last_row[-1:, :] + depth[-1:, :]
    to_south[2:3, :] = depth[-1:, :]
    to_south[3:4, :] = r_row[-1:, :]
    to_south[4:5, :] = sopen[-1:, :]


def step_kernel(with_edges, flags_ref, d_ref, e_ref, s_ref, bed_ref, r_ref, land_ref,
                east_ref, south_ref, west_ref, north_ref, *rest):
    if with_edges:
        ahead_ref, d_out, e_out, s_out, tile_out, to_west, to_north, to_east, to_south = rest
    else:
        d_out, e_out, s_out = rest
    ny, nx = d_ref.shape
    depth = d_ref[...]
    bed = bed_ref[...]
    land = land_ref[...].astype(jnp.float32)
    rough = r_ref[...]
    level = bed + depth
    col, row, eopen, sopen = open_masks(flags_ref, land)
    east = rows_as_cols(east_ref[...])
    west = rows_as_cols(west_ref[...])
    level_e = jnp.where(col == nx - 1, east[:, 0:1], pltpu.roll(level, nx - 1, 1))
    depth_e = jnp.where(col == nx - 1, east[:, 1:2], pltpu.roll(depth, nx - 1, 1))
    level_s = jnp.where(row == ny - 1, south_ref[0:1, :], pltpu.roll(level, ny - 1, 0))
    depth_s = jnp.where(row == ny - 1, south_ref[1:2, :], pltpu.roll(depth, ny - 1, 0))
    flux_e = face_update(e_ref[...], level, level_e, depth, depth_e, rough, eopen)
    flux_s = face_update(s_ref[...], level, level_s, depth, depth_s, rough, sopen)
    west_edge = face_update(
        west[:, 0:1], west[:, 1:2], level[:, 0:1], west[:, 2:3], depth[:, 0:1],
        west[:, 3:4], west[:, 4:5],
    )
    north_edge = face_update(
        north_ref[0:1, :], north_ref[1:2, :], level[0:1, :], north_ref[2:3, :], depth[0:1, :],
        north_ref[3:4, :], north_ref[4:5, :],
    )
    west_edge = jnp.where(flags_ref[2] == 1, 0.0, west_edge)
    west_flux = jnp.where(col == 0, west_edge, pltpu.roll(flux_e, 1, 1))
    north_flux = jnp.where(row == 0, north_edge, pltpu.roll(flux_s, 1, 0))
    drained = drain_rate * land * jnp.abs(depth)
    new_depth = depth - mass_gain * (flux_e - west_flux + (flux_s - north_flux)) - drained
    d_out[...] = new_depth
    e_out[...] = flux_e
    s_out[...] = flux_s
    if with_edges:
        write_ahead(ahead_ref, to_east)
        next_drained = drain_rate * land * jnp.abs(new_depth)
        tile_out[...] = tile_rows(next_drained)
        write_edges(bed + new_depth, new_depth, flux_e, flux_s, rough, eopen, sopen,
                    to_west, to_north, to_east, to_south)


def edge_shapes(ny, nx):
    f32 = jnp.float32
    return (
        jax.ShapeDtypeStruct((2, ny), f32),
        jax.ShapeDtypeStruct((2, nx), f32),
        jax.ShapeDtypeStruct((5, ny), f32),
        jax.ShapeDtypeStruct((5, nx), f32),
    )


def vmem_specs(count):
    return [pl.BlockSpec(memory_space=pltpu.VMEM) for _ in range(count)]


def body(
    water_depth,
    flux_east,
    flux_south,
    bed_level,
    roughness,
    land_mask,
    tile_block,
    storage,
    reach_rate,
    downstream,
):
    cell_rows, cell_cols = water_depth.shape
    block_rows, reach_width = storage.shape
    row_count = lax.axis_size("gy")
    col_count = lax.axis_size("gx")
    row_index = lax.axis_index("gy")
    col_index = lax.axis_index("gx")
    device_count = row_count * col_count
    tile_count = tile_block.shape[0]
    slot_cap = max(2, 2 * tile_count // device_count)
    flags = jnp.stack(
        [
            (col_index == col_count - 1).astype(jnp.int32),
            (row_index == row_count - 1).astype(jnp.int32),
            (col_index == 0).astype(jnp.int32),
        ]
    )
    device_index = row_index * col_count + col_index
    first_block = device_index * block_rows
    f32 = jnp.float32
    grid_shape = jax.ShapeDtypeStruct((cell_rows, cell_cols), f32)
    smem_spec = pl.BlockSpec(memory_space=pltpu.SMEM)

    def reach_outflow(storage):
        ratio = reach_rate * jnp.power(storage, 2.0 / 3.0)
        outflow = storage * ratio / (1.0 + ratio)
        own_part = block_term(downstream, outflow, first_block, block_rows)
        ahead_part = block_term(downstream, outflow, first_block + block_rows, SPAN)
        return outflow, own_part, ahead_part

    first_outflow = reach_outflow(storage)
    ahead_rows = SPAN * reach_width // cell_cols
    col_blocks = cell_cols // 128
    row_blocks = cell_rows // 8
    col_spec = lambda k: pl.BlockSpec((cell_rows, 128), lambda i: (0, k))
    row_spec = lambda k: pl.BlockSpec((8, cell_cols), lambda i: (k, 0))
    tile_shape = jax.ShapeDtypeStruct((cell_rows // STRIP * cell_cols // 128, 128), f32)
    first_shapes = list(edge_shapes(cell_rows, cell_cols))
    first_shapes[2] = jax.ShapeDtypeStruct((5 + ahead_rows, cell_rows), f32)
    tiles, *edges = pl.pallas_call(
        edge_kernel,
        grid=(1,),
        out_shape=(tile_shape,) + tuple(first_shapes),
        in_specs=[smem_spec] + vmem_specs(2)
        + [col_spec(0), col_spec(col_blocks - 1), row_spec(0), row_spec(row_blocks - 1),
           col_spec(col_blocks - 1), row_spec(row_blocks - 1),
           col_spec(col_blocks - 1), row_spec(row_blocks - 1)] + vmem_specs(1),
        out_specs=vmem_specs(5),
    )(flags, water_depth, land_mask, bed_level, bed_level, bed_level, bed_level,
      flux_east, flux_south, roughness, roughness, first_outflow[2])
    tile_parts = [tiles]

    def step_call(with_edges):
        outs = (grid_shape, grid_shape, grid_shape)
        if with_edges:
            outs = outs + (tile_shape,) + tuple(first_shapes)
        return pl.pallas_call(
            functools.partial(step_kernel, with_edges),
            out_shape=outs,
            in_specs=[smem_spec] + vmem_specs(11 if with_edges else 10),
            out_specs=vmem_specs(len(outs)),
        )

    tile_owner = tile_block // block_rows
    owner_hits = (tile_owner[:, None] == lax.iota(jnp.int32, device_count)[None, :]).astype(
        jnp.int32
    )
    earlier = jnp.sum((jnp.cumsum(owner_hits, axis=0) - owner_hits) * owner_hits, axis=1)
    send_pos = tile_owner * slot_cap + earlier
    local_ids = (tile_block % block_rows).astype(f32)
    gather_onehot = (
        lax.iota(jnp.int32, device_count * slot_cap)[:, None] == send_pos[None, :]
    ).astype(f32)
    send_ids = jnp.dot(gather_onehot, local_ids + 1.0, precision=lax.Precision.DEFAULT) - 1.0
    lane_blocks = cell_cols // 128
    row_pos = send_pos.reshape(cell_rows // STRIP, lane_blocks).T.reshape(-1)
    row_onehot = (
        lax.iota(jnp.int32, device_count * slot_cap)[:, None] == row_pos[None, :]
    ).astype(f32)
    id_rows = -(-slot_cap // reach_width)
    send_ids = jnp.pad(
        send_ids.reshape(device_count, slot_cap),
        ((0, 0), (0, id_rows * reach_width - slot_cap)),
        constant_values=-1.0,
    ).reshape(device_count, id_rows, reach_width)
    def start_lateral(parts, with_ids=True):
        packed = [
            jnp.dot(row_onehot, part, precision=lax.Precision.HIGH).reshape(
                device_count, slot_cap, reach_width
            )
            for part in parts
        ]
        return jnp.concatenate(packed + ([send_ids] if with_ids else []), axis=1)

    first_rows = slot_cap + id_rows
    first_message = start_lateral(tile_parts).reshape(device_count, first_rows * reach_width)


    def lateral_from(got):
        return jnp.dot(
            scatter_onehot,
            got[:, :slot_cap].reshape(-1, reach_width),
            precision=lax.Precision.HIGHEST,
        )

    def with_upstream(storage, outflow_parts, ahead, lateral):
        outflow, own_part, _ = outflow_parts
        upstream = own_part + jnp.pad(ahead, ((0, block_rows - SPAN), (0, 0)))
        return storage - outflow + upstream + lateral_gain * lateral

    depth = water_depth
    for step in range(STEPS):
        to_west, to_north, to_east, to_south = edges
        east_in = shifted(to_west, "gx", -1)
        south_in = shifted(to_north, "gy", -1)
        west_in = shifted(to_east, ("gy", "gx"), 1)
        ahead_in = west_in[5:].reshape(SPAN, reach_width)
        north_in = shifted(to_south, "gy", 1)
        last = step == STEPS - 1
        extra = ()
        if step == 0:
            east_in, south_in, west_in, north_in, first_message = lax.optimization_barrier(
                (east_in, south_in, west_in, north_in, first_message)
            )
            ahead_in = west_in[5:].reshape(SPAN, reach_width)
            got_first = lax.all_to_all(
                first_message, ("gy", "gx"), 0, 0, tiled=True
            ).reshape(device_count, first_rows, reach_width)
            got_ids = got_first[:, slot_cap:].reshape(device_count, -1)[:, :slot_cap].reshape(-1)
            targets = lax.iota(f32, block_rows)
            scatter_onehot = (targets[:, None] == got_ids[None, :]).astype(f32)
            storage = with_upstream(storage, first_outflow, ahead_in, lateral_from(got_first))
            second_outflow = reach_outflow(storage)
            extra = (second_outflow[2],)
        if last:
            second_ahead = ahead_in
            lateral_started = start_lateral(tile_parts[1:], False)
            east_in, south_in, west_in, north_in, lateral_started = lax.optimization_barrier(
                (east_in, south_in, west_in, north_in, lateral_started)
            )
        outs = step_call(not last)(
            flags, depth, flux_east, flux_south, bed_level, roughness, land_mask,
            east_in, south_in, west_in, north_in, *extra,
        )
        depth, flux_east, flux_south = outs[:3]
        if not last:
            tile_parts.append(outs[3])
            edges = outs[4:]

    got_second = lax.all_to_all(lateral_started, ("gy", "gx"), 0, 0, tiled=True)
    storage = with_upstream(storage, second_outflow, second_ahead, lateral_from(got_second))
    return (depth, flux_east, flux_south, storage)


def solution(mesh):
    placed = (
        P("gy", "gx"),
        P("gy", "gx"),
        P("gy", "gx"),
        P("gy", "gx"),
        P("gy", "gx"),
        P("gy", "gx"),
        P(("gy", "gx")),
        P(("gy", "gx"), None),
        P(("gy", "gx"), None),
        P(("gy", "gx")),
    )
    return jax.shard_map(
        body,
        mesh=mesh,
        in_specs=placed,
        out_specs=(P("gy", "gx"), P("gy", "gx"), P("gy", "gx"), P(("gy", "gx"), None)),
        check_vma=False,
    )
```

```python
import functools

import jax
import jax.numpy as jnp
from jax import lax
from jax.experimental import pallas as pl
from jax.experimental.pallas import tpu as pltpu
from jax.sharding import PartitionSpec as P

STRIP = 8
STEPS = 2
SPAN = 8


rim_depth = 0.1
slope_gain = 0.1
friction_gain = 1.0
mass_gain = 0.05
drain_rate = 0.05
lateral_gain = 0.125


def shifted(value, axis, steps):
    count = lax.axis_size(axis)
    first, last = (max(0, -steps), min(count, count - steps))
    return lax.ppermute(value, axis, [(source, source + steps) for source in range(first, last)])


def face_update(flux, level, level_next, depth, depth_next, roughness, active):
    face_depth = rim_depth + 0.5 * (jnp.abs(depth) + jnp.abs(depth_next))
    drive = flux - slope_gain * face_depth * (level_next - level)
    inverse_power = jnp.exp((-7.0 / 3.0) * jnp.log(face_depth))
    damping = 1.0 + friction_gain * roughness * jnp.abs(flux) * inverse_power
    return active * drive / damping


def block_term(target_ids, values, start, count):
    targets = start + lax.iota(jnp.int32, count)
    onehot = (target_ids[:, None] == targets[None, :]).astype(jnp.float32)
    return jnp.einsum("tb,tc->bc", onehot, values, precision=lax.Precision.HIGHEST)


def first_col_row(x):
    return jnp.transpose(x[:, :128])[0:1, :]


def last_col_row(x):
    return jnp.transpose(x[:, -128:])[127:128, :]


def rows_as_cols(msg):
    count, length = msg.shape
    pad = jnp.zeros((128 - count, length), jnp.float32)
    return jnp.transpose(jnp.concatenate([msg, pad], axis=0))


def write_edges(level, depth, flux_e, flux_s, rough, eopen, sopen, to_west, to_north, to_east,
                to_south):
    to_west[0:1, :] = first_col_row(level)
    to_west[1:2, :] = first_col_row(depth)
    to_north[0:1, :] = level[0:1, :]
    to_north[1:2, :] = depth[0:1, :]
    to_east[0:1, :] = last_col_row(flux_e)
    to_east[1:2, :] = last_col_row(level)
    to_east[2:3, :] = last_col_row(depth)
    to_east[3:4, :] = last_col_row(rough)
    to_east[4:5, :] = last_col_row(eopen)
    to_south[0:1, :] = flux_s[-1:, :]
    to_south[1:2, :] = level[-1:, :]
    to_south[2:3, :] = depth[-1:, :]
    to_south[3:4, :] = rough[-1:, :]
    to_south[4:5, :] = sopen[-1:, :]


def tile_rows(drained):
    ny, nx = drained.shape
    strips = drained.reshape(ny // STRIP, STRIP, nx).sum(axis=1)
    return jnp.concatenate([strips[:, k * 128:(k + 1) * 128] for k in range(nx // 128)], axis=0)


def open_masks(flags_ref, land):
    ny, nx = land.shape
    col = lax.broadcasted_iota(jnp.int32, (1, nx), 1)
    row = lax.broadcasted_iota(jnp.int32, (ny, 1), 0)
    east_keep = jnp.where((col == nx - 1) & (flags_ref[0] == 1), 0.0, 1.0)
    south_keep = jnp.where((row == ny - 1) & (flags_ref[1] == 1), 0.0, 1.0)
    return col, row, land * east_keep, land * south_keep


def edge_kernel(flags_ref, d_ref, land_ref, bed_first_col, bed_last_col, bed_first_row,
                bed_last_row, e_ref, s_ref, r_col, r_row,
                tile_out, to_west, to_north, to_east, to_south):
    ny, nx = d_ref.shape
    depth = d_ref[...]
    land = land_ref[...].astype(jnp.float32)
    drained = drain_rate * land * jnp.abs(depth)
    tile_out[...] = tile_rows(drained)
    _, _, eopen, sopen = open_masks(flags_ref, land)
    to_west[0:1, :] = first_col_row(bed_first_col[...] + depth[:, :128])
    to_west[1:2, :] = first_col_row(depth)
    to_north[0:1, :] = bed_first_row[0:1, :] + depth[0:1, :]
    to_north[1:2, :] = depth[0:1, :]
    to_east[0:1, :] = last_col_row(e_ref[...])
    to_east[1:2, :] = last_col_row(bed_last_col[...] + depth[:, -128:])
    to_east[2:3, :] = last_col_row(depth)
    to_east[3:4, :] = last_col_row(r_col[...])
    to_east[4:5, :] = last_col_row(eopen)
    to_south[0:1, :] = s_ref[-1:, :]
    to_south[1:2, :] = bed_last_row[-1:, :] + depth[-1:, :]
    to_south[2:3, :] = depth[-1:, :]
    to_south[3:4, :] = r_row[-1:, :]
    to_south[4:5, :] = sopen[-1:, :]


def step_kernel(with_edges, flags_ref, d_ref, e_ref, s_ref, bed_ref, r_ref, land_ref,
                east_ref, south_ref, west_ref, north_ref,
                d_out, e_out, s_out, *more):
    ny, nx = d_ref.shape
    depth = d_ref[...]
    bed = bed_ref[...]
    land = land_ref[...].astype(jnp.float32)
    rough = r_ref[...]
    level = bed + depth
    col, row, eopen, sopen = open_masks(flags_ref, land)
    east = rows_as_cols(east_ref[...])
    west = rows_as_cols(west_ref[...])
    level_e = jnp.where(col == nx - 1, east[:, 0:1], pltpu.roll(level, nx - 1, 1))
    depth_e = jnp.where(col == nx - 1, east[:, 1:2], pltpu.roll(depth, nx - 1, 1))
    level_s = jnp.where(row == ny - 1, south_ref[0:1, :], pltpu.roll(level, ny - 1, 0))
    depth_s = jnp.where(row == ny - 1, south_ref[1:2, :], pltpu.roll(depth, ny - 1, 0))
    flux_e = face_update(e_ref[...], level, level_e, depth, depth_e, rough, eopen)
    flux_s = face_update(s_ref[...], level, level_s, depth, depth_s, rough, sopen)
    west_edge = face_update(
        west[:, 0:1], west[:, 1:2], level[:, 0:1], west[:, 2:3], depth[:, 0:1],
        west[:, 3:4], west[:, 4:5],
    )
    north_edge = face_update(
        north_ref[0:1, :], north_ref[1:2, :], level[0:1, :], north_ref[2:3, :], depth[0:1, :],
        north_ref[3:4, :], north_ref[4:5, :],
    )
    west_edge = jnp.where(flags_ref[2] == 1, 0.0, west_edge)
    west_flux = jnp.where(col == 0, west_edge, pltpu.roll(flux_e, 1, 1))
    north_flux = jnp.where(row == 0, north_edge, pltpu.roll(flux_s, 1, 0))
    drained = drain_rate * land * jnp.abs(depth)
    new_depth = depth - mass_gain * (flux_e - west_flux + (flux_s - north_flux)) - drained
    d_out[...] = new_depth
    e_out[...] = flux_e
    s_out[...] = flux_s
    if with_edges:
        tile_out, to_west, to_north, to_east, to_south = more
        next_drained = drain_rate * land * jnp.abs(new_depth)
        tile_out[...] = tile_rows(next_drained)
        write_edges(bed + new_depth, new_depth, flux_e, flux_s, rough, eopen, sopen,
                    to_west, to_north, to_east, to_south)


def edge_shapes(ny, nx):
    f32 = jnp.float32
    return (
        jax.ShapeDtypeStruct((2, ny), f32),
        jax.ShapeDtypeStruct((2, nx), f32),
        jax.ShapeDtypeStruct((5, ny), f32),
        jax.ShapeDtypeStruct((5, nx), f32),
    )


def vmem_specs(count):
    return [pl.BlockSpec(memory_space=pltpu.VMEM) for _ in range(count)]


def body(
    water_depth,
    flux_east,
    flux_south,
    bed_level,
    roughness,
    land_mask,
    tile_block,
    storage,
    reach_rate,
    downstream,
):
    cell_rows, cell_cols = water_depth.shape
    block_rows, reach_width = storage.shape
    row_count = lax.axis_size("gy")
    col_count = lax.axis_size("gx")
    row_index = lax.axis_index("gy")
    col_index = lax.axis_index("gx")
    device_count = row_count * col_count
    tile_count = tile_block.shape[0]
    slot_cap = max(2, 2 * tile_count // device_count)
    flags = jnp.stack(
        [
            (col_index == col_count - 1).astype(jnp.int32),
            (row_index == row_count - 1).astype(jnp.int32),
            (col_index == 0).astype(jnp.int32),
        ]
    )
    device_index = row_index * col_count + col_index
    first_block = device_index * block_rows
    f32 = jnp.float32
    grid_shape = jax.ShapeDtypeStruct((cell_rows, cell_cols), f32)
    smem_spec = pl.BlockSpec(memory_space=pltpu.SMEM)

    col_blocks = cell_cols // 128
    row_blocks = cell_rows // 8
    col_spec = lambda k: pl.BlockSpec((cell_rows, 128), lambda i: (0, k))
    row_spec = lambda k: pl.BlockSpec((8, cell_cols), lambda i: (k, 0))
    tile_shape = jax.ShapeDtypeStruct((cell_rows // STRIP * cell_cols // 128, 128), f32)
    tiles, *edges = pl.pallas_call(
        edge_kernel,
        grid=(1,),
        out_shape=(tile_shape,) + edge_shapes(cell_rows, cell_cols),
        in_specs=[smem_spec] + vmem_specs(2)
        + [col_spec(0), col_spec(col_blocks - 1), row_spec(0), row_spec(row_blocks - 1),
           col_spec(col_blocks - 1), row_spec(row_blocks - 1),
           col_spec(col_blocks - 1), row_spec(row_blocks - 1)],
        out_specs=vmem_specs(5),
    )(flags, water_depth, land_mask, bed_level, bed_level, bed_level, bed_level,
      flux_east, flux_south, roughness, roughness)
    tile_parts = [tiles]

    def step_call(with_edges):
        outs = (grid_shape, grid_shape, grid_shape)
        if with_edges:
            outs = outs + (tile_shape,) + edge_shapes(cell_rows, cell_cols)
        return pl.pallas_call(
            functools.partial(step_kernel, with_edges),
            out_shape=outs,
            in_specs=[smem_spec] + vmem_specs(10),
            out_specs=vmem_specs(len(outs)),
        )

    tile_owner = tile_block // block_rows
    owner_hits = (tile_owner[:, None] == lax.iota(jnp.int32, device_count)[None, :]).astype(
        jnp.int32
    )
    earlier = jnp.sum((jnp.cumsum(owner_hits, axis=0) - owner_hits) * owner_hits, axis=1)
    send_pos = tile_owner * slot_cap + earlier
    local_ids = (tile_block % block_rows).astype(f32)
    gather_onehot = (
        lax.iota(jnp.int32, device_count * slot_cap)[:, None] == send_pos[None, :]
    ).astype(f32)
    send_ids = jnp.dot(gather_onehot, local_ids + 1.0, precision=lax.Precision.DEFAULT) - 1.0
    lane_blocks = cell_cols // 128
    row_pos = send_pos.reshape(cell_rows // STRIP, lane_blocks).T.reshape(-1)
    row_onehot = (
        lax.iota(jnp.int32, device_count * slot_cap)[:, None] == row_pos[None, :]
    ).astype(f32)
    id_rows = -(-slot_cap // reach_width)
    send_ids = jnp.pad(
        send_ids.reshape(device_count, slot_cap),
        ((0, 0), (0, id_rows * reach_width - slot_cap)),
        constant_values=-1.0,
    ).reshape(device_count, id_rows, reach_width)
    def start_lateral(parts, with_ids=True):
        packed = [
            jnp.dot(row_onehot, part, precision=lax.Precision.HIGH).reshape(
                device_count, slot_cap, reach_width
            )
            for part in parts
        ]
        return jnp.concatenate(packed + ([send_ids] if with_ids else []), axis=1)

    first_rows = slot_cap + id_rows
    got_first = lax.all_to_all(
        start_lateral(tile_parts).reshape(device_count, first_rows * reach_width),
        ("gy", "gx"), 0, 0, tiled=True,
    ).reshape(device_count, first_rows, reach_width)

    def reach_outflow(storage):
        ratio = reach_rate * jnp.power(storage, 2.0 / 3.0)
        outflow = storage * ratio / (1.0 + ratio)
        own_part = block_term(downstream, outflow, first_block, block_rows)
        ahead_part = block_term(downstream, outflow, first_block + block_rows, SPAN)
        return outflow, own_part, ahead_part

    first_outflow = reach_outflow(storage)
    ahead_rows = SPAN * reach_width // cell_cols
    depth = water_depth
    for step in range(STEPS):
        to_west, to_north, to_east, to_south = edges
        east_in = shifted(to_west, "gx", -1)
        south_in = shifted(to_north, "gy", -1)
        if step == 0:
            joined = shifted(
                jnp.concatenate(
                    [to_east, first_outflow[2].reshape(ahead_rows, cell_cols)], axis=0
                ),
                ("gy", "gx"),
                1,
            )
            west_in = joined[: to_east.shape[0]]
            first_ahead = joined[to_east.shape[0]:].reshape(SPAN, reach_width)
        else:
            west_in = shifted(to_east, "gx", 1)
        north_in = shifted(to_south, "gy", 1)
        last = step == STEPS - 1
        if last:
            lateral_started = start_lateral(tile_parts[1:], False)
            east_in, south_in, west_in, north_in, lateral_started, got_first = (
                lax.optimization_barrier(
                    (east_in, south_in, west_in, north_in, lateral_started, got_first)
                )
            )
        outs = step_call(not last)(
            flags, depth, flux_east, flux_south, bed_level, roughness, land_mask,
            east_in, south_in, west_in, north_in,
        )
        depth, flux_east, flux_south = outs[:3]
        if not last:
            tile_parts.append(outs[3])
            edges = outs[4:]

    got_second = lax.all_to_all(lateral_started, ("gy", "gx"), 0, 0, tiled=True)
    got_ids = got_first[:, slot_cap:].reshape(device_count, -1)[:, :slot_cap].reshape(-1)
    targets = lax.iota(f32, block_rows)
    scatter_onehot = (targets[:, None] == got_ids[None, :]).astype(f32)
    laterals = [
        jnp.dot(
            scatter_onehot,
            got[:, :slot_cap].reshape(-1, reach_width),
            precision=lax.Precision.HIGHEST,
        )
        for got in (got_first, got_second)
    ]

    for step in range(STEPS):
        if step == 0:
            outflow, own_part, _ = first_outflow
            upstream = own_part + jnp.pad(first_ahead, ((0, block_rows - SPAN), (0, 0)))
        else:
            outflow, own_part, ahead_part = reach_outflow(storage)
            upstream = own_part + jnp.pad(
                shifted(ahead_part, ("gy", "gx"), 1), ((0, block_rows - SPAN), (0, 0))
            )
        storage = storage - outflow + upstream + lateral_gain * laterals[step]
    return (depth, flux_east, flux_south, storage)


def solution(mesh):
    placed = (
        P("gy", "gx"),
        P("gy", "gx"),
        P("gy", "gx"),
        P("gy", "gx"),
        P("gy", "gx"),
        P("gy", "gx"),
        P(("gy", "gx")),
        P(("gy", "gx"), None),
        P(("gy", "gx"), None),
        P(("gy", "gx")),
    )
    return jax.shard_map(
        body,
        mesh=mesh,
        in_specs=placed,
        out_specs=(P("gy", "gx"), P("gy", "gx"), P("gy", "gx"), P(("gy", "gx"), None)),
        check_vma=False,
    )
```

```python
import functools

import jax
import jax.numpy as jnp
from jax import lax
from jax.experimental import pallas as pl
from jax.experimental.pallas import tpu as pltpu
from jax.sharding import PartitionSpec as P

STRIP = 8
STEPS = 2
SPAN = 8


rim_depth = 0.1
slope_gain = 0.1
friction_gain = 1.0
mass_gain = 0.05
drain_rate = 0.05
lateral_gain = 0.125


def shifted(value, axis, steps):
    count = lax.axis_size(axis)
    first, last = (max(0, -steps), min(count, count - steps))
    return lax.ppermute(value, axis, [(source, source + steps) for source in range(first, last)])


def face_update(flux, level, level_next, depth, depth_next, roughness, active):
    face_depth = rim_depth + 0.5 * (jnp.abs(depth) + jnp.abs(depth_next))
    drive = flux - slope_gain * face_depth * (level_next - level)
    inverse_power = jnp.exp((-7.0 / 3.0) * jnp.log(face_depth))
    damping = 1.0 + friction_gain * roughness * jnp.abs(flux) * inverse_power
    return active * drive / damping


def block_term(target_ids, values, start, count):
    targets = start + lax.iota(jnp.int32, count)
    onehot = (target_ids[:, None] == targets[None, :]).astype(jnp.float32)
    return jnp.einsum("tb,tc->bc", onehot, values, precision=lax.Precision.HIGHEST)


def first_col_row(x):
    return jnp.transpose(x[:, :128])[0:1, :]


def last_col_row(x):
    return jnp.transpose(x[:, -128:])[127:128, :]


def rows_as_cols(msg):
    count, length = msg.shape
    pad = jnp.zeros((128 - count, length), jnp.float32)
    return jnp.transpose(jnp.concatenate([msg, pad], axis=0))


def write_edges(level, depth, flux_e, flux_s, rough, eopen, sopen, to_west, to_north, to_east,
                to_south):
    to_west[0:1, :] = first_col_row(level)
    to_west[1:2, :] = first_col_row(depth)
    to_north[0:1, :] = level[0:1, :]
    to_north[1:2, :] = depth[0:1, :]
    to_east[0:1, :] = last_col_row(flux_e)
    to_east[1:2, :] = last_col_row(level)
    to_east[2:3, :] = last_col_row(depth)
    to_east[3:4, :] = last_col_row(rough)
    to_east[4:5, :] = last_col_row(eopen)
    to_south[0:1, :] = flux_s[-1:, :]
    to_south[1:2, :] = level[-1:, :]
    to_south[2:3, :] = depth[-1:, :]
    to_south[3:4, :] = rough[-1:, :]
    to_south[4:5, :] = sopen[-1:, :]


def tile_rows(drained):
    ny, nx = drained.shape
    strips = drained.reshape(ny // STRIP, STRIP, nx).sum(axis=1)
    return jnp.concatenate([strips[:, k * 128:(k + 1) * 128] for k in range(nx // 128)], axis=0)


def open_masks(flags_ref, land):
    ny, nx = land.shape
    col = lax.broadcasted_iota(jnp.int32, (ny, nx), 1)
    row = lax.broadcasted_iota(jnp.int32, (ny, nx), 0)
    eopen = jnp.where((col == nx - 1) & (flags_ref[0] == 1), 0.0, land)
    sopen = jnp.where((row == ny - 1) & (flags_ref[1] == 1), 0.0, land)
    return col, row, eopen, sopen


def edge_kernel(flags_ref, d_ref, land_ref, bed_first_col, bed_last_col, bed_first_row,
                bed_last_row, e_ref, s_ref, r_col, r_row,
                tile_out, to_west, to_north, to_east, to_south):
    ny, nx = d_ref.shape
    depth = d_ref[...]
    land = land_ref[...].astype(jnp.float32)
    drained = drain_rate * land * jnp.abs(depth)
    tile_out[...] = tile_rows(drained)
    _, _, eopen, sopen = open_masks(flags_ref, land)
    to_west[0:1, :] = first_col_row(bed_first_col[...] + depth[:, :128])
    to_west[1:2, :] = first_col_row(depth)
    to_north[0:1, :] = bed_first_row[0:1, :] + depth[0:1, :]
    to_north[1:2, :] = depth[0:1, :]
    to_east[0:1, :] = last_col_row(e_ref[...])
    to_east[1:2, :] = last_col_row(bed_last_col[...] + depth[:, -128:])
    to_east[2:3, :] = last_col_row(depth)
    to_east[3:4, :] = last_col_row(r_col[...])
    to_east[4:5, :] = last_col_row(eopen)
    to_south[0:1, :] = s_ref[-1:, :]
    to_south[1:2, :] = bed_last_row[-1:, :] + depth[-1:, :]
    to_south[2:3, :] = depth[-1:, :]
    to_south[3:4, :] = r_row[-1:, :]
    to_south[4:5, :] = sopen[-1:, :]


def step_kernel(with_edges, flags_ref, d_ref, e_ref, s_ref, bed_ref, r_ref, land_ref,
                east_ref, south_ref, west_ref, north_ref,
                d_out, e_out, s_out, *more):
    ny, nx = d_ref.shape
    depth = d_ref[...]
    bed = bed_ref[...]
    land = land_ref[...].astype(jnp.float32)
    rough = r_ref[...]
    level = bed + depth
    col, row, eopen, sopen = open_masks(flags_ref, land)
    east = rows_as_cols(east_ref[...])
    west = rows_as_cols(west_ref[...])
    level_e = jnp.where(col == nx - 1, east[:, 0:1], pltpu.roll(level, nx - 1, 1))
    depth_e = jnp.where(col == nx - 1, east[:, 1:2], pltpu.roll(depth, nx - 1, 1))
    level_s = jnp.where(row == ny - 1, south_ref[0:1, :], pltpu.roll(level, ny - 1, 0))
    depth_s = jnp.where(row == ny - 1, south_ref[1:2, :], pltpu.roll(depth, ny - 1, 0))
    flux_e = face_update(e_ref[...], level, level_e, depth, depth_e, rough, eopen)
    flux_s = face_update(s_ref[...], level, level_s, depth, depth_s, rough, sopen)
    west_edge = face_update(
        west[:, 0:1], west[:, 1:2], level[:, 0:1], west[:, 2:3], depth[:, 0:1],
        west[:, 3:4], west[:, 4:5],
    )
    north_edge = face_update(
        north_ref[0:1, :], north_ref[1:2, :], level[0:1, :], north_ref[2:3, :], depth[0:1, :],
        north_ref[3:4, :], north_ref[4:5, :],
    )
    west_edge = jnp.where(flags_ref[2] == 1, 0.0, west_edge)
    west_flux = jnp.where(col == 0, west_edge, pltpu.roll(flux_e, 1, 1))
    north_flux = jnp.where(row == 0, north_edge, pltpu.roll(flux_s, 1, 0))
    drained = drain_rate * land * jnp.abs(depth)
    new_depth = depth - mass_gain * (flux_e - west_flux + (flux_s - north_flux)) - drained
    d_out[...] = new_depth
    e_out[...] = flux_e
    s_out[...] = flux_s
    if with_edges:
        tile_out, to_west, to_north, to_east, to_south = more
        next_drained = drain_rate * land * jnp.abs(new_depth)
        tile_out[...] = tile_rows(next_drained)
        write_edges(bed + new_depth, new_depth, flux_e, flux_s, rough, eopen, sopen,
                    to_west, to_north, to_east, to_south)


def last_step_kernel(total_rows, flags_ref, d_ref, e_ref, s_ref, bed_ref, r_ref, land_ref,
                     d_up, s_up, bed_up, r_up, land_up, d_dn, bed_dn,
                     east_ref, south_ref, west_ref, north_ref, d_out, e_out, s_out):
    block = pl.program_id(0)
    blocks = pl.num_programs(0)
    tr, nx = d_ref.shape
    depth = d_ref[...]
    bed = bed_ref[...]
    land = land_ref[...].astype(jnp.float32)
    rough = r_ref[...]
    level = bed + depth
    col = lax.broadcasted_iota(jnp.int32, (1, nx), 1)
    row = lax.broadcasted_iota(jnp.int32, (tr, 1), 0)
    eopen = land * jnp.where((col == nx - 1) & (flags_ref[0] == 1), 0.0, 1.0)
    sopen = land * jnp.where(
        (block * tr + row == total_rows - 1) & (flags_ref[1] == 1), 0.0, 1.0
    )
    east = rows_as_cols(east_ref[...])
    west = rows_as_cols(west_ref[...])
    level_e = jnp.where(col == nx - 1, east[:, 0:1], pltpu.roll(level, nx - 1, 1))
    depth_e = jnp.where(col == nx - 1, east[:, 1:2], pltpu.roll(depth, nx - 1, 1))
    at_bottom = block == blocks - 1
    below_depth = jnp.where(at_bottom, south_ref[1:2, :], d_dn[0:1, :])
    below_level = jnp.where(at_bottom, south_ref[0:1, :], bed_dn[0:1, :] + d_dn[0:1, :])
    level_s = jnp.where(row == tr - 1, below_level, pltpu.roll(level, tr - 1, 0))
    depth_s = jnp.where(row == tr - 1, below_depth, pltpu.roll(depth, tr - 1, 0))
    flux_e = face_update(e_ref[...], level, level_e, depth, depth_e, rough, eopen)
    flux_s = face_update(s_ref[...], level, level_s, depth, depth_s, rough, sopen)
    west_edge = face_update(
        west[:, 0:1], west[:, 1:2], level[:, 0:1], west[:, 2:3], depth[:, 0:1],
        west[:, 3:4], west[:, 4:5],
    )
    west_edge = jnp.where(flags_ref[2] == 1, 0.0, west_edge)
    outer_north = face_update(
        north_ref[0:1, :], north_ref[1:2, :], level[0:1, :], north_ref[2:3, :], depth[0:1, :],
        north_ref[3:4, :], north_ref[4:5, :],
    )
    up_depth = d_up[7:8, :]
    inner_north = face_update(
        s_up[7:8, :], bed_up[7:8, :] + up_depth, level[0:1, :], up_depth, depth[0:1, :],
        r_up[7:8, :], land_up[7:8, :].astype(jnp.float32),
    )
    north_edge = jnp.where(block == 0, outer_north, inner_north)
    west_flux = jnp.where(col == 0, west_edge, pltpu.roll(flux_e, 1, 1))
    north_flux = jnp.where(row == 0, north_edge, pltpu.roll(flux_s, 1, 0))
    drained = drain_rate * land * jnp.abs(depth)
    d_out[...] = depth - mass_gain * (flux_e - west_flux + (flux_s - north_flux)) - drained
    e_out[...] = flux_e
    s_out[...] = flux_s


def edge_shapes(ny, nx):
    f32 = jnp.float32
    return (
        jax.ShapeDtypeStruct((2, ny), f32),
        jax.ShapeDtypeStruct((2, nx), f32),
        jax.ShapeDtypeStruct((5, ny), f32),
        jax.ShapeDtypeStruct((5, nx), f32),
    )


def vmem_specs(count):
    return [pl.BlockSpec(memory_space=pltpu.VMEM) for _ in range(count)]


def body(
    water_depth,
    flux_east,
    flux_south,
    bed_level,
    roughness,
    land_mask,
    tile_block,
    storage,
    reach_rate,
    downstream,
):
    cell_rows, cell_cols = water_depth.shape
    block_rows, reach_width = storage.shape
    row_count = lax.axis_size("gy")
    col_count = lax.axis_size("gx")
    row_index = lax.axis_index("gy")
    col_index = lax.axis_index("gx")
    device_count = row_count * col_count
    tile_count = tile_block.shape[0]
    slot_cap = max(2, 2 * tile_count // device_count)
    flags = jnp.stack(
        [
            (col_index == col_count - 1).astype(jnp.int32),
            (row_index == row_count - 1).astype(jnp.int32),
            (col_index == 0).astype(jnp.int32),
        ]
    )
    device_index = row_index * col_count + col_index
    first_block = device_index * block_rows
    f32 = jnp.float32
    grid_shape = jax.ShapeDtypeStruct((cell_rows, cell_cols), f32)
    smem_spec = pl.BlockSpec(memory_space=pltpu.SMEM)

    col_blocks = cell_cols // 128
    row_blocks = cell_rows // 8
    col_spec = lambda k: pl.BlockSpec((cell_rows, 128), lambda i: (0, k))
    row_spec = lambda k: pl.BlockSpec((8, cell_cols), lambda i: (k, 0))
    tile_shape = jax.ShapeDtypeStruct((cell_rows // STRIP * cell_cols // 128, 128), f32)
    tiles, *edges = pl.pallas_call(
        edge_kernel,
        grid=(1,),
        out_shape=(tile_shape,) + edge_shapes(cell_rows, cell_cols),
        in_specs=[smem_spec] + vmem_specs(2)
        + [col_spec(0), col_spec(col_blocks - 1), row_spec(0), row_spec(row_blocks - 1),
           col_spec(col_blocks - 1), row_spec(row_blocks - 1),
           col_spec(col_blocks - 1), row_spec(row_blocks - 1)],
        out_specs=vmem_specs(5),
    )(flags, water_depth, land_mask, bed_level, bed_level, bed_level, bed_level,
      flux_east, flux_south, roughness, roughness)
    tile_parts = [tiles]

    def step_call(with_edges):
        outs = (grid_shape, grid_shape, grid_shape)
        if with_edges:
            outs = outs + (tile_shape,) + edge_shapes(cell_rows, cell_cols)
        return pl.pallas_call(
            functools.partial(step_kernel, with_edges),
            out_shape=outs,
            in_specs=[smem_spec] + vmem_specs(10),
            out_specs=vmem_specs(len(outs)),
        )

    tile_owner = tile_block // block_rows
    owner_hits = (tile_owner[:, None] == lax.iota(jnp.int32, device_count)[None, :]).astype(
        jnp.int32
    )
    earlier = jnp.sum((jnp.cumsum(owner_hits, axis=0) - owner_hits) * owner_hits, axis=1)
    send_pos = tile_owner * slot_cap + earlier
    local_ids = (tile_block % block_rows).astype(f32)
    gather_onehot = (
        lax.iota(jnp.int32, device_count * slot_cap)[:, None] == send_pos[None, :]
    ).astype(f32)
    send_ids = jnp.dot(gather_onehot, local_ids + 1.0, precision=lax.Precision.DEFAULT) - 1.0
    lane_blocks = cell_cols // 128
    row_pos = send_pos.reshape(cell_rows // STRIP, lane_blocks).T.reshape(-1)
    row_onehot = (
        lax.iota(jnp.int32, device_count * slot_cap)[:, None] == row_pos[None, :]
    ).astype(f32)
    id_rows = -(-slot_cap // reach_width)
    send_ids = jnp.pad(
        send_ids.reshape(device_count, slot_cap),
        ((0, 0), (0, id_rows * reach_width - slot_cap)),
        constant_values=-1.0,
    ).reshape(device_count, id_rows, reach_width)
    def start_lateral(parts, with_ids=True):
        packed = [
            jnp.dot(row_onehot, part, precision=lax.Precision.HIGH).reshape(
                device_count, slot_cap, reach_width
            )
            for part in parts
        ]
        return jnp.concatenate(packed + ([send_ids] if with_ids else []), axis=1)

    first_rows = slot_cap + id_rows
    got_first = lax.all_to_all(
        start_lateral(tile_parts).reshape(device_count, first_rows * reach_width),
        ("gy", "gx"), 0, 0, tiled=True,
    ).reshape(device_count, first_rows, reach_width)

    def reach_outflow(storage):
        ratio = reach_rate * jnp.power(storage, 2.0 / 3.0)
        outflow = storage * ratio / (1.0 + ratio)
        own_part = block_term(downstream, outflow, first_block, block_rows)
        ahead_part = block_term(downstream, outflow, first_block + block_rows, SPAN)
        return outflow, own_part, ahead_part

    first_outflow = reach_outflow(storage)
    ahead_rows = SPAN * reach_width // cell_cols
    tr = 128
    nblk = cell_rows // tr
    main_spec = pl.BlockSpec((tr, cell_cols), lambda i: (i, 0))
    up_spec = pl.BlockSpec((8, cell_cols), lambda i: (jnp.maximum(i * (tr // 8) - 1, 0), 0))
    dn_spec = pl.BlockSpec(
        (8, cell_cols), lambda i: (jnp.minimum((i + 1) * (tr // 8), cell_rows // 8 - 1), 0)
    )
    last_call = pl.pallas_call(
        functools.partial(last_step_kernel, cell_rows),
        grid=(nblk,),
        out_shape=(grid_shape, grid_shape, grid_shape),
        in_specs=[smem_spec] + [main_spec] * 6 + [up_spec] * 5 + [dn_spec] * 2
        + [
            pl.BlockSpec((2, tr), lambda i: (0, i)),
            pl.BlockSpec((2, cell_cols), lambda i: (0, 0)),
            pl.BlockSpec((5, tr), lambda i: (0, i)),
            pl.BlockSpec((5, cell_cols), lambda i: (0, 0)),
        ],
        out_specs=[main_spec] * 3,
    )

    depth = water_depth
    for step in range(STEPS):
        to_west, to_north, to_east, to_south = edges
        east_in = shifted(to_west, "gx", -1)
        south_in = shifted(to_north, "gy", -1)
        if step == 0:
            joined = shifted(
                jnp.concatenate(
                    [to_east, first_outflow[2].reshape(ahead_rows, cell_cols)], axis=0
                ),
                ("gy", "gx"),
                1,
            )
            west_in = joined[: to_east.shape[0]]
            first_ahead = joined[to_east.shape[0]:].reshape(SPAN, reach_width)
        else:
            west_in = shifted(to_east, "gx", 1)
        north_in = shifted(to_south, "gy", 1)
        last = step == STEPS - 1
        if last:
            lateral_started = start_lateral(tile_parts[1:], False)
            east_in, south_in, west_in, north_in, lateral_started, got_first = (
                lax.optimization_barrier(
                    (east_in, south_in, west_in, north_in, lateral_started, got_first)
                )
            )
        if last:
            outs = last_call(
                flags, depth, flux_east, flux_south, bed_level, roughness, land_mask,
                depth, flux_south, bed_level, roughness, land_mask, depth, bed_level,
                east_in, south_in, west_in, north_in,
            )
        else:
            outs = step_call(True)(
                flags, depth, flux_east, flux_south, bed_level, roughness, land_mask,
                east_in, south_in, west_in, north_in,
            )
        depth, flux_east, flux_south = outs[:3]
        if not last:
            tile_parts.append(outs[3])
            edges = outs[4:]

    got_second = lax.all_to_all(lateral_started, ("gy", "gx"), 0, 0, tiled=True)
    got_ids = got_first[:, slot_cap:].reshape(device_count, -1)[:, :slot_cap].reshape(-1)
    targets = lax.iota(f32, block_rows)
    scatter_onehot = (targets[:, None] == got_ids[None, :]).astype(f32)
    laterals = [
        jnp.dot(
            scatter_onehot,
            got[:, :slot_cap].reshape(-1, reach_width),
            precision=lax.Precision.HIGHEST,
        )
        for got in (got_first, got_second)
    ]

    for step in range(STEPS):
        if step == 0:
            outflow, own_part, _ = first_outflow
            upstream = own_part + jnp.pad(first_ahead, ((0, block_rows - SPAN), (0, 0)))
        else:
            outflow, own_part, ahead_part = reach_outflow(storage)
            upstream = own_part + jnp.pad(
                shifted(ahead_part, ("gy", "gx"), 1), ((0, block_rows - SPAN), (0, 0))
            )
        storage = storage - outflow + upstream + lateral_gain * laterals[step]
    return (depth, flux_east, flux_south, storage)


def solution(mesh):
    placed = (
        P("gy", "gx"),
        P("gy", "gx"),
        P("gy", "gx"),
        P("gy", "gx"),
        P("gy", "gx"),
        P("gy", "gx"),
        P(("gy", "gx")),
        P(("gy", "gx"), None),
        P(("gy", "gx"), None),
        P(("gy", "gx")),
    )
    return jax.shard_map(
        body,
        mesh=mesh,
        in_specs=placed,
        out_specs=(P("gy", "gx"), P("gy", "gx"), P("gy", "gx"), P(("gy", "gx"), None)),
        check_vma=False,
    )
```

```python
import functools

import jax
import jax.numpy as jnp
from jax import lax
from jax.experimental import pallas as pl
from jax.experimental.pallas import tpu as pltpu
from jax.sharding import PartitionSpec as P

STRIP = 8
STEPS = 2
SPAN = 8


rim_depth = 0.1
slope_gain = 0.1
friction_gain = 1.0
mass_gain = 0.05
drain_rate = 0.05
lateral_gain = 0.125


def shifted(value, axis, steps):
    count = lax.axis_size(axis)
    first, last = (max(0, -steps), min(count, count - steps))
    return lax.ppermute(value, axis, [(source, source + steps) for source in range(first, last)])


def face_update(flux, level, level_next, depth, depth_next, roughness, active):
    face_depth = rim_depth + 0.5 * (jnp.abs(depth) + jnp.abs(depth_next))
    drive = flux - slope_gain * face_depth * (level_next - level)
    inverse_power = jnp.exp((-7.0 / 3.0) * jnp.log(face_depth))
    damping = 1.0 + friction_gain * roughness * jnp.abs(flux) * inverse_power
    return active * drive / damping


def block_term(target_ids, values, start, count):
    targets = start + lax.iota(jnp.int32, count)
    onehot = (target_ids[:, None] == targets[None, :]).astype(jnp.float32)
    return jnp.einsum("tb,tc->bc", onehot, values, precision=lax.Precision.HIGHEST)


def first_col_row(x):
    return jnp.transpose(x[:, :128])[0:1, :]


def last_col_row(x):
    return jnp.transpose(x[:, -128:])[127:128, :]


def rows_as_cols(msg):
    count, length = msg.shape
    pad = jnp.zeros((128 - count, length), jnp.float32)
    return jnp.transpose(jnp.concatenate([msg, pad], axis=0))


def write_edges(level, depth, flux_e, flux_s, rough, eopen, sopen, to_west, to_north, to_east,
                to_south):
    to_west[0:1, :] = first_col_row(level)
    to_west[1:2, :] = first_col_row(depth)
    to_north[0:1, :] = level[0:1, :]
    to_north[1:2, :] = depth[0:1, :]
    to_east[0:1, :] = last_col_row(flux_e)
    to_east[1:2, :] = last_col_row(level)
    to_east[2:3, :] = last_col_row(depth)
    to_east[3:4, :] = last_col_row(rough)
    to_east[4:5, :] = last_col_row(eopen)
    to_south[0:1, :] = flux_s[-1:, :]
    to_south[1:2, :] = level[-1:, :]
    to_south[2:3, :] = depth[-1:, :]
    to_south[3:4, :] = rough[-1:, :]
    to_south[4:5, :] = sopen[-1:, :]


def tile_rows(drained):
    ny, nx = drained.shape
    strips = drained.reshape(ny // STRIP, STRIP, nx).sum(axis=1)
    return jnp.concatenate([strips[:, k * 128:(k + 1) * 128] for k in range(nx // 128)], axis=0)


def open_masks(flags_ref, land):
    ny, nx = land.shape
    col = lax.broadcasted_iota(jnp.int32, (ny, nx), 1)
    row = lax.broadcasted_iota(jnp.int32, (ny, nx), 0)
    eopen = jnp.where((col == nx - 1) & (flags_ref[0] == 1), 0.0, land)
    sopen = jnp.where((row == ny - 1) & (flags_ref[1] == 1), 0.0, land)
    return col, row, eopen, sopen


def edge_kernel(flags_ref, d_ref, land_ref, bed_first_col, bed_last_col, bed_first_row,
                bed_last_row, e_ref, s_ref, r_col, r_row,
                tile_out, to_west, to_north, to_east, to_south):
    ny, nx = d_ref.shape
    depth = d_ref[...]
    land = land_ref[...].astype(jnp.float32)
    drained = drain_rate * land * jnp.abs(depth)
    tile_out[...] = tile_rows(drained)
    _, _, eopen, sopen = open_masks(flags_ref, land)
    to_west[0:1, :] = first_col_row(bed_first_col[...] + depth[:, :128])
    to_west[1:2, :] = first_col_row(depth)
    to_north[0:1, :] = bed_first_row[0:1, :] + depth[0:1, :]
    to_north[1:2, :] = depth[0:1, :]
    to_east[0:1, :] = last_col_row(e_ref[...])
    to_east[1:2, :] = last_col_row(bed_last_col[...] + depth[:, -128:])
    to_east[2:3, :] = last_col_row(depth)
    to_east[3:4, :] = last_col_row(r_col[...])
    to_east[4:5, :] = last_col_row(eopen)
    to_south[0:1, :] = s_ref[-1:, :]
    to_south[1:2, :] = bed_last_row[-1:, :] + depth[-1:, :]
    to_south[2:3, :] = depth[-1:, :]
    to_south[3:4, :] = r_row[-1:, :]
    to_south[4:5, :] = sopen[-1:, :]


def step_kernel(with_edges, flags_ref, d_ref, e_ref, s_ref, bed_ref, r_ref, land_ref,
                east_ref, south_ref, west_ref, north_ref,
                d_out, e_out, s_out, *more):
    ny, nx = d_ref.shape
    depth = d_ref[...]
    bed = bed_ref[...]
    land = land_ref[...].astype(jnp.float32)
    rough = r_ref[...]
    level = bed + depth
    col, row, eopen, sopen = open_masks(flags_ref, land)
    east = rows_as_cols(east_ref[...])
    west = rows_as_cols(west_ref[...])
    level_e = jnp.where(col == nx - 1, east[:, 0:1], pltpu.roll(level, nx - 1, 1))
    depth_e = jnp.where(col == nx - 1, east[:, 1:2], pltpu.roll(depth, nx - 1, 1))
    level_s = jnp.where(row == ny - 1, south_ref[0:1, :], pltpu.roll(level, ny - 1, 0))
    depth_s = jnp.where(row == ny - 1, south_ref[1:2, :], pltpu.roll(depth, ny - 1, 0))
    flux_e = face_update(e_ref[...], level, level_e, depth, depth_e, rough, eopen)
    flux_s = face_update(s_ref[...], level, level_s, depth, depth_s, rough, sopen)
    west_edge = face_update(
        west[:, 0:1], west[:, 1:2], level[:, 0:1], west[:, 2:3], depth[:, 0:1],
        west[:, 3:4], west[:, 4:5],
    )
    north_edge = face_update(
        north_ref[0:1, :], north_ref[1:2, :], level[0:1, :], north_ref[2:3, :], depth[0:1, :],
        north_ref[3:4, :], north_ref[4:5, :],
    )
    west_edge = jnp.where(flags_ref[2] == 1, 0.0, west_edge)
    west_flux = jnp.where(col == 0, west_edge, pltpu.roll(flux_e, 1, 1))
    north_flux = jnp.where(row == 0, north_edge, pltpu.roll(flux_s, 1, 0))
    drained = drain_rate * land * jnp.abs(depth)
    new_depth = depth - mass_gain * (flux_e - west_flux + (flux_s - north_flux)) - drained
    d_out[...] = new_depth
    e_out[...] = flux_e
    s_out[...] = flux_s
    if with_edges:
        tile_out, to_west, to_north, to_east, to_south = more
        next_drained = drain_rate * land * jnp.abs(new_depth)
        tile_out[...] = tile_rows(next_drained)
        write_edges(bed + new_depth, new_depth, flux_e, flux_s, rough, eopen, sopen,
                    to_west, to_north, to_east, to_south)


def last_step_kernel(total_rows, flags_ref, d_ref, e_ref, s_ref, bed_ref, r_ref, land_ref,
                     d_up, s_up, bed_up, r_up, land_up, d_dn, bed_dn,
                     east_ref, south_ref, west_ref, north_ref, d_out, e_out, s_out,
                     east_cols, west_cols):
    block = pl.program_id(0)
    blocks = pl.num_programs(0)
    tr, nx = d_ref.shape
    depth = d_ref[...]
    bed = bed_ref[...]
    land = land_ref[...].astype(jnp.float32)
    rough = r_ref[...]
    level = bed + depth
    col = lax.broadcasted_iota(jnp.int32, (1, nx), 1)
    row = lax.broadcasted_iota(jnp.int32, (tr, 1), 0)
    eopen = land * jnp.where((col == nx - 1) & (flags_ref[0] == 1), 0.0, 1.0)
    sopen = land * jnp.where(
        (block * tr + row == total_rows - 1) & (flags_ref[1] == 1), 0.0, 1.0
    )
    east_cols[...] = rows_as_cols(east_ref[...])
    west_cols[...] = rows_as_cols(west_ref[...])
    start = pl.multiple_of(block * tr, 8)
    east = east_cols[pl.ds(start, tr), :]
    west = west_cols[pl.ds(start, tr), :]
    level_e = jnp.where(col == nx - 1, east[:, 0:1], pltpu.roll(level, nx - 1, 1))
    depth_e = jnp.where(col == nx - 1, east[:, 1:2], pltpu.roll(depth, nx - 1, 1))
    at_bottom = block == blocks - 1
    below_depth = jnp.where(at_bottom, south_ref[1:2, :], d_dn[0:1, :])
    below_level = jnp.where(at_bottom, south_ref[0:1, :], bed_dn[0:1, :] + d_dn[0:1, :])
    level_s = jnp.where(row == tr - 1, below_level, pltpu.roll(level, tr - 1, 0))
    depth_s = jnp.where(row == tr - 1, below_depth, pltpu.roll(depth, tr - 1, 0))
    flux_e = face_update(e_ref[...], level, level_e, depth, depth_e, rough, eopen)
    flux_s = face_update(s_ref[...], level, level_s, depth, depth_s, rough, sopen)
    west_edge = face_update(
        west[:, 0:1], west[:, 1:2], level[:, 0:1], west[:, 2:3], depth[:, 0:1],
        west[:, 3:4], west[:, 4:5],
    )
    west_edge = jnp.where(flags_ref[2] == 1, 0.0, west_edge)
    outer_north = face_update(
        north_ref[0:1, :], north_ref[1:2, :], level[0:1, :], north_ref[2:3, :], depth[0:1, :],
        north_ref[3:4, :], north_ref[4:5, :],
    )
    up_depth = d_up[7:8, :]
    inner_north = face_update(
        s_up[7:8, :], bed_up[7:8, :] + up_depth, level[0:1, :], up_depth, depth[0:1, :],
        r_up[7:8, :], land_up[7:8, :].astype(jnp.float32),
    )
    north_edge = jnp.where(block == 0, outer_north, inner_north)
    west_flux = jnp.where(col == 0, west_edge, pltpu.roll(flux_e, 1, 1))
    north_flux = jnp.where(row == 0, north_edge, pltpu.roll(flux_s, 1, 0))
    drained = drain_rate * land * jnp.abs(depth)
    d_out[...] = depth - mass_gain * (flux_e - west_flux + (flux_s - north_flux)) - drained
    e_out[...] = flux_e
    s_out[...] = flux_s


def edge_shapes(ny, nx):
    f32 = jnp.float32
    return (
        jax.ShapeDtypeStruct((2, ny), f32),
        jax.ShapeDtypeStruct((2, nx), f32),
        jax.ShapeDtypeStruct((5, ny), f32),
        jax.ShapeDtypeStruct((5, nx), f32),
    )


def vmem_specs(count):
    return [pl.BlockSpec(memory_space=pltpu.VMEM) for _ in range(count)]


def body(
    water_depth,
    flux_east,
    flux_south,
    bed_level,
    roughness,
    land_mask,
    tile_block,
    storage,
    reach_rate,
    downstream,
):
    cell_rows, cell_cols = water_depth.shape
    block_rows, reach_width = storage.shape
    row_count = lax.axis_size("gy")
    col_count = lax.axis_size("gx")
    row_index = lax.axis_index("gy")
    col_index = lax.axis_index("gx")
    device_count = row_count * col_count
    tile_count = tile_block.shape[0]
    slot_cap = max(2, 2 * tile_count // device_count)
    flags = jnp.stack(
        [
            (col_index == col_count - 1).astype(jnp.int32),
            (row_index == row_count - 1).astype(jnp.int32),
            (col_index == 0).astype(jnp.int32),
        ]
    )
    device_index = row_index * col_count + col_index
    first_block = device_index * block_rows
    f32 = jnp.float32
    grid_shape = jax.ShapeDtypeStruct((cell_rows, cell_cols), f32)
    smem_spec = pl.BlockSpec(memory_space=pltpu.SMEM)

    col_blocks = cell_cols // 128
    row_blocks = cell_rows // 8
    col_spec = lambda k: pl.BlockSpec((cell_rows, 128), lambda i: (0, k))
    row_spec = lambda k: pl.BlockSpec((8, cell_cols), lambda i: (k, 0))
    tile_shape = jax.ShapeDtypeStruct((cell_rows // STRIP * cell_cols // 128, 128), f32)
    tiles, *edges = pl.pallas_call(
        edge_kernel,
        grid=(1,),
        out_shape=(tile_shape,) + edge_shapes(cell_rows, cell_cols),
        in_specs=[smem_spec] + vmem_specs(2)
        + [col_spec(0), col_spec(col_blocks - 1), row_spec(0), row_spec(row_blocks - 1),
           col_spec(col_blocks - 1), row_spec(row_blocks - 1),
           col_spec(col_blocks - 1), row_spec(row_blocks - 1)],
        out_specs=vmem_specs(5),
    )(flags, water_depth, land_mask, bed_level, bed_level, bed_level, bed_level,
      flux_east, flux_south, roughness, roughness)
    tile_parts = [tiles]

    def step_call(with_edges):
        outs = (grid_shape, grid_shape, grid_shape)
        if with_edges:
            outs = outs + (tile_shape,) + edge_shapes(cell_rows, cell_cols)
        return pl.pallas_call(
            functools.partial(step_kernel, with_edges),
            out_shape=outs,
            in_specs=[smem_spec] + vmem_specs(10),
            out_specs=vmem_specs(len(outs)),
        )

    tile_owner = tile_block // block_rows
    owner_hits = (tile_owner[:, None] == lax.iota(jnp.int32, device_count)[None, :]).astype(
        jnp.int32
    )
    earlier = jnp.sum((jnp.cumsum(owner_hits, axis=0) - owner_hits) * owner_hits, axis=1)
    send_pos = tile_owner * slot_cap + earlier
    local_ids = (tile_block % block_rows).astype(f32)
    gather_onehot = (
        lax.iota(jnp.int32, device_count * slot_cap)[:, None] == send_pos[None, :]
    ).astype(f32)
    send_ids = jnp.dot(gather_onehot, local_ids + 1.0, precision=lax.Precision.DEFAULT) - 1.0
    lane_blocks = cell_cols // 128
    row_pos = send_pos.reshape(cell_rows // STRIP, lane_blocks).T.reshape(-1)
    row_onehot = (
        lax.iota(jnp.int32, device_count * slot_cap)[:, None] == row_pos[None, :]
    ).astype(f32)
    id_rows = -(-slot_cap // reach_width)
    send_ids = jnp.pad(
        send_ids.reshape(device_count, slot_cap),
        ((0, 0), (0, id_rows * reach_width - slot_cap)),
        constant_values=-1.0,
    ).reshape(device_count, id_rows, reach_width)
    def start_lateral(parts, with_ids=True):
        packed = [
            jnp.dot(row_onehot, part, precision=lax.Precision.HIGH).reshape(
                device_count, slot_cap, reach_width
            )
            for part in parts
        ]
        return jnp.concatenate(packed + ([send_ids] if with_ids else []), axis=1)

    first_rows = slot_cap + id_rows
    got_first = lax.all_to_all(
        start_lateral(tile_parts).reshape(device_count, first_rows * reach_width),
        ("gy", "gx"), 0, 0, tiled=True,
    ).reshape(device_count, first_rows, reach_width)

    def reach_outflow(storage):
        ratio = reach_rate * jnp.power(storage, 2.0 / 3.0)
        outflow = storage * ratio / (1.0 + ratio)
        own_part = block_term(downstream, outflow, first_block, block_rows)
        ahead_part = block_term(downstream, outflow, first_block + block_rows, SPAN)
        return outflow, own_part, ahead_part

    first_outflow = reach_outflow(storage)
    ahead_rows = SPAN * reach_width // cell_cols
    tr = 64
    nblk = cell_rows // tr
    main_spec = pl.BlockSpec((tr, cell_cols), lambda i: (i, 0))
    up_spec = pl.BlockSpec((8, cell_cols), lambda i: (jnp.maximum(i * (tr // 8) - 1, 0), 0))
    dn_spec = pl.BlockSpec(
        (8, cell_cols), lambda i: (jnp.minimum((i + 1) * (tr // 8), cell_rows // 8 - 1), 0)
    )
    last_call = pl.pallas_call(
        functools.partial(last_step_kernel, cell_rows),
        grid=(nblk,),
        out_shape=(grid_shape, grid_shape, grid_shape),
        in_specs=[smem_spec] + [main_spec] * 6 + [up_spec] * 5 + [dn_spec] * 2
        + [
            pl.BlockSpec((2, cell_rows), lambda i: (0, 0)),
            pl.BlockSpec((2, cell_cols), lambda i: (0, 0)),
            pl.BlockSpec((5, cell_rows), lambda i: (0, 0)),
            pl.BlockSpec((5, cell_cols), lambda i: (0, 0)),
        ],
        out_specs=[main_spec] * 3,
        scratch_shapes=[pltpu.VMEM((cell_rows, 128), f32), pltpu.VMEM((cell_rows, 128), f32)],
    )

    depth = water_depth
    for step in range(STEPS):
        to_west, to_north, to_east, to_south = edges
        east_in = shifted(to_west, "gx", -1)
        south_in = shifted(to_north, "gy", -1)
        if step == 0:
            joined = shifted(
                jnp.concatenate(
                    [to_east, first_outflow[2].reshape(ahead_rows, cell_cols)], axis=0
                ),
                ("gy", "gx"),
                1,
            )
            west_in = joined[: to_east.shape[0]]
            first_ahead = joined[to_east.shape[0]:].reshape(SPAN, reach_width)
        else:
            west_in = shifted(to_east, "gx", 1)
        north_in = shifted(to_south, "gy", 1)
        last = step == STEPS - 1
        if last:
            lateral_started = start_lateral(tile_parts[1:], False)
            east_in, south_in, west_in, north_in, lateral_started, got_first = (
                lax.optimization_barrier(
                    (east_in, south_in, west_in, north_in, lateral_started, got_first)
                )
            )
        if last:
            outs = last_call(
                flags, depth, flux_east, flux_south, bed_level, roughness, land_mask,
                depth, flux_south, bed_level, roughness, land_mask, depth, bed_level,
                east_in, south_in, west_in, north_in,
            )
        else:
            outs = step_call(True)(
                flags, depth, flux_east, flux_south, bed_level, roughness, land_mask,
                east_in, south_in, west_in, north_in,
            )
        depth, flux_east, flux_south = outs[:3]
        if not last:
            tile_parts.append(outs[3])
            edges = outs[4:]

    got_second = lax.all_to_all(lateral_started, ("gy", "gx"), 0, 0, tiled=True)
    got_ids = got_first[:, slot_cap:].reshape(device_count, -1)[:, :slot_cap].reshape(-1)
    targets = lax.iota(f32, block_rows)
    scatter_onehot = (targets[:, None] == got_ids[None, :]).astype(f32)
    laterals = [
        jnp.dot(
            scatter_onehot,
            got[:, :slot_cap].reshape(-1, reach_width),
            precision=lax.Precision.HIGHEST,
        )
        for got in (got_first, got_second)
    ]

    for step in range(STEPS):
        if step == 0:
            outflow, own_part, _ = first_outflow
            upstream = own_part + jnp.pad(first_ahead, ((0, block_rows - SPAN), (0, 0)))
        else:
            outflow, own_part, ahead_part = reach_outflow(storage)
            upstream = own_part + jnp.pad(
                shifted(ahead_part, ("gy", "gx"), 1), ((0, block_rows - SPAN), (0, 0))
            )
        storage = storage - outflow + upstream + lateral_gain * laterals[step]
    return (depth, flux_east, flux_south, storage)


def solution(mesh):
    placed = (
        P("gy", "gx"),
        P("gy", "gx"),
        P("gy", "gx"),
        P("gy", "gx"),
        P("gy", "gx"),
        P("gy", "gx"),
        P(("gy", "gx")),
        P(("gy", "gx"), None),
        P(("gy", "gx"), None),
        P(("gy", "gx")),
    )
    return jax.shard_map(
        body,
        mesh=mesh,
        in_specs=placed,
        out_specs=(P("gy", "gx"), P("gy", "gx"), P("gy", "gx"), P(("gy", "gx"), None)),
        check_vma=False,
    )
```

```python
import functools

import jax
import jax.numpy as jnp
from jax import lax
from jax.experimental import pallas as pl
from jax.experimental.pallas import tpu as pltpu
from jax.sharding import PartitionSpec as P

STRIP = 8
STEPS = 2
SPAN = 8


rim_depth = 0.1
slope_gain = 0.1
friction_gain = 1.0
mass_gain = 0.05
drain_rate = 0.05
lateral_gain = 0.125


def shifted(value, axis, steps):
    count = lax.axis_size(axis)
    first, last = (max(0, -steps), min(count, count - steps))
    return lax.ppermute(value, axis, [(source, source + steps) for source in range(first, last)])


def face_update(flux, level, level_next, depth, depth_next, roughness, active):
    face_depth = rim_depth + 0.5 * (jnp.abs(depth) + jnp.abs(depth_next))
    drive = flux - slope_gain * face_depth * (level_next - level)
    inverse_power = jnp.exp((-7.0 / 3.0) * jnp.log(face_depth))
    damping = 1.0 + friction_gain * roughness * jnp.abs(flux) * inverse_power
    return active * drive / damping


def block_term(target_ids, values, start, count):
    targets = start + lax.iota(jnp.int32, count)
    onehot = (target_ids[:, None] == targets[None, :]).astype(jnp.float32)
    return jnp.einsum("tb,tc->bc", onehot, values, precision=lax.Precision.HIGHEST)


def first_col_row(x):
    return jnp.transpose(x[:, :128])[0:1, :]


def last_col_row(x):
    return jnp.transpose(x[:, -128:])[127:128, :]


def rows_as_cols(msg):
    count, length = msg.shape
    pad = jnp.zeros((128 - count, length), jnp.float32)
    return jnp.transpose(jnp.concatenate([msg, pad], axis=0))


def write_edges(level, depth, flux_e, flux_s, rough, eopen, sopen, to_west, to_north, to_east,
                to_south):
    to_west[0:1, :] = first_col_row(level)
    to_west[1:2, :] = first_col_row(depth)
    to_north[0:1, :] = level[0:1, :]
    to_north[1:2, :] = depth[0:1, :]
    to_east[0:1, :] = last_col_row(flux_e)
    to_east[1:2, :] = last_col_row(level)
    to_east[2:3, :] = last_col_row(depth)
    to_east[3:4, :] = last_col_row(rough)
    to_east[4:5, :] = last_col_row(eopen)
    to_south[0:1, :] = flux_s[-1:, :]
    to_south[1:2, :] = level[-1:, :]
    to_south[2:3, :] = depth[-1:, :]
    to_south[3:4, :] = rough[-1:, :]
    to_south[4:5, :] = sopen[-1:, :]


def tile_rows(drained):
    ny, nx = drained.shape
    strips = drained.reshape(ny // STRIP, STRIP, nx).sum(axis=1)
    return jnp.concatenate([strips[:, k * 128:(k + 1) * 128] for k in range(nx // 128)], axis=0)


def open_masks(flags_ref, land):
    ny, nx = land.shape
    col = lax.broadcasted_iota(jnp.int32, (ny, nx), 1)
    row = lax.broadcasted_iota(jnp.int32, (ny, nx), 0)
    eopen = jnp.where((col == nx - 1) & (flags_ref[0] == 1), 0.0, land)
    sopen = jnp.where((row == ny - 1) & (flags_ref[1] == 1), 0.0, land)
    return col, row, eopen, sopen


def edge_kernel(flags_ref, d_ref, land_ref, bed_first_col, bed_last_col, bed_first_row,
                bed_last_row, e_ref, s_ref, r_col, r_row,
                tile_out, to_west, to_north, to_east, to_south):
    ny, nx = d_ref.shape
    depth = d_ref[...]
    land = land_ref[...].astype(jnp.float32)
    drained = drain_rate * land * jnp.abs(depth)
    tile_out[...] = tile_rows(drained)
    _, _, eopen, sopen = open_masks(flags_ref, land)
    to_west[0:1, :] = first_col_row(bed_first_col[...] + depth[:, :128])
    to_west[1:2, :] = first_col_row(depth)
    to_north[0:1, :] = bed_first_row[0:1, :] + depth[0:1, :]
    to_north[1:2, :] = depth[0:1, :]
    to_east[0:1, :] = last_col_row(e_ref[...])
    to_east[1:2, :] = last_col_row(bed_last_col[...] + depth[:, -128:])
    to_east[2:3, :] = last_col_row(depth)
    to_east[3:4, :] = last_col_row(r_col[...])
    to_east[4:5, :] = last_col_row(eopen)
    to_south[0:1, :] = s_ref[-1:, :]
    to_south[1:2, :] = bed_last_row[-1:, :] + depth[-1:, :]
    to_south[2:3, :] = depth[-1:, :]
    to_south[3:4, :] = r_row[-1:, :]
    to_south[4:5, :] = sopen[-1:, :]


def step_kernel(with_edges, flags_ref, d_ref, e_ref, s_ref, bed_ref, r_ref, land_ref,
                east_ref, south_ref, west_ref, north_ref,
                d_out, e_out, s_out, *more):
    ny, nx = d_ref.shape
    depth = d_ref[...]
    bed = bed_ref[...]
    land = land_ref[...].astype(jnp.float32)
    rough = r_ref[...]
    level = bed + depth
    col, row, eopen, sopen = open_masks(flags_ref, land)
    east = rows_as_cols(east_ref[...])
    west = rows_as_cols(west_ref[...])
    level_e = jnp.where(col == nx - 1, east[:, 0:1], pltpu.roll(level, nx - 1, 1))
    depth_e = jnp.where(col == nx - 1, east[:, 1:2], pltpu.roll(depth, nx - 1, 1))
    level_s = jnp.where(row == ny - 1, south_ref[0:1, :], pltpu.roll(level, ny - 1, 0))
    depth_s = jnp.where(row == ny - 1, south_ref[1:2, :], pltpu.roll(depth, ny - 1, 0))
    flux_e = face_update(e_ref[...], level, level_e, depth, depth_e, rough, eopen)
    flux_s = face_update(s_ref[...], level, level_s, depth, depth_s, rough, sopen)
    west_edge = face_update(
        west[:, 0:1], west[:, 1:2], level[:, 0:1], west[:, 2:3], depth[:, 0:1],
        west[:, 3:4], west[:, 4:5],
    )
    north_edge = face_update(
        north_ref[0:1, :], north_ref[1:2, :], level[0:1, :], north_ref[2:3, :], depth[0:1, :],
        north_ref[3:4, :], north_ref[4:5, :],
    )
    west_edge = jnp.where(flags_ref[2] == 1, 0.0, west_edge)
    west_flux = jnp.where(col == 0, west_edge, pltpu.roll(flux_e, 1, 1))
    north_flux = jnp.where(row == 0, north_edge, pltpu.roll(flux_s, 1, 0))
    drained = drain_rate * land * jnp.abs(depth)
    new_depth = depth - mass_gain * (flux_e - west_flux + (flux_s - north_flux)) - drained
    d_out[...] = new_depth
    e_out[...] = flux_e
    s_out[...] = flux_s
    if with_edges:
        tile_out, to_west, to_north, to_east, to_south = more
        next_drained = drain_rate * land * jnp.abs(new_depth)
        tile_out[...] = tile_rows(next_drained)
        write_edges(bed + new_depth, new_depth, flux_e, flux_s, rough, eopen, sopen,
                    to_west, to_north, to_east, to_south)


def last_step_kernel(total_rows, flags_ref, d_ref, e_ref, s_ref, bed_ref, r_ref, land_ref,
                     d_up, s_up, bed_up, r_up, land_up, d_dn, bed_dn,
                     east_ref, south_ref, west_ref, north_ref, d_out, e_out, s_out):
    block = pl.program_id(0)
    blocks = pl.num_programs(0)
    tr, nx = d_ref.shape
    depth = d_ref[...]
    bed = bed_ref[...]
    land = land_ref[...].astype(jnp.float32)
    rough = r_ref[...]
    level = bed + depth
    col = lax.broadcasted_iota(jnp.int32, (1, nx), 1)
    row = lax.broadcasted_iota(jnp.int32, (tr, 1), 0)
    eopen = land * jnp.where((col == nx - 1) & (flags_ref[0] == 1), 0.0, 1.0)
    sopen = land * jnp.where(
        (block * tr + row == total_rows - 1) & (flags_ref[1] == 1), 0.0, 1.0
    )
    east = rows_as_cols(east_ref[...])
    west = rows_as_cols(west_ref[...])
    level_e = jnp.where(col == nx - 1, east[:, 0:1], pltpu.roll(level, nx - 1, 1))
    depth_e = jnp.where(col == nx - 1, east[:, 1:2], pltpu.roll(depth, nx - 1, 1))
    at_bottom = block == blocks - 1
    below_depth = jnp.where(at_bottom, south_ref[1:2, :], d_dn[0:1, :])
    below_level = jnp.where(at_bottom, south_ref[0:1, :], bed_dn[0:1, :] + d_dn[0:1, :])
    level_s = jnp.where(row == tr - 1, below_level, pltpu.roll(level, tr - 1, 0))
    depth_s = jnp.where(row == tr - 1, below_depth, pltpu.roll(depth, tr - 1, 0))
    flux_e = face_update(e_ref[...], level, level_e, depth, depth_e, rough, eopen)
    flux_s = face_update(s_ref[...], level, level_s, depth, depth_s, rough, sopen)
    west_edge = face_update(
        west[:, 0:1], west[:, 1:2], level[:, 0:1], west[:, 2:3], depth[:, 0:1],
        west[:, 3:4], west[:, 4:5],
    )
    west_edge = jnp.where(flags_ref[2] == 1, 0.0, west_edge)
    outer_north = face_update(
        north_ref[0:1, :], north_ref[1:2, :], level[0:1, :], north_ref[2:3, :], depth[0:1, :],
        north_ref[3:4, :], north_ref[4:5, :],
    )
    up_depth = d_up[7:8, :]
    inner_north = face_update(
        s_up[7:8, :], bed_up[7:8, :] + up_depth, level[0:1, :], up_depth, depth[0:1, :],
        r_up[7:8, :], land_up[7:8, :].astype(jnp.float32),
    )
    north_edge = jnp.where(block == 0, outer_north, inner_north)
    west_flux = jnp.where(col == 0, west_edge, pltpu.roll(flux_e, 1, 1))
    north_flux = jnp.where(row == 0, north_edge, pltpu.roll(flux_s, 1, 0))
    drained = drain_rate * land * jnp.abs(depth)
    d_out[...] = depth - mass_gain * (flux_e - west_flux + (flux_s - north_flux)) - drained
    e_out[...] = flux_e
    s_out[...] = flux_s


def edge_shapes(ny, nx):
    f32 = jnp.float32
    return (
        jax.ShapeDtypeStruct((2, ny), f32),
        jax.ShapeDtypeStruct((2, nx), f32),
        jax.ShapeDtypeStruct((5, ny), f32),
        jax.ShapeDtypeStruct((5, nx), f32),
    )


def vmem_specs(count):
    return [pl.BlockSpec(memory_space=pltpu.VMEM) for _ in range(count)]


def body(
    water_depth,
    flux_east,
    flux_south,
    bed_level,
    roughness,
    land_mask,
    tile_block,
    storage,
    reach_rate,
    downstream,
):
    cell_rows, cell_cols = water_depth.shape
    block_rows, reach_width = storage.shape
    row_count = lax.axis_size("gy")
    col_count = lax.axis_size("gx")
    row_index = lax.axis_index("gy")
    col_index = lax.axis_index("gx")
    device_count = row_count * col_count
    tile_count = tile_block.shape[0]
    slot_cap = max(2, 2 * tile_count // device_count)
    flags = jnp.stack(
        [
            (col_index == col_count - 1).astype(jnp.int32),
            (row_index == row_count - 1).astype(jnp.int32),
            (col_index == 0).astype(jnp.int32),
        ]
    )
    device_index = row_index * col_count + col_index
    first_block = device_index * block_rows
    f32 = jnp.float32
    grid_shape = jax.ShapeDtypeStruct((cell_rows, cell_cols), f32)
    smem_spec = pl.BlockSpec(memory_space=pltpu.SMEM)

    col_blocks = cell_cols // 128
    row_blocks = cell_rows // 8
    col_spec = lambda k: pl.BlockSpec((cell_rows, 128), lambda i: (0, k))
    row_spec = lambda k: pl.BlockSpec((8, cell_cols), lambda i: (k, 0))
    tile_shape = jax.ShapeDtypeStruct((cell_rows // STRIP * cell_cols // 128, 128), f32)
    tiles, *edges = pl.pallas_call(
        edge_kernel,
        grid=(1,),
        out_shape=(tile_shape,) + edge_shapes(cell_rows, cell_cols),
        in_specs=[smem_spec] + vmem_specs(2)
        + [col_spec(0), col_spec(col_blocks - 1), row_spec(0), row_spec(row_blocks - 1),
           col_spec(col_blocks - 1), row_spec(row_blocks - 1),
           col_spec(col_blocks - 1), row_spec(row_blocks - 1)],
        out_specs=vmem_specs(5),
    )(flags, water_depth, land_mask, bed_level, bed_level, bed_level, bed_level,
      flux_east, flux_south, roughness, roughness)
    tile_parts = [tiles]

    def step_call(with_edges):
        outs = (grid_shape, grid_shape, grid_shape)
        if with_edges:
            outs = outs + (tile_shape,) + edge_shapes(cell_rows, cell_cols)
        return pl.pallas_call(
            functools.partial(step_kernel, with_edges),
            out_shape=outs,
            in_specs=[smem_spec] + vmem_specs(10),
            out_specs=vmem_specs(len(outs)),
        )

    tile_owner = tile_block // block_rows
    owner_hits = (tile_owner[:, None] == lax.iota(jnp.int32, device_count)[None, :]).astype(
        jnp.int32
    )
    earlier = jnp.sum((jnp.cumsum(owner_hits, axis=0) - owner_hits) * owner_hits, axis=1)
    send_pos = tile_owner * slot_cap + earlier
    local_ids = (tile_block % block_rows).astype(f32)
    gather_onehot = (
        lax.iota(jnp.int32, device_count * slot_cap)[:, None] == send_pos[None, :]
    ).astype(f32)
    send_ids = jnp.dot(gather_onehot, local_ids + 1.0, precision=lax.Precision.DEFAULT) - 1.0
    lane_blocks = cell_cols // 128
    row_pos = send_pos.reshape(cell_rows // STRIP, lane_blocks).T.reshape(-1)
    row_onehot = (
        lax.iota(jnp.int32, device_count * slot_cap)[:, None] == row_pos[None, :]
    ).astype(f32)
    id_rows = -(-slot_cap // reach_width)
    send_ids = jnp.pad(
        send_ids.reshape(device_count, slot_cap),
        ((0, 0), (0, id_rows * reach_width - slot_cap)),
        constant_values=-1.0,
    ).reshape(device_count, id_rows, reach_width)
    def start_lateral(parts, with_ids=True):
        packed = [
            jnp.dot(row_onehot, part, precision=lax.Precision.HIGH).reshape(
                device_count, slot_cap, reach_width
            )
            for part in parts
        ]
        return jnp.concatenate(packed + ([send_ids] if with_ids else []), axis=1)

    first_rows = slot_cap + id_rows
    got_first = lax.all_to_all(
        start_lateral(tile_parts).reshape(device_count, first_rows * reach_width),
        ("gy", "gx"), 0, 0, tiled=True,
    ).reshape(device_count, first_rows, reach_width)

    def reach_outflow(storage):
        ratio = reach_rate * jnp.power(storage, 2.0 / 3.0)
        outflow = storage * ratio / (1.0 + ratio)
        own_part = block_term(downstream, outflow, first_block, block_rows)
        ahead_part = block_term(downstream, outflow, first_block + block_rows, SPAN)
        return outflow, own_part, ahead_part

    first_outflow = reach_outflow(storage)
    ahead_rows = SPAN * reach_width // cell_cols
    tr = 256
    nblk = cell_rows // tr
    main_spec = pl.BlockSpec((tr, cell_cols), lambda i: (i, 0))
    up_spec = pl.BlockSpec((8, cell_cols), lambda i: (jnp.maximum(i * (tr // 8) - 1, 0), 0))
    dn_spec = pl.BlockSpec(
        (8, cell_cols), lambda i: (jnp.minimum((i + 1) * (tr // 8), cell_rows // 8 - 1), 0)
    )
    last_call = pl.pallas_call(
        functools.partial(last_step_kernel, cell_rows),
        grid=(nblk,),
        out_shape=(grid_shape, grid_shape, grid_shape),
        in_specs=[smem_spec] + [main_spec] * 6 + [up_spec] * 5 + [dn_spec] * 2
        + [
            pl.BlockSpec((2, tr), lambda i: (0, i)),
            pl.BlockSpec((2, cell_cols), lambda i: (0, 0)),
            pl.BlockSpec((5, tr), lambda i: (0, i)),
            pl.BlockSpec((5, cell_cols), lambda i: (0, 0)),
        ],
        out_specs=[main_spec] * 3,
    )

    depth = water_depth
    for step in range(STEPS):
        to_west, to_north, to_east, to_south = edges
        east_in = shifted(to_west, "gx", -1)
        south_in = shifted(to_north, "gy", -1)
        if step == 0:
            joined = shifted(
                jnp.concatenate(
                    [to_east, first_outflow[2].reshape(ahead_rows, cell_cols)], axis=0
                ),
                ("gy", "gx"),
                1,
            )
            west_in = joined[: to_east.shape[0]]
            first_ahead = joined[to_east.shape[0]:].reshape(SPAN, reach_width)
        else:
            west_in = shifted(to_east, "gx", 1)
        north_in = shifted(to_south, "gy", 1)
        last = step == STEPS - 1
        if last:
            lateral_started = start_lateral(tile_parts[1:], False)
            east_in, south_in, west_in, north_in, lateral_started, got_first = (
                lax.optimization_barrier(
                    (east_in, south_in, west_in, north_in, lateral_started, got_first)
                )
            )
        if last:
            outs = last_call(
                flags, depth, flux_east, flux_south, bed_level, roughness, land_mask,
                depth, flux_south, bed_level, roughness, land_mask, depth, bed_level,
                east_in, south_in, west_in, north_in,
            )
        else:
            outs = step_call(True)(
                flags, depth, flux_east, flux_south, bed_level, roughness, land_mask,
                east_in, south_in, west_in, north_in,
            )
        depth, flux_east, flux_south = outs[:3]
        if not last:
            tile_parts.append(outs[3])
            edges = outs[4:]

    got_second = lax.all_to_all(lateral_started, ("gy", "gx"), 0, 0, tiled=True)
    got_ids = got_first[:, slot_cap:].reshape(device_count, -1)[:, :slot_cap].reshape(-1)
    targets = lax.iota(f32, block_rows)
    scatter_onehot = (targets[:, None] == got_ids[None, :]).astype(f32)
    laterals = [
        jnp.dot(
            scatter_onehot,
            got[:, :slot_cap].reshape(-1, reach_width),
            precision=lax.Precision.HIGHEST,
        )
        for got in (got_first, got_second)
    ]

    for step in range(STEPS):
        if step == 0:
            outflow, own_part, _ = first_outflow
            upstream = own_part + jnp.pad(first_ahead, ((0, block_rows - SPAN), (0, 0)))
        else:
            outflow, own_part, ahead_part = reach_outflow(storage)
            upstream = own_part + jnp.pad(
                shifted(ahead_part, ("gy", "gx"), 1), ((0, block_rows - SPAN), (0, 0))
            )
        storage = storage - outflow + upstream + lateral_gain * laterals[step]
    return (depth, flux_east, flux_south, storage)


def solution(mesh):
    placed = (
        P("gy", "gx"),
        P("gy", "gx"),
        P("gy", "gx"),
        P("gy", "gx"),
        P("gy", "gx"),
        P("gy", "gx"),
        P(("gy", "gx")),
        P(("gy", "gx"), None),
        P(("gy", "gx"), None),
        P(("gy", "gx")),
    )
    return jax.shard_map(
        body,
        mesh=mesh,
        in_specs=placed,
        out_specs=(P("gy", "gx"), P("gy", "gx"), P("gy", "gx"), P(("gy", "gx"), None)),
        check_vma=False,
    )
```

```python
import functools

import jax
import jax.numpy as jnp
from jax import lax
from jax.experimental import pallas as pl
from jax.experimental.pallas import tpu as pltpu
from jax.sharding import PartitionSpec as P

STRIP = 8
STEPS = 2
SPAN = 8


rim_depth = 0.1
slope_gain = 0.1
friction_gain = 1.0
mass_gain = 0.05
drain_rate = 0.05
lateral_gain = 0.125


def shifted(value, axis, steps):
    count = lax.axis_size(axis)
    first, last = (max(0, -steps), min(count, count - steps))
    return lax.ppermute(value, axis, [(source, source + steps) for source in range(first, last)])


def face_update(flux, level, level_next, depth, depth_next, roughness, active):
    face_depth = rim_depth + 0.5 * (jnp.abs(depth) + jnp.abs(depth_next))
    drive = flux - slope_gain * face_depth * (level_next - level)
    inverse_power = jnp.exp((-7.0 / 3.0) * jnp.log(face_depth))
    damping = 1.0 + friction_gain * roughness * jnp.abs(flux) * inverse_power
    return active * drive / damping


def block_term(target_ids, values, start, count):
    targets = start + lax.iota(jnp.int32, count)
    onehot = (target_ids[:, None] == targets[None, :]).astype(jnp.float32)
    return jnp.einsum("tb,tc->bc", onehot, values, precision=lax.Precision.HIGHEST)


def first_col_row(x):
    return jnp.transpose(x[:, :128])[0:1, :]


def last_col_row(x):
    return jnp.transpose(x[:, -128:])[127:128, :]


def rows_as_cols(msg):
    count, length = msg.shape
    pad = jnp.zeros((128 - count, length), jnp.float32)
    return jnp.transpose(jnp.concatenate([msg, pad], axis=0))


def write_edges(level, depth, flux_e, flux_s, rough, eopen, sopen, to_west, to_north, to_east,
                to_south):
    to_west[0:1, :] = first_col_row(level)
    to_west[1:2, :] = first_col_row(depth)
    to_north[0:1, :] = level[0:1, :]
    to_north[1:2, :] = depth[0:1, :]
    to_east[0:1, :] = last_col_row(flux_e)
    to_east[1:2, :] = last_col_row(level)
    to_east[2:3, :] = last_col_row(depth)
    to_east[3:4, :] = last_col_row(rough)
    to_east[4:5, :] = last_col_row(eopen)
    to_south[0:1, :] = flux_s[-1:, :]
    to_south[1:2, :] = level[-1:, :]
    to_south[2:3, :] = depth[-1:, :]
    to_south[3:4, :] = rough[-1:, :]
    to_south[4:5, :] = sopen[-1:, :]


def tile_rows(drained):
    ny, nx = drained.shape
    strips = drained.reshape(ny // STRIP, STRIP, nx).sum(axis=1)
    return jnp.concatenate([strips[:, k * 128:(k + 1) * 128] for k in range(nx // 128)], axis=0)


def open_masks(flags_ref, land):
    ny, nx = land.shape
    col = lax.broadcasted_iota(jnp.int32, (ny, nx), 1)
    row = lax.broadcasted_iota(jnp.int32, (ny, nx), 0)
    eopen = jnp.where((col == nx - 1) & (flags_ref[0] == 1), 0.0, land)
    sopen = jnp.where((row == ny - 1) & (flags_ref[1] == 1), 0.0, land)
    return col, row, eopen, sopen


def edge_kernel(flags_ref, d_ref, land_ref, bed_first_col, bed_last_col, bed_first_row,
                bed_last_row, e_ref, s_ref, r_col, r_row,
                tile_out, to_west, to_north, to_east, to_south):
    ny, nx = d_ref.shape
    depth = d_ref[...]
    land = land_ref[...].astype(jnp.float32)
    drained = drain_rate * land * jnp.abs(depth)
    tile_out[...] = tile_rows(drained)
    _, _, eopen, sopen = open_masks(flags_ref, land)
    to_west[0:1, :] = first_col_row(bed_first_col[...] + depth[:, :128])
    to_west[1:2, :] = first_col_row(depth)
    to_north[0:1, :] = bed_first_row[0:1, :] + depth[0:1, :]
    to_north[1:2, :] = depth[0:1, :]
    to_east[0:1, :] = last_col_row(e_ref[...])
    to_east[1:2, :] = last_col_row(bed_last_col[...] + depth[:, -128:])
    to_east[2:3, :] = last_col_row(depth)
    to_east[3:4, :] = last_col_row(r_col[...])
    to_east[4:5, :] = last_col_row(eopen)
    to_south[0:1, :] = s_ref[-1:, :]
    to_south[1:2, :] = bed_last_row[-1:, :] + depth[-1:, :]
    to_south[2:3, :] = depth[-1:, :]
    to_south[3:4, :] = r_row[-1:, :]
    to_south[4:5, :] = sopen[-1:, :]


def step_kernel(with_edges, flags_ref, d_ref, e_ref, s_ref, bed_ref, r_ref, land_ref,
                east_ref, south_ref, west_ref, north_ref,
                d_out, e_out, s_out, *more):
    ny, nx = d_ref.shape
    depth = d_ref[...]
    bed = bed_ref[...]
    land = land_ref[...].astype(jnp.float32)
    rough = r_ref[...]
    level = bed + depth
    col, row, eopen, sopen = open_masks(flags_ref, land)
    east = rows_as_cols(east_ref[...])
    west = rows_as_cols(west_ref[...])
    level_e = jnp.where(col == nx - 1, east[:, 0:1], pltpu.roll(level, nx - 1, 1))
    depth_e = jnp.where(col == nx - 1, east[:, 1:2], pltpu.roll(depth, nx - 1, 1))
    level_s = jnp.where(row == ny - 1, south_ref[0:1, :], pltpu.roll(level, ny - 1, 0))
    depth_s = jnp.where(row == ny - 1, south_ref[1:2, :], pltpu.roll(depth, ny - 1, 0))
    flux_e = face_update(e_ref[...], level, level_e, depth, depth_e, rough, eopen)
    flux_s = face_update(s_ref[...], level, level_s, depth, depth_s, rough, sopen)
    west_edge = face_update(
        west[:, 0:1], west[:, 1:2], level[:, 0:1], west[:, 2:3], depth[:, 0:1],
        west[:, 3:4], west[:, 4:5],
    )
    north_edge = face_update(
        north_ref[0:1, :], north_ref[1:2, :], level[0:1, :], north_ref[2:3, :], depth[0:1, :],
        north_ref[3:4, :], north_ref[4:5, :],
    )
    west_edge = jnp.where(flags_ref[2] == 1, 0.0, west_edge)
    west_flux = jnp.where(col == 0, west_edge, pltpu.roll(flux_e, 1, 1))
    north_flux = jnp.where(row == 0, north_edge, pltpu.roll(flux_s, 1, 0))
    drained = drain_rate * land * jnp.abs(depth)
    new_depth = depth - mass_gain * (flux_e - west_flux + (flux_s - north_flux)) - drained
    d_out[...] = new_depth
    e_out[...] = flux_e
    s_out[...] = flux_s
    if with_edges:
        tile_out, to_west, to_north, to_east, to_south = more
        next_drained = drain_rate * land * jnp.abs(new_depth)
        tile_out[...] = tile_rows(next_drained)
        write_edges(bed + new_depth, new_depth, flux_e, flux_s, rough, eopen, sopen,
                    to_west, to_north, to_east, to_south)


def edge_shapes(ny, nx):
    f32 = jnp.float32
    return (
        jax.ShapeDtypeStruct((2, ny), f32),
        jax.ShapeDtypeStruct((2, nx), f32),
        jax.ShapeDtypeStruct((5, ny), f32),
        jax.ShapeDtypeStruct((5, nx), f32),
    )


def vmem_specs(count):
    return [pl.BlockSpec(memory_space=pltpu.VMEM) for _ in range(count)]


def body(
    water_depth,
    flux_east,
    flux_south,
    bed_level,
    roughness,
    land_mask,
    tile_block,
    storage,
    reach_rate,
    downstream,
):
    cell_rows, cell_cols = water_depth.shape
    block_rows, reach_width = storage.shape
    row_count = lax.axis_size("gy")
    col_count = lax.axis_size("gx")
    row_index = lax.axis_index("gy")
    col_index = lax.axis_index("gx")
    device_count = row_count * col_count
    tile_count = tile_block.shape[0]
    slot_cap = max(2, 2 * tile_count // device_count)
    flags = jnp.stack(
        [
            (col_index == col_count - 1).astype(jnp.int32),
            (row_index == row_count - 1).astype(jnp.int32),
            (col_index == 0).astype(jnp.int32),
        ]
    )
    device_index = row_index * col_count + col_index
    first_block = device_index * block_rows
    f32 = jnp.float32
    grid_shape = jax.ShapeDtypeStruct((cell_rows, cell_cols), f32)
    smem_spec = pl.BlockSpec(memory_space=pltpu.SMEM)

    col_blocks = cell_cols // 128
    row_blocks = cell_rows // 8
    col_spec = lambda k: pl.BlockSpec((cell_rows, 128), lambda i: (0, k))
    row_spec = lambda k: pl.BlockSpec((8, cell_cols), lambda i: (k, 0))
    tile_shape = jax.ShapeDtypeStruct((cell_rows // STRIP * cell_cols // 128, 128), f32)
    tiles, *edges = pl.pallas_call(
        edge_kernel,
        grid=(1,),
        out_shape=(tile_shape,) + edge_shapes(cell_rows, cell_cols),
        in_specs=[smem_spec] + vmem_specs(2)
        + [col_spec(0), col_spec(col_blocks - 1), row_spec(0), row_spec(row_blocks - 1),
           col_spec(col_blocks - 1), row_spec(row_blocks - 1),
           col_spec(col_blocks - 1), row_spec(row_blocks - 1)],
        out_specs=vmem_specs(5),
    )(flags, water_depth, land_mask, bed_level, bed_level, bed_level, bed_level,
      flux_east, flux_south, roughness, roughness)
    tile_parts = [tiles]

    def step_call(with_edges):
        outs = (grid_shape, grid_shape, grid_shape)
        if with_edges:
            outs = outs + (tile_shape,) + edge_shapes(cell_rows, cell_cols)
        return pl.pallas_call(
            functools.partial(step_kernel, with_edges),
            out_shape=outs,
            in_specs=[smem_spec] + vmem_specs(10),
            out_specs=vmem_specs(len(outs)),
        )

    tile_owner = tile_block // block_rows
    owner_hits = (tile_owner[:, None] == lax.iota(jnp.int32, device_count)[None, :]).astype(
        jnp.int32
    )
    earlier = jnp.sum((jnp.cumsum(owner_hits, axis=0) - owner_hits) * owner_hits, axis=1)
    send_pos = tile_owner * slot_cap + earlier
    local_ids = (tile_block % block_rows).astype(f32)
    gather_onehot = (
        lax.iota(jnp.int32, device_count * slot_cap)[:, None] == send_pos[None, :]
    ).astype(f32)
    send_ids = jnp.dot(gather_onehot, local_ids + 1.0, precision=lax.Precision.DEFAULT) - 1.0
    lane_blocks = cell_cols // 128
    row_pos = send_pos.reshape(cell_rows // STRIP, lane_blocks).T.reshape(-1)
    row_onehot = (
        lax.iota(jnp.int32, device_count * slot_cap)[:, None] == row_pos[None, :]
    ).astype(f32)
    id_rows = -(-slot_cap // reach_width)
    send_ids = jnp.pad(
        send_ids.reshape(device_count, slot_cap),
        ((0, 0), (0, id_rows * reach_width - slot_cap)),
        constant_values=-1.0,
    ).reshape(device_count, id_rows, reach_width)
    def start_lateral(parts, with_ids=True):
        packed = [
            jnp.dot(row_onehot, part, precision=lax.Precision.HIGH).reshape(
                device_count, slot_cap, reach_width
            )
            for part in parts
        ]
        return jnp.concatenate(packed + ([send_ids] if with_ids else []), axis=1)

    first_rows = slot_cap + id_rows
    got_first = lax.all_to_all(
        start_lateral(tile_parts).reshape(device_count, first_rows * reach_width),
        ("gy", "gx"), 0, 0, tiled=True,
    ).reshape(device_count, first_rows, reach_width)

    def reach_outflow(storage):
        ratio = reach_rate * jnp.power(storage, 2.0 / 3.0)
        outflow = storage * ratio / (1.0 + ratio)
        own_part = block_term(downstream, outflow, first_block, block_rows)
        ahead_part = block_term(downstream, outflow, first_block + block_rows, SPAN)
        return outflow, own_part, ahead_part

    first_outflow = reach_outflow(storage)
    ahead_rows = SPAN * reach_width // cell_cols
    depth = water_depth
    for step in range(STEPS):
        to_west, to_north, to_east, to_south = edges
        east_in = shifted(to_west, "gx", -1)
        south_in = shifted(to_north, "gy", -1)
        if step == 0:
            joined = shifted(
                jnp.concatenate(
                    [to_east, first_outflow[2].reshape(ahead_rows, cell_cols)], axis=0
                ),
                ("gy", "gx"),
                1,
            )
            west_in = joined[: to_east.shape[0]]
            first_ahead = joined[to_east.shape[0]:].reshape(SPAN, reach_width)
        else:
            west_in = shifted(to_east, "gx", 1)
        north_in = shifted(to_south, "gy", 1)
        last = step == STEPS - 1
        if last:
            lateral_started = start_lateral(tile_parts[1:], False)
            east_in, south_in, west_in, north_in, lateral_started, got_first = (
                lax.optimization_barrier(
                    (east_in, south_in, west_in, north_in, lateral_started, got_first)
                )
            )
        outs = step_call(not last)(
            flags, depth, flux_east, flux_south, bed_level, roughness, land_mask,
            east_in, south_in, west_in, north_in,
        )
        depth, flux_east, flux_south = outs[:3]
        if not last:
            tile_parts.append(outs[3])
            edges = outs[4:]

    got_second = lax.all_to_all(lateral_started, ("gy", "gx"), 0, 0, tiled=True)
    got_ids = got_first[:, slot_cap:].reshape(device_count, -1)[:, :slot_cap].reshape(-1)
    targets = lax.iota(f32, block_rows)
    scatter_onehot = (targets[:, None] == got_ids[None, :]).astype(f32)
    laterals = [
        jnp.dot(
            scatter_onehot,
            got[:, :slot_cap].reshape(-1, reach_width),
            precision=lax.Precision.HIGH,
        )
        for got in (got_first, got_second)
    ]

    for step in range(STEPS):
        if step == 0:
            outflow, own_part, _ = first_outflow
            upstream = own_part + jnp.pad(first_ahead, ((0, block_rows - SPAN), (0, 0)))
        else:
            outflow, own_part, ahead_part = reach_outflow(storage)
            upstream = own_part + jnp.pad(
                shifted(ahead_part, ("gy", "gx"), 1), ((0, block_rows - SPAN), (0, 0))
            )
        storage = storage - outflow + upstream + lateral_gain * laterals[step]
    return (depth, flux_east, flux_south, storage)


def solution(mesh):
    placed = (
        P("gy", "gx"),
        P("gy", "gx"),
        P("gy", "gx"),
        P("gy", "gx"),
        P("gy", "gx"),
        P("gy", "gx"),
        P(("gy", "gx")),
        P(("gy", "gx"), None),
        P(("gy", "gx"), None),
        P(("gy", "gx")),
    )
    return jax.shard_map(
        body,
        mesh=mesh,
        in_specs=placed,
        out_specs=(P("gy", "gx"), P("gy", "gx"), P("gy", "gx"), P(("gy", "gx"), None)),
        check_vma=False,
    )
```
